32 devices in a mesh: row: 4 (over x, core), col: 8 (over z, y).
Axes of the slice: x: 2, y: 2, z: 4, core: 2. Of those that a mesh axis runs over, the one named last changes fastest.
Arguments:
- a_blocks: bfloat16 [16, 32, 9, 64, 64], P('row', 'col'), may hold values from -0.375 to 0.375
- a_cols: int32 [16, 32, 9], P('row', 'col'), may hold values from 0 to 511, as said below
- p_blocks: bfloat16 [16, 32, 4, 64, 64], P('row', 'col'), may hold values from -1.5 to 1.5
- p_cols: int32 [16, 32, 4], P('row', 'col'), may hold values from 0 to 127, as said below
- c_cols: int32 [8, 16, 25], P('row', 'col'), may hold values from 0 to 127, as said below
Outputs:
- galerkin: bfloat16 [8, 16, 25, 64, 64], P('row', 'col')
The draws below stay inside these ranges and needn't reach their ends.
Inputs may be any that keep to these rules, and one draw needn't show every extreme that they name: a_cols of tile (y, x) names, in an order drawn per tile, the 9 tiles (y + dy, x + dx) with dy, dx in -1, 0, 1, where a row or column outside the grid is mirrored at the edge (-1 becomes 1, 16 becomes 16 - 2, likewise for columns). p_cols of tile (y, x) names, in an order drawn per tile, the 4 aggregates (Y, X) with Y in floor((y - 1) / 2) + 0 or 1 and X in floor((x - 1) / 2) + 0 or 1, an aggregate row or column outside the grid mirrored at the edge (-1 becomes 1, 8 becomes 8 - 2, likewise for columns). c_cols of aggregate (Y, X) names, in an order drawn per aggregate, the 25 aggregates (Y + dY, X + dX) with dY, dX in -2 to 2, mirrored at the edges as for p_cols (so some are named twice).
All inputs are finite; a program needn't handle non-finite values.
Results may differ from the reference program's by a relative error of at most 0.006.
Values may be sent and summed in bfloat16 or wider, within the bound.
No kernel may reach another device: no remote copies, remote signals or barrier semaphores. Data moves between devices by JAX's collectives and lax.ppermute only.
A program may use at most 128 MiB of HBM per device.

```python
import math
import jax
import jax.numpy as jnp
from jax import lax

BS = 64
GY = 16
GX = 32
NCY = 8
NCX = 16


def mirror(values, limit):
    values = jnp.where(values < 0, -values, values)
    return jnp.where(values >= limit, 2 * (limit - 1) - values, values)


def shuffled(key, shape, count):
    scores = jax.random.randint(key, shape + (count,), 0, 1 << 20) * 64 + jnp.arange(count, dtype=jnp.int32)
    return jnp.argsort(scores, axis=-1).astype(jnp.int32)


def draw_a_cols(key, part):
    order = shuffled(jax.random.fold_in(key, 11), (GY, GX), 9)
    steps_y = order // 3 - 1
    steps_x = order % 3 - 1
    rows = jnp.arange(GY, dtype=jnp.int32)[:, None, None] + steps_y
    cols = jnp.arange(GX, dtype=jnp.int32)[None, :, None] + steps_x
    return (mirror(rows, GY) * GX + mirror(cols, GX)).astype(jnp.int32)


def draw_p_cols(key, part):
    order = shuffled(jax.random.fold_in(key, 23), (GY, GX), 4)
    rows = (jnp.arange(GY, dtype=jnp.int32)[:, None, None] - 1) // 2 + order // 2
    cols = (jnp.arange(GX, dtype=jnp.int32)[None, :, None] - 1) // 2 + order % 2
    return (mirror(rows, NCY) * NCX + mirror(cols, NCX)).astype(jnp.int32)


def draw_c_cols(key, part):
    order = shuffled(jax.random.fold_in(key, 37), (NCY, NCX), 25)
    rows = jnp.arange(NCY, dtype=jnp.int32)[:, None, None] + order // 5 - 2
    cols = jnp.arange(NCX, dtype=jnp.int32)[None, :, None] + order % 5 - 2
    return (mirror(rows, NCY) * NCX + mirror(cols, NCX)).astype(jnp.int32)


def block_scale(key, shape, pieces, smallest, largest):
    def one(position, shards_of):
        draws = jax.random.uniform(jax.random.fold_in(jax.random.fold_in(key, 6), position), (shards_of,), jnp.float32, smallest / len(pieces), largest / len(pieces))
        return jnp.repeat(jnp.exp(draws), shape[position] // shards_of).reshape((-1,) + (1,) * (len(shape) - position - 1))

    factor_of = one(*pieces[0])
    for cut in pieces[1:]:
        factor_of = factor_of * one(*cut)
    return factor_of


def centred(key, shape, spread, most, shards=(), held_as=jnp.bfloat16):
    factor_of = block_scale(key, shape, shards, -0.22, 0.18) if shards else 1.0
    entries = jax.random.normal(key, shape, jnp.float32) * spread * factor_of
    return jnp.minimum(jnp.maximum(entries, -most), most).astype(held_as)


def setup_inputs(seed: int = 0) -> dict:
    seeds = jax.random.split(jax.random.key(seed), 6)
    return {
        "a_blocks": centred(seeds[0], (GY, GX, 9, BS, BS), (4.0 / BS), 0.375, ((0, 4), (1, 8))),
        "a_cols": draw_a_cols(jax.random.fold_in(seeds[5], 71), 0),
        "p_blocks": centred(seeds[2], (GY, GX, 4, BS, BS), 0.25, 1.5, ((0, 4), (1, 8))),
        "p_cols": draw_p_cols(jax.random.fold_in(seeds[5], 71), 0),
        "c_cols": draw_c_cols(jax.random.fold_in(seeds[5], 71), 0),
    }


def reference(a_blocks, a_cols, p_blocks, p_cols, c_cols):
    grid_rows, grid_cols = a_blocks.shape[0], a_blocks.shape[1]
    block_size = a_blocks.shape[-1]
    coarse_cols = grid_cols // 2
    coarse_total = (grid_rows // 2) * coarse_cols
    tiles = grid_rows * grid_cols
    a_flat = a_blocks.reshape(tiles, 9, block_size, block_size)
    a_index = a_cols.reshape(tiles, 9)
    p_flat = p_blocks.reshape(tiles, 4, block_size, block_size)
    p_index = p_cols.reshape(tiles, 4)
    batch = math.gcd(tiles, 256)
    tile_ids = jnp.arange(tiles, dtype=jnp.int32).reshape(tiles // batch, batch)
    slots = jnp.arange(9, dtype=jnp.int32)

    def form(ids):
        blocks = a_flat[ids].astype(jnp.float32)
        cols = a_index[ids]
        near = p_flat[cols].astype(jnp.float32)
        near_cols = p_index[cols]
        base_y = (ids // grid_cols) // 2 - 1
        base_x = (ids % grid_cols) // 2 - 1
        slot = (near_cols // coarse_cols - base_y[:, None, None]) * 3 + (near_cols % coarse_cols - base_x[:, None, None])
        hot = (slot[..., None] == slots).astype(jnp.float32)
        prod = jnp.einsum('rkab,rklbc->rklac', blocks, near)
        summed = jnp.einsum('rkle,rklac->reac', hot, prod, precision=lax.Precision.HIGHEST)
        return summed.astype(jnp.bfloat16)

    products = lax.map(form, tile_ids).reshape(tiles, 9, block_size, block_size)
    part_y = slots // 3
    part_x = slots % 3

    def add_terms(total, ids):
        prol = p_flat[ids].astype(jnp.float32)
        cols = p_index[ids]
        rows_ap = products[ids].astype(jnp.float32)
        terms = jnp.einsum('rmbu,rebv->rmeuv', prol, rows_ap)
        cy = cols // coarse_cols
        cx = cols % coarse_cols
        dy = ((ids // grid_cols) // 2 - 1)[:, None] + part_y[None, :]
        dx = ((ids % grid_cols) // 2 - 1)[:, None] + part_x[None, :]
        offset = (dy[:, None, :] - cy[:, :, None] + 2) * 5 + (dx[:, None, :] - cx[:, :, None] + 2)
        target = cols[:, :, None] * 25 + offset
        total = total.at[target.reshape(-1)].add(terms.reshape(-1, block_size, block_size))
        return total, None

    start = jnp.zeros((coarse_total * 25, block_size, block_size), jnp.float32)
    total, _ = lax.scan(add_terms, start, tile_ids)
    total = total.reshape(coarse_total, 25, block_size, block_size)
    wanted = c_cols.reshape(coarse_total, 25)
    coarse_ids = jnp.arange(coarse_total, dtype=jnp.int32)
    offset = (wanted // coarse_cols - (coarse_ids // coarse_cols)[:, None] + 2) * 5 + (wanted % coarse_cols - (coarse_ids % coarse_cols)[:, None] + 2)
    picked = jax.vmap(lambda blocks, where: blocks[where])(total, offset)
    return picked.astype(jnp.bfloat16).reshape(grid_rows // 2, coarse_cols, 25, block_size, block_size)
```

```python
import jax
import jax.numpy as jnp
from jax import lax
from jax.experimental import pallas as pl
from jax.experimental.pallas import tpu as pltpu
from jax.sharding import PartitionSpec as P


def mirror(values, limit):
    values = jnp.where(values < 0, -values, values)
    return jnp.where(values >= limit, 2 * (limit - 1) - values, values)


def shifted(piece, down, right):
    rows, cols = lax.axis_size("row"), lax.axis_size("col")
    if right == 0:
        pairs = [(s, s + down) for s in range(rows) if 0 <= s + down < rows]
        return lax.ppermute(piece, "row", pairs)
    if down == 0:
        pairs = [(s, s + right) for s in range(cols) if 0 <= s + right < cols]
        return lax.ppermute(piece, "col", pairs)
    pairs = []
    for sr in range(rows):
        for sc in range(cols):
            tr, tc = sr + down, sc + right
            if 0 <= tr < rows and 0 <= tc < cols:
                pairs.append((sr * cols + sc, tr * cols + tc))
    return lax.ppermute(piece, ("row", "col"), pairs)


def with_halo(x):
    top = shifted(x[-1], 1, 0)
    bottom = shifted(x[0], -1, 0)
    left = shifted(x[:, -1], 0, 1)
    right = shifted(x[:, 0], 0, -1)
    top_left = shifted(x[-1, -1], 1, 1)
    top_right = shifted(x[-1, 0], 1, -1)
    bottom_left = shifted(x[0, -1], -1, 1)
    bottom_right = shifted(x[0, 0], -1, -1)
    first = jnp.concatenate([top_left[None], top, top_right[None]], axis=0)
    last = jnp.concatenate([bottom_left[None], bottom, bottom_right[None]], axis=0)
    middle = jnp.concatenate([left[:, None], x, right[:, None]], axis=1)
    return jnp.concatenate([first[None], middle, last[None]], axis=0)


def ap_kernel(near_ref, slot_ref, a_ref, p_ref, out_ref, acc_ref):
    tiles, terms = a_ref.shape[0], a_ref.shape[1]

    def one_tile(t, carry):
        acc_ref[...] = jnp.zeros(acc_ref.shape, jnp.float32)
        for k in range(terms):
            j = near_ref[t * terms + k]
            a = a_ref[t, k]
            for q in range(4):
                e = slot_ref[(t * terms + k) * 4 + q]

                @pl.when(e >= 0)
                def _():
                    acc_ref[e] += jnp.dot(a, p_ref[j, q], preferred_element_type=jnp.float32)

        out_ref[t] = acc_ref[...].astype(out_ref.dtype)
        return carry

    lax.fori_loop(0, tiles, one_tile, 0)


def coarse_kernel(target_ref, pick_ref, ap_ref, pt_ref, out_ref, acc_ref):
    tiles = ap_ref.shape[0]
    owned, stencil = out_ref.shape[0], out_ref.shape[1]
    acc_ref[...] = jnp.zeros(acc_ref.shape, jnp.float32)

    def one_tile(t, carry):
        for q in range(4):
            g = target_ref[t * 4 + q]

            @pl.when(g >= 0)
            def _():
                pt = pt_ref[t, q]
                for e in range(9):
                    acc_ref[g + (e // 3) * 5 + e % 3] += jnp.dot(
                        pt, ap_ref[t, e], preferred_element_type=jnp.float32
                    )

        return carry

    lax.fori_loop(0, tiles, one_tile, 0)

    def one_pick(i, carry):
        a = i // stencil
        s = i % stencil
        out_ref[a, s] = acc_ref[a * stencil + pick_ref[i]].astype(out_ref.dtype)
        return carry

    lax.fori_loop(0, owned * stencil, one_pick, 0)


def body(a_blocks, a_cols, p_blocks, p_cols, c_cols):
    n_r, n_c = a_blocks.shape[0], a_blocks.shape[1]
    bs = a_blocks.shape[-1]
    terms = a_blocks.shape[2]
    grid_rows = n_r * lax.axis_size("row")
    grid_cols = n_c * lax.axis_size("col")
    coarse_rows, coarse_cols = grid_rows // 2, grid_cols // 2
    y0 = lax.axis_index("row") * n_r
    x0 = lax.axis_index("col") * n_c
    ys = y0 + jnp.arange(n_r, dtype=jnp.int32)
    xs = x0 + jnp.arange(n_c, dtype=jnp.int32)
    two = jnp.arange(2, dtype=jnp.int32)

    agg_y = mirror((ys - 1)[:, None] // 2 + two, coarse_rows)
    agg_x = mirror((xs - 1)[:, None] // 2 + two, coarse_cols)
    wanted = (agg_y[:, None, :, None] * coarse_cols + agg_x[None, :, None, :]).reshape(n_r, n_c, 4)
    match = p_cols[:, :, None, :] == wanted[:, :, :, None]
    canon = jnp.sum(
        jnp.where(match[..., None, None], p_blocks[:, :, None], jnp.zeros((), p_blocks.dtype)),
        axis=3,
        dtype=p_blocks.dtype,
    )
    p_ext = with_halo(canon)
    ext_r, ext_c = n_r + 2, n_c + 2

    near_y = a_cols // grid_cols
    near_x = a_cols % grid_cols
    near = jnp.clip(near_y - (y0 - 1), 0, ext_r - 1) * ext_c + jnp.clip(near_x - (x0 - 1), 0, ext_c - 1)
    near_agg_y = mirror((near_y - 1)[..., None] // 2 + two, coarse_rows)
    near_agg_x = mirror((near_x - 1)[..., None] // 2 + two, coarse_cols)
    slot_y = near_agg_y - (ys // 2 - 1)[:, None, None, None]
    slot_x = near_agg_x - (xs // 2 - 1)[None, :, None, None]
    slot = (slot_y[..., :, None] * 3 + slot_x[..., None, :]).reshape(n_r, n_c, terms, 4)
    slot = jnp.where((slot >= 0) & (slot < 9), slot, -1)

    ap = pl.pallas_call(
        ap_kernel,
        out_shape=jax.ShapeDtypeStruct((n_r * n_c, 9, bs, bs), jnp.bfloat16),
        in_specs=[
            pl.BlockSpec(memory_space=pltpu.SMEM),
            pl.BlockSpec(memory_space=pltpu.SMEM),
            pl.BlockSpec(memory_space=pltpu.VMEM),
            pl.BlockSpec(memory_space=pltpu.VMEM),
        ],
        out_specs=pl.BlockSpec(memory_space=pltpu.VMEM),
        scratch_shapes=[pltpu.VMEM((9, bs, bs), jnp.float32)],
    )(
        near.reshape(-1),
        slot.reshape(-1),
        a_blocks.reshape(n_r * n_c, terms, bs, bs),
        p_ext.reshape(ext_r * ext_c, 4, bs, bs),
    )
    ap_ext = with_halo(ap.reshape(n_r, n_c, 9, bs, bs))

    o_r, o_c = n_r // 2, n_c // 2
    ey = y0 - 1 + jnp.arange(ext_r, dtype=jnp.int32)
    ex = x0 - 1 + jnp.arange(ext_c, dtype=jnp.int32)
    e_agg_y = mirror((ey - 1)[:, None] // 2 + two, coarse_rows)
    e_agg_x = mirror((ex - 1)[:, None] // 2 + two, coarse_cols)
    own_y = e_agg_y - y0 // 2
    own_x = e_agg_x - x0 // 2
    off_y = (ey // 2 - 1)[:, None] - e_agg_y + 2
    off_x = (ex // 2 - 1)[:, None] - e_agg_x + 2
    ok_y = (ey >= 0)[:, None] & (ey < grid_rows)[:, None] & (own_y >= 0) & (own_y < o_r) & (off_y >= 0) & (off_y <= 2)
    ok_x = (ex >= 0)[:, None] & (ex < grid_cols)[:, None] & (own_x >= 0) & (own_x < o_c) & (off_x >= 0) & (off_x <= 2)
    target = (own_y[:, None, :, None] * o_c + own_x[None, :, None, :]) * 25 + (
        off_y[:, None, :, None] * 5 + off_x[None, :, None, :]
    )
    target = jnp.where(ok_y[:, None, :, None] & ok_x[None, :, None, :], target, -1).reshape(-1)

    cy = ys[0] // 2 + jnp.arange(o_r, dtype=jnp.int32)
    cx = xs[0] // 2 + jnp.arange(o_c, dtype=jnp.int32)
    pick = (c_cols // coarse_cols - cy[:, None, None] + 2) * 5 + (c_cols % coarse_cols - cx[None, :, None] + 2)
    pick = jnp.clip(pick, 0, 24).reshape(-1)

    p_t = jnp.swapaxes(p_ext, -1, -2).reshape(ext_r * ext_c, 4, bs, bs)
    stencil = c_cols.shape[-1]
    out = pl.pallas_call(
        coarse_kernel,
        out_shape=jax.ShapeDtypeStruct((o_r * o_c, stencil, bs, bs), jnp.bfloat16),
        in_specs=[
            pl.BlockSpec(memory_space=pltpu.SMEM),
            pl.BlockSpec(memory_space=pltpu.SMEM),
            pl.BlockSpec(memory_space=pltpu.VMEM),
            pl.BlockSpec(memory_space=pltpu.VMEM),
        ],
        out_specs=pl.BlockSpec(memory_space=pltpu.VMEM),
        scratch_shapes=[pltpu.VMEM((o_r * o_c * 25, bs, bs), jnp.float32)],
    )(target, pick, ap_ext.reshape(ext_r * ext_c, 9, bs, bs), p_t)
    return out.reshape(o_r, o_c, stencil, bs, bs)


def solution(mesh):
    return jax.shard_map(
        body,
        mesh=mesh,
        in_specs=(
            P("row", "col", None, None, None),
            P("row", "col", None),
            P("row", "col", None, None, None),
            P("row", "col", None),
            P("row", "col", None),
        ),
        out_specs=P("row", "col", None, None, None),
        check_vma=False,
    )
```

```python
import jax
import jax.numpy as jnp
from jax import lax
from jax.experimental import pallas as pl
from jax.experimental.pallas import tpu as pltpu
from jax.sharding import PartitionSpec as P


def mirror(values, limit):
    values = jnp.where(values < 0, -values, values)
    return jnp.where(values >= limit, 2 * (limit - 1) - values, values)


def shifted(piece, down, right):
    rows, cols = lax.axis_size("row"), lax.axis_size("col")
    if right == 0:
        pairs = [(s, s + down) for s in range(rows) if 0 <= s + down < rows]
        return lax.ppermute(piece, "row", pairs)
    if down == 0:
        pairs = [(s, s + right) for s in range(cols) if 0 <= s + right < cols]
        return lax.ppermute(piece, "col", pairs)
    pairs = []
    for sr in range(rows):
        for sc in range(cols):
            tr, tc = sr + down, sc + right
            if 0 <= tr < rows and 0 <= tc < cols:
                pairs.append((sr * cols + sc, tr * cols + tc))
    return lax.ppermute(piece, ("row", "col"), pairs)


def with_halo(x):
    top = shifted(x[-1], 1, 0)
    bottom = shifted(x[0], -1, 0)
    left = shifted(x[:, -1], 0, 1)
    right = shifted(x[:, 0], 0, -1)
    top_left = shifted(x[-1, -1], 1, 1)
    top_right = shifted(x[-1, 0], 1, -1)
    bottom_left = shifted(x[0, -1], -1, 1)
    bottom_right = shifted(x[0, 0], -1, -1)
    first = jnp.concatenate([top_left[None], top, top_right[None]], axis=0)
    last = jnp.concatenate([bottom_left[None], bottom, bottom_right[None]], axis=0)
    middle = jnp.concatenate([left[:, None], x, right[:, None]], axis=1)
    return jnp.concatenate([first[None], middle, last[None]], axis=0)


def ap_kernel(near_ref, slot_ref, a_ref, p_ref, out_ref, acc_ref):
    tiles, terms = a_ref.shape[0], a_ref.shape[1]

    def one_tile(t, carry):
        acc_ref[...] = jnp.zeros(acc_ref.shape, jnp.float32)
        for k in range(terms):
            j = near_ref[t * terms + k]
            a = a_ref[t, k]
            for q in range(4):
                e = slot_ref[(t * terms + k) * 4 + q]
                keep = jnp.where(e >= 0, 1.0, 0.0).astype(jnp.float32)
                prod = jnp.dot(a, p_ref[j, q], preferred_element_type=jnp.float32)
                acc_ref[jnp.clip(e, 0, 8)] += prod * keep

        out_ref[t] = acc_ref[...].astype(out_ref.dtype)
        return carry

    lax.fori_loop(0, tiles, one_tile, 0)


def add_terms(where_ref, target_ref, ap_ref, pt_ref, acc_ref):
    def one_tile(t, carry):
        w = where_ref[t]
        for q in range(4):
            g = target_ref[t * 4 + q]

            @pl.when(g >= 0)
            def _():
                pt = pt_ref[w * 4 + q]
                for e in range(9):
                    acc_ref[g + (e // 3) * 5 + e % 3] += jnp.dot(
                        pt, ap_ref[t, e], preferred_element_type=jnp.float32
                    )

        return carry

    lax.fori_loop(0, ap_ref.shape[0], one_tile, 0)


def own_kernel(where_ref, target_ref, ap_ref, pt_ref, acc_ref):
    acc_ref[...] = jnp.zeros(acc_ref.shape, jnp.float32)
    add_terms(where_ref, target_ref, ap_ref, pt_ref, acc_ref)


def ring_kernel(where_ref, target_ref, pick_ref, ap_ref, pt_ref, part_ref, out_ref, acc_ref):
    acc_ref[...] = part_ref[...]
    add_terms(where_ref, target_ref, ap_ref, pt_ref, acc_ref)
    owned, stencil = out_ref.shape[0], out_ref.shape[1]

    def one_pick(i, carry):
        a = i // stencil
        out_ref[a, i % stencil] = acc_ref[a * stencil + pick_ref[i]].astype(out_ref.dtype)
        return carry

    lax.fori_loop(0, owned * stencil, one_pick, 0)


def ring_of(x):
    return jnp.concatenate([x[0], x[-1], x[1:-1, 0], x[1:-1, -1]], axis=0)


def body(a_blocks, a_cols, p_blocks, p_cols, c_cols):
    n_r, n_c = a_blocks.shape[0], a_blocks.shape[1]
    bs = a_blocks.shape[-1]
    terms = a_blocks.shape[2]
    grid_rows = n_r * lax.axis_size("row")
    grid_cols = n_c * lax.axis_size("col")
    coarse_rows, coarse_cols = grid_rows // 2, grid_cols // 2
    y0 = lax.axis_index("row") * n_r
    x0 = lax.axis_index("col") * n_c
    ys = y0 + jnp.arange(n_r, dtype=jnp.int32)
    xs = x0 + jnp.arange(n_c, dtype=jnp.int32)
    two = jnp.arange(2, dtype=jnp.int32)

    agg_y = mirror((ys - 1)[:, None] // 2 + two, coarse_rows)
    agg_x = mirror((xs - 1)[:, None] // 2 + two, coarse_cols)
    wanted = (agg_y[:, None, :, None] * coarse_cols + agg_x[None, :, None, :]).reshape(n_r, n_c, 4)
    match = p_cols[:, :, None, :] == wanted[:, :, :, None]
    canon = jnp.sum(
        jnp.where(match[..., None, None], p_blocks[:, :, None], jnp.zeros((), p_blocks.dtype)),
        axis=3,
        dtype=p_blocks.dtype,
    )
    p_ext = with_halo(canon)
    ext_r, ext_c = n_r + 2, n_c + 2

    near_y = a_cols // grid_cols
    near_x = a_cols % grid_cols
    near = jnp.clip(near_y - (y0 - 1), 0, ext_r - 1) * ext_c + jnp.clip(near_x - (x0 - 1), 0, ext_c - 1)
    near_agg_y = mirror((near_y - 1)[..., None] // 2 + two, coarse_rows)
    near_agg_x = mirror((near_x - 1)[..., None] // 2 + two, coarse_cols)
    slot_y = near_agg_y - (ys // 2 - 1)[:, None, None, None]
    slot_x = near_agg_x - (xs // 2 - 1)[None, :, None, None]
    slot = (slot_y[..., :, None] * 3 + slot_x[..., None, :]).reshape(n_r, n_c, terms, 4)
    slot = jnp.where((slot >= 0) & (slot < 9), slot, -1)

    ap = pl.pallas_call(
        ap_kernel,
        out_shape=jax.ShapeDtypeStruct((n_r * n_c, 9, bs, bs), jnp.bfloat16),
        in_specs=[
            pl.BlockSpec(memory_space=pltpu.SMEM),
            pl.BlockSpec(memory_space=pltpu.SMEM),
            pl.BlockSpec(memory_space=pltpu.VMEM),
            pl.BlockSpec(memory_space=pltpu.VMEM),
        ],
        out_specs=pl.BlockSpec(memory_space=pltpu.VMEM),
        scratch_shapes=[pltpu.VMEM((9, bs, bs), jnp.float32)],
    )(
        near.reshape(-1),
        slot.reshape(-1),
        a_blocks.reshape(n_r * n_c, terms, bs, bs),
        p_ext.reshape(ext_r * ext_c, 4, bs, bs),
    )
    ap = ap.reshape(n_r, n_c, 9, bs, bs)
    ap_ext = with_halo(ap)

    o_r, o_c = n_r // 2, n_c // 2
    ey = y0 - 1 + jnp.arange(ext_r, dtype=jnp.int32)
    ex = x0 - 1 + jnp.arange(ext_c, dtype=jnp.int32)
    e_agg_y = mirror((ey - 1)[:, None] // 2 + two, coarse_rows)
    e_agg_x = mirror((ex - 1)[:, None] // 2 + two, coarse_cols)
    own_y = e_agg_y - y0 // 2
    own_x = e_agg_x - x0 // 2
    off_y = (ey // 2 - 1)[:, None] - e_agg_y + 2
    off_x = (ex // 2 - 1)[:, None] - e_agg_x + 2
    ok_y = (ey >= 0)[:, None] & (ey < grid_rows)[:, None] & (own_y >= 0) & (own_y < o_r) & (off_y >= 0) & (off_y <= 2)
    ok_x = (ex >= 0)[:, None] & (ex < grid_cols)[:, None] & (own_x >= 0) & (own_x < o_c) & (off_x >= 0) & (off_x <= 2)
    target = (own_y[:, None, :, None] * o_c + own_x[None, :, None, :]) * 25 + (
        off_y[:, None, :, None] * 5 + off_x[None, :, None, :]
    )
    target = jnp.where(ok_y[:, None, :, None] & ok_x[None, :, None, :], target, -1).reshape(ext_r, ext_c, 4)
    place = jnp.arange(ext_r * ext_c, dtype=jnp.int32).reshape(ext_r, ext_c)

    cy = ys[0] // 2 + jnp.arange(o_r, dtype=jnp.int32)
    cx = xs[0] // 2 + jnp.arange(o_c, dtype=jnp.int32)
    pick = (c_cols // coarse_cols - cy[:, None, None] + 2) * 5 + (c_cols % coarse_cols - cx[None, :, None] + 2)
    pick = jnp.clip(pick, 0, 24).reshape(-1)

    p_t = jnp.swapaxes(p_ext, -1, -2).reshape(ext_r * ext_c * 4, bs, bs)
    stencil = c_cols.shape[-1]
    acc_shape = jax.ShapeDtypeStruct((o_r * o_c * 25, bs, bs), jnp.float32)
    dot_cost = 2 * bs * bs * bs * 9
    part = pl.pallas_call(
        own_kernel,
        out_shape=acc_shape,
        in_specs=[pl.BlockSpec(memory_space=pltpu.SMEM)] * 2 + [pl.BlockSpec(memory_space=pltpu.VMEM)] * 2,
        out_specs=pl.BlockSpec(memory_space=pltpu.VMEM),
        cost_estimate=pl.CostEstimate(
            flops=dot_cost * n_r * n_c * 4, bytes_accessed=4 * 1024 * 1024, transcendentals=0
        ),
    )(
        place[1:-1, 1:-1].reshape(-1),
        target[1:-1, 1:-1].reshape(-1),
        ap.reshape(n_r * n_c, 9, bs, bs),
        p_t,
    )
    ring_tiles = 2 * ext_c + 2 * n_r
    out = pl.pallas_call(
        ring_kernel,
        out_shape=jax.ShapeDtypeStruct((o_r * o_c, stencil, bs, bs), jnp.bfloat16),
        in_specs=[pl.BlockSpec(memory_space=pltpu.SMEM)] * 3 + [pl.BlockSpec(memory_space=pltpu.VMEM)] * 3,
        out_specs=pl.BlockSpec(memory_space=pltpu.VMEM),
        scratch_shapes=[pltpu.VMEM(acc_shape.shape, jnp.float32)],
        cost_estimate=pl.CostEstimate(
            flops=dot_cost * ring_tiles * 4, bytes_accessed=5 * 1024 * 1024, transcendentals=0
        ),
    )(
        ring_of(place),
        ring_of(target).reshape(-1),
        pick,
        ring_of(ap_ext),
        p_t,
        part,
    )
    return out.reshape(o_r, o_c, stencil, bs, bs)


def solution(mesh):
    return jax.shard_map(
        body,
        mesh=mesh,
        in_specs=(
            P("row", "col", None, None, None),
            P("row", "col", None),
            P("row", "col", None, None, None),
            P("row", "col", None),
            P("row", "col", None),
        ),
        out_specs=P("row", "col", None, None, None),
        check_vma=False,
    )
```

```python
import math

import jax
import jax.numpy as jnp
from jax import lax
from jax.experimental import pallas as pl
from jax.experimental.pallas import tpu as pltpu
from jax.sharding import PartitionSpec as P


def mirror(values, limit):
    values = jnp.where(values < 0, -values, values)
    return jnp.where(values >= limit, 2 * (limit - 1) - values, values)


def shifted(piece, down, right):
    rows, cols = lax.axis_size("row"), lax.axis_size("col")
    if right == 0:
        pairs = [(s, s + down) for s in range(rows) if 0 <= s + down < rows]
        return lax.ppermute(piece, "row", pairs)
    if down == 0:
        pairs = [(s, s + right) for s in range(cols) if 0 <= s + right < cols]
        return lax.ppermute(piece, "col", pairs)
    pairs = []
    for sr in range(rows):
        for sc in range(cols):
            tr, tc = sr + down, sc + right
            if 0 <= tr < rows and 0 <= tc < cols:
                pairs.append((sr * cols + sc, tr * cols + tc))
    return lax.ppermute(piece, ("row", "col"), pairs)


def edge(x, step, width, axis):
    if step == 1:
        return lax.slice_in_dim(x, x.shape[axis] - width, None, axis=axis)
    if step == -1:
        return lax.slice_in_dim(x, 0, width, axis=axis)
    return x


def with_rings(arrays):
    got = {}
    for down in (1, 0, -1):
        for right in (1, 0, -1):
            if down == 0 and right == 0:
                continue
            pieces = [edge(edge(x, down, w, 0), right, w, 1) for x, w in arrays]
            packed = jnp.concatenate([p.reshape((-1,) + p.shape[-2:]) for p in pieces], axis=0)
            arrived = shifted(packed, down, right)
            parts, start = [], 0
            for p in pieces:
                count = math.prod(p.shape[:-2])
                parts.append(arrived[start : start + count].reshape(p.shape))
                start += count
            got[(down, right)] = parts
    out = []
    for i, (x, _) in enumerate(arrays):
        g = lambda d, r: got[(d, r)][i]
        top = jnp.concatenate([g(1, 1), g(1, 0), g(1, -1)], axis=1)
        middle = jnp.concatenate([g(0, 1), x, g(0, -1)], axis=1)
        bottom = jnp.concatenate([g(-1, 1), g(-1, 0), g(-1, -1)], axis=1)
        out.append(jnp.concatenate([top, middle, bottom], axis=0))
    return out


def galerkin_kernel(
    near_ref, slot_ref, target_ref, pick_ref, a_ref, p_ref, pt_ref, out_ref, ap_ref, sum_ref, acc_ref
):
    tiles, terms = a_ref.shape[0], a_ref.shape[1]

    def form(t, carry):
        sum_ref[...] = jnp.zeros(sum_ref.shape, jnp.float32)
        for k in range(terms):
            j = near_ref[t * terms + k]
            a = a_ref[t, k]
            for q in range(4):
                e = slot_ref[(t * terms + k) * 4 + q]
                keep = jnp.where(e >= 0, 1.0, 0.0).astype(jnp.float32)
                prod = jnp.dot(a, p_ref[j, q], preferred_element_type=jnp.float32)
                sum_ref[jnp.clip(e, 0, 8)] += prod * keep

        ap_ref[t] = sum_ref[...].astype(ap_ref.dtype)
        return carry

    lax.fori_loop(0, tiles, form, 0)
    acc_ref[...] = jnp.zeros(acc_ref.shape, jnp.float32)

    def add(t, carry):
        for q in range(4):
            g = target_ref[t * 4 + q]

            @pl.when(g >= 0)
            def _():
                pt = pt_ref[t * 4 + q]
                for e in range(9):
                    acc_ref[g + (e // 3) * 5 + e % 3] += jnp.dot(
                        pt, ap_ref[t, e], preferred_element_type=jnp.float32
                    )

        return carry

    lax.fori_loop(0, tiles, add, 0)
    owned, stencil = out_ref.shape[0], out_ref.shape[1]

    def one_pick(i, carry):
        a = i // stencil
        out_ref[a, i % stencil] = acc_ref[a * stencil + pick_ref[i]].astype(out_ref.dtype)
        return carry

    lax.fori_loop(0, owned * stencil, one_pick, 0)


def rank_among_equal(values):
    n = values.shape[-1]
    same = values[..., :, None] == values[..., None, :]
    earlier = jnp.arange(n)[None, :] < jnp.arange(n)[:, None]
    return jnp.sum(same & earlier, axis=-1, dtype=jnp.int32)


def body(a_blocks, a_cols, p_blocks, p_cols, c_cols):
    n_r, n_c = a_blocks.shape[0], a_blocks.shape[1]
    bs = a_blocks.shape[-1]
    terms = a_blocks.shape[2]
    grid_rows = n_r * lax.axis_size("row")
    grid_cols = n_c * lax.axis_size("col")
    coarse_rows, coarse_cols = grid_rows // 2, grid_cols // 2
    y0 = lax.axis_index("row") * n_r
    x0 = lax.axis_index("col") * n_c
    ys = y0 + jnp.arange(n_r, dtype=jnp.int32)
    xs = x0 + jnp.arange(n_c, dtype=jnp.int32)
    two = jnp.arange(2, dtype=jnp.int32)
    dirs = jnp.arange(terms, dtype=jnp.int32)
    dir_y, dir_x = dirs // 3 - 1, dirs % 3 - 1
    zero = jnp.zeros((), a_blocks.dtype)

    agg_y = mirror((ys - 1)[:, None] // 2 + two, coarse_rows)
    agg_x = mirror((xs - 1)[:, None] // 2 + two, coarse_cols)
    wanted = (agg_y[:, None, :, None] * coarse_cols + agg_x[None, :, None, :]).reshape(n_r, n_c, 4)
    match = p_cols[:, :, None, :] == wanted[:, :, :, None]
    p_canon = jnp.sum(jnp.where(match[..., None, None], p_blocks[:, :, None], zero), axis=3, dtype=zero.dtype)

    to_y = mirror(ys[:, None] + dir_y, grid_rows)
    to_x = mirror(xs[:, None] + dir_x, grid_cols)
    to = to_y[:, None, :] * grid_cols + to_x[None, :, :]
    match = (a_cols[:, :, None, :] == to[:, :, :, None]) & (
        rank_among_equal(a_cols)[:, :, None, :] == rank_among_equal(to)[:, :, :, None]
    )
    a_canon = jnp.sum(jnp.where(match[..., None, None], a_blocks[:, :, None], zero), axis=3, dtype=zero.dtype)

    a_ext, p_ext = with_rings([(a_canon, 1), (p_canon, 2)])
    ext_r, ext_c = n_r + 2, n_c + 2
    wide_r, wide_c = n_r + 4, n_c + 4

    ey = y0 - 1 + jnp.arange(ext_r, dtype=jnp.int32)
    ex = x0 - 1 + jnp.arange(ext_c, dtype=jnp.int32)
    real_y = (ey >= 0) & (ey < grid_rows)
    real_x = (ex >= 0) & (ex < grid_cols)
    ny = mirror(ey[:, None] + dir_y, grid_rows)
    nx = mirror(ex[:, None] + dir_x, grid_cols)
    near = (
        jnp.clip(ny - (y0 - 2), 0, wide_r - 1)[:, None, :] * wide_c
        + jnp.clip(nx - (x0 - 2), 0, wide_c - 1)[None, :, :]
    )
    slot_y = mirror((ny - 1)[..., None] // 2 + two, coarse_rows) - (ey // 2 - 1)[:, None, None]
    slot_x = mirror((nx - 1)[..., None] // 2 + two, coarse_cols) - (ex // 2 - 1)[:, None, None]
    slot = slot_y[:, None, :, :, None] * 3 + slot_x[None, :, :, None, :]
    real = real_y[:, None, None, None, None] & real_x[None, :, None, None, None]
    slot = jnp.where(real & (slot >= 0) & (slot < 9), slot, -1)

    o_r, o_c = n_r // 2, n_c // 2
    e_agg_y = mirror((ey - 1)[:, None] // 2 + two, coarse_rows)
    e_agg_x = mirror((ex - 1)[:, None] // 2 + two, coarse_cols)
    own_y = e_agg_y - y0 // 2
    own_x = e_agg_x - x0 // 2
    off_y = (ey // 2 - 1)[:, None] - e_agg_y + 2
    off_x = (ex // 2 - 1)[:, None] - e_agg_x + 2
    ok_y = real_y[:, None] & (own_y >= 0) & (own_y < o_r) & (off_y >= 0) & (off_y <= 2)
    ok_x = real_x[:, None] & (own_x >= 0) & (own_x < o_c) & (off_x >= 0) & (off_x <= 2)
    target = (own_y[:, None, :, None] * o_c + own_x[None, :, None, :]) * 25 + (
        off_y[:, None, :, None] * 5 + off_x[None, :, None, :]
    )
    target = jnp.where(ok_y[:, None, :, None] & ok_x[None, :, None, :], target, -1)

    cy = y0 // 2 + jnp.arange(o_r, dtype=jnp.int32)
    cx = x0 // 2 + jnp.arange(o_c, dtype=jnp.int32)
    pick = (c_cols // coarse_cols - cy[:, None, None] + 2) * 5 + (c_cols % coarse_cols - cx[None, :, None] + 2)
    pick = jnp.clip(pick, 0, 24)

    p_t = jnp.swapaxes(p_ext[1:-1, 1:-1], -1, -2).reshape(ext_r * ext_c * 4, bs, bs)
    stencil = c_cols.shape[-1]
    tiles = ext_r * ext_c
    smem = pl.BlockSpec(memory_space=pltpu.SMEM)
    vmem = pl.BlockSpec(memory_space=pltpu.VMEM)
    out = pl.pallas_call(
        galerkin_kernel,
        out_shape=jax.ShapeDtypeStruct((o_r * o_c, stencil, bs, bs), jnp.bfloat16),
        in_specs=[smem] * 4 + [vmem] * 3,
        out_specs=vmem,
        scratch_shapes=[
            pltpu.VMEM((tiles, 9, bs, bs), jnp.bfloat16),
            pltpu.VMEM((9, bs, bs), jnp.float32),
            pltpu.VMEM((o_r * o_c * 25, bs, bs), jnp.float32),
        ],
        compiler_params=pltpu.CompilerParams(vmem_limit_bytes=48 * 1024 * 1024),
    )(
        near.reshape(-1),
        slot.reshape(-1),
        target.reshape(-1),
        pick.reshape(-1),
        a_ext.reshape(tiles, terms, bs, bs),
        p_ext.reshape(wide_r * wide_c, 4, bs, bs),
        p_t,
    )
    return out.reshape(o_r, o_c, stencil, bs, bs)


def solution(mesh):
    return jax.shard_map(
        body,
        mesh=mesh,
        in_specs=(
            P("row", "col", None, None, None),
            P("row", "col", None),
            P("row", "col", None, None, None),
            P("row", "col", None),
            P("row", "col", None),
        ),
        out_specs=P("row", "col", None, None, None),
        check_vma=False,
    )
```

```python
import jax
import jax.numpy as jnp
from jax import lax
from jax.experimental import pallas as pl
from jax.experimental.pallas import tpu as pltpu
from jax.sharding import PartitionSpec as P


def mirror(values, limit):
    values = jnp.where(values < 0, -values, values)
    return jnp.where(values >= limit, 2 * (limit - 1) - values, values)


def shifted(piece, down, right):
    rows, cols = lax.axis_size("row"), lax.axis_size("col")
    if right == 0:
        pairs = [(s, s + down) for s in range(rows) if 0 <= s + down < rows]
        return lax.ppermute(piece, "row", pairs)
    if down == 0:
        pairs = [(s, s + right) for s in range(cols) if 0 <= s + right < cols]
        return lax.ppermute(piece, "col", pairs)
    pairs = []
    for sr in range(rows):
        for sc in range(cols):
            tr, tc = sr + down, sc + right
            if 0 <= tr < rows and 0 <= tc < cols:
                pairs.append((sr * cols + sc, tr * cols + tc))
    return lax.ppermute(piece, ("row", "col"), pairs)


def dense_shifted(piece, down, right):
    rows, cols = piece.shape[-2], piece.shape[-1]
    lanes = 128 if (rows * cols) % 128 == 0 and cols < 128 else cols
    packed = piece.reshape(piece.shape[:-2] + (rows * cols // lanes, lanes))
    return shifted(packed, down, right).reshape(piece.shape)


def with_halo(x):
    top = dense_shifted(x[-1], 1, 0)
    bottom = dense_shifted(x[0], -1, 0)
    left = dense_shifted(x[:, -1], 0, 1)
    right = dense_shifted(x[:, 0], 0, -1)
    top_left = dense_shifted(x[-1, -1], 1, 1)
    top_right = dense_shifted(x[-1, 0], 1, -1)
    bottom_left = dense_shifted(x[0, -1], -1, 1)
    bottom_right = dense_shifted(x[0, 0], -1, -1)
    first = jnp.concatenate([top_left[None], top, top_right[None]], axis=0)
    last = jnp.concatenate([bottom_left[None], bottom, bottom_right[None]], axis=0)
    middle = jnp.concatenate([left[:, None], x, right[:, None]], axis=1)
    return jnp.concatenate([first[None], middle, last[None]], axis=0)


def ap_kernel(near_ref, slot_ref, a_ref, p_ref, out_ref, acc_ref):
    tiles, terms = a_ref.shape[0], a_ref.shape[1]

    def one_tile(t, carry):
        acc_ref[...] = jnp.zeros(acc_ref.shape, jnp.float32)
        for k in range(terms):
            j = near_ref[t * terms + k]
            a = a_ref[t, k]
            for q in range(4):
                e = slot_ref[(t * terms + k) * 4 + q]
                keep = jnp.where(e >= 0, 1.0, 0.0).astype(jnp.float32)
                prod = jnp.dot(a, p_ref[j, q], preferred_element_type=jnp.float32)
                acc_ref[jnp.clip(e, 0, 8)] += prod * keep

        out_ref[t] = acc_ref[...].astype(out_ref.dtype)
        return carry

    lax.fori_loop(0, tiles, one_tile, 0)


def add_terms(where_ref, target_ref, ap_ref, pt_ref, acc_ref):
    def one_tile(t, carry):
        w = where_ref[t]
        for q in range(4):
            g = target_ref[t * 4 + q]

            @pl.when(g >= 0)
            def _():
                pt = pt_ref[w * 4 + q]
                for e in range(9):
                    acc_ref[g + (e // 3) * 5 + e % 3] += jnp.dot(
                        pt, ap_ref[t, e], preferred_element_type=jnp.float32
                    )

        return carry

    lax.fori_loop(0, ap_ref.shape[0], one_tile, 0)


def own_kernel(where_ref, target_ref, ap_ref, pt_ref, acc_ref):
    acc_ref[...] = jnp.zeros(acc_ref.shape, jnp.float32)
    add_terms(where_ref, target_ref, ap_ref, pt_ref, acc_ref)


def ring_kernel(where_ref, target_ref, pick_ref, ap_ref, pt_ref, part_ref, out_ref, acc_ref):
    acc_ref[...] = part_ref[...]
    add_terms(where_ref, target_ref, ap_ref, pt_ref, acc_ref)
    owned, stencil = out_ref.shape[0], out_ref.shape[1]

    def one_pick(i, carry):
        a = i // stencil
        out_ref[a, i % stencil] = acc_ref[a * stencil + pick_ref[i]].astype(out_ref.dtype)
        return carry

    lax.fori_loop(0, owned * stencil, one_pick, 0)


def ring_of(x):
    return jnp.concatenate([x[0], x[-1], x[1:-1, 0], x[1:-1, -1]], axis=0)


def body(a_blocks, a_cols, p_blocks, p_cols, c_cols):
    n_r, n_c = a_blocks.shape[0], a_blocks.shape[1]
    bs = a_blocks.shape[-1]
    terms = a_blocks.shape[2]
    grid_rows = n_r * lax.axis_size("row")
    grid_cols = n_c * lax.axis_size("col")
    coarse_rows, coarse_cols = grid_rows // 2, grid_cols // 2
    y0 = lax.axis_index("row") * n_r
    x0 = lax.axis_index("col") * n_c
    ys = y0 + jnp.arange(n_r, dtype=jnp.int32)
    xs = x0 + jnp.arange(n_c, dtype=jnp.int32)
    two = jnp.arange(2, dtype=jnp.int32)

    agg_y = mirror((ys - 1)[:, None] // 2 + two, coarse_rows)
    agg_x = mirror((xs - 1)[:, None] // 2 + two, coarse_cols)
    wanted = (agg_y[:, None, :, None] * coarse_cols + agg_x[None, :, None, :]).reshape(n_r, n_c, 4)
    match = p_cols[:, :, None, :] == wanted[:, :, :, None]
    canon = jnp.sum(
        jnp.where(match[..., None, None], p_blocks[:, :, None], jnp.zeros((), p_blocks.dtype)),
        axis=3,
        dtype=p_blocks.dtype,
    )
    p_ext = with_halo(canon)
    ext_r, ext_c = n_r + 2, n_c + 2

    near_y = a_cols // grid_cols
    near_x = a_cols % grid_cols
    near = jnp.clip(near_y - (y0 - 1), 0, ext_r - 1) * ext_c + jnp.clip(near_x - (x0 - 1), 0, ext_c - 1)
    near_agg_y = mirror((near_y - 1)[..., None] // 2 + two, coarse_rows)
    near_agg_x = mirror((near_x - 1)[..., None] // 2 + two, coarse_cols)
    slot_y = near_agg_y - (ys // 2 - 1)[:, None, None, None]
    slot_x = near_agg_x - (xs // 2 - 1)[None, :, None, None]
    slot = (slot_y[..., :, None] * 3 + slot_x[..., None, :]).reshape(n_r, n_c, terms, 4)
    slot = jnp.where((slot >= 0) & (slot < 9), slot, -1)

    ap = pl.pallas_call(
        ap_kernel,
        out_shape=jax.ShapeDtypeStruct((n_r * n_c, 9, bs, bs), jnp.bfloat16),
        in_specs=[
            pl.BlockSpec(memory_space=pltpu.SMEM),
            pl.BlockSpec(memory_space=pltpu.SMEM),
            pl.BlockSpec(memory_space=pltpu.VMEM),
            pl.BlockSpec(memory_space=pltpu.VMEM),
        ],
        out_specs=pl.BlockSpec(memory_space=pltpu.VMEM),
        scratch_shapes=[pltpu.VMEM((9, bs, bs), jnp.float32)],
    )(
        near.reshape(-1),
        slot.reshape(-1),
        a_blocks.reshape(n_r * n_c, terms, bs, bs),
        p_ext.reshape(ext_r * ext_c, 4, bs, bs),
    )
    ap = ap.reshape(n_r, n_c, 9, bs, bs)
    ap_ext = with_halo(ap)

    o_r, o_c = n_r // 2, n_c // 2
    ey = y0 - 1 + jnp.arange(ext_r, dtype=jnp.int32)
    ex = x0 - 1 + jnp.arange(ext_c, dtype=jnp.int32)
    e_agg_y = mirror((ey - 1)[:, None] // 2 + two, coarse_rows)
    e_agg_x = mirror((ex - 1)[:, None] // 2 + two, coarse_cols)
    own_y = e_agg_y - y0 // 2
    own_x = e_agg_x - x0 // 2
    off_y = (ey // 2 - 1)[:, None] - e_agg_y + 2
    off_x = (ex // 2 - 1)[:, None] - e_agg_x + 2
    ok_y = (ey >= 0)[:, None] & (ey < grid_rows)[:, None] & (own_y >= 0) & (own_y < o_r) & (off_y >= 0) & (off_y <= 2)
    ok_x = (ex >= 0)[:, None] & (ex < grid_cols)[:, None] & (own_x >= 0) & (own_x < o_c) & (off_x >= 0) & (off_x <= 2)
    target = (own_y[:, None, :, None] * o_c + own_x[None, :, None, :]) * 25 + (
        off_y[:, None, :, None] * 5 + off_x[None, :, None, :]
    )
    target = jnp.where(ok_y[:, None, :, None] & ok_x[None, :, None, :], target, -1).reshape(ext_r, ext_c, 4)
    place = jnp.arange(ext_r * ext_c, dtype=jnp.int32).reshape(ext_r, ext_c)

    cy = ys[0] // 2 + jnp.arange(o_r, dtype=jnp.int32)
    cx = xs[0] // 2 + jnp.arange(o_c, dtype=jnp.int32)
    pick = (c_cols // coarse_cols - cy[:, None, None] + 2) * 5 + (c_cols % coarse_cols - cx[None, :, None] + 2)
    pick = jnp.clip(pick, 0, 24).reshape(-1)

    p_t = jnp.swapaxes(p_ext, -1, -2).reshape(ext_r * ext_c * 4, bs, bs)
    stencil = c_cols.shape[-1]
    acc_shape = jax.ShapeDtypeStruct((o_r * o_c * 25, bs, bs), jnp.float32)
    dot_cost = 2 * bs * bs * bs * 9
    part = pl.pallas_call(
        own_kernel,
        out_shape=acc_shape,
        in_specs=[pl.BlockSpec(memory_space=pltpu.SMEM)] * 2 + [pl.BlockSpec(memory_space=pltpu.VMEM)] * 2,
        out_specs=pl.BlockSpec(memory_space=pltpu.VMEM),
        cost_estimate=pl.CostEstimate(
            flops=dot_cost * n_r * n_c * 4, bytes_accessed=4 * 1024 * 1024, transcendentals=0
        ),
    )(
        place[1:-1, 1:-1].reshape(-1),
        target[1:-1, 1:-1].reshape(-1),
        ap.reshape(n_r * n_c, 9, bs, bs),
        p_t,
    )
    ring_tiles = 2 * ext_c + 2 * n_r
    out = pl.pallas_call(
        ring_kernel,
        out_shape=jax.ShapeDtypeStruct((o_r * o_c, stencil, bs, bs), jnp.bfloat16),
        in_specs=[pl.BlockSpec(memory_space=pltpu.SMEM)] * 3 + [pl.BlockSpec(memory_space=pltpu.VMEM)] * 3,
        out_specs=pl.BlockSpec(memory_space=pltpu.VMEM),
        scratch_shapes=[pltpu.VMEM(acc_shape.shape, jnp.float32)],
        cost_estimate=pl.CostEstimate(
            flops=dot_cost * ring_tiles * 4, bytes_accessed=5 * 1024 * 1024, transcendentals=0
        ),
    )(
        ring_of(place),
        ring_of(target).reshape(-1),
        pick,
        ring_of(ap_ext),
        p_t,
        part,
    )
    return out.reshape(o_r, o_c, stencil, bs, bs)


def solution(mesh):
    return jax.shard_map(
        body,
        mesh=mesh,
        in_specs=(
            P("row", "col", None, None, None),
            P("row", "col", None),
            P("row", "col", None, None, None),
            P("row", "col", None),
            P("row", "col", None),
        ),
        out_specs=P("row", "col", None, None, None),
        check_vma=False,
    )
```

```python
import jax
import jax.numpy as jnp
from jax import lax
from jax.experimental import pallas as pl
from jax.experimental.pallas import tpu as pltpu
from jax.sharding import PartitionSpec as P


def mirror(values, limit):
    values = jnp.where(values < 0, -values, values)
    return jnp.where(values >= limit, 2 * (limit - 1) - values, values)


def shifted(piece, down, right):
    rows, cols = lax.axis_size("row"), lax.axis_size("col")
    if right == 0:
        pairs = [(s, s + down) for s in range(rows) if 0 <= s + down < rows]
        return lax.ppermute(piece, "row", pairs)
    if down == 0:
        pairs = [(s, s + right) for s in range(cols) if 0 <= s + right < cols]
        return lax.ppermute(piece, "col", pairs)
    pairs = []
    for sr in range(rows):
        for sc in range(cols):
            tr, tc = sr + down, sc + right
            if 0 <= tr < rows and 0 <= tc < cols:
                pairs.append((sr * cols + sc, tr * cols + tc))
    return lax.ppermute(piece, ("row", "col"), pairs)


def dense_shifted(piece, down, right):
    rows, cols = piece.shape[-2], piece.shape[-1]
    lanes = 128 if (rows * cols) % 128 == 0 and cols < 128 else cols
    packed = piece.reshape(piece.shape[:-2] + (rows * cols // lanes, lanes))
    return shifted(packed, down, right).reshape(piece.shape)


def halo_pieces(x):
    return {
        "left": dense_shifted(x[:, -1], 0, 1),
        "right": dense_shifted(x[:, 0], 0, -1),
        "top": dense_shifted(x[-1], 1, 0),
        "bottom": dense_shifted(x[0], -1, 0),
        "top_left": dense_shifted(x[-1, -1], 1, 1),
        "top_right": dense_shifted(x[-1, 0], 1, -1),
        "bottom_left": dense_shifted(x[0, -1], -1, 1),
        "bottom_right": dense_shifted(x[0, 0], -1, -1),
    }


def with_halo(x):
    h = halo_pieces(x)
    first = jnp.concatenate([h["top_left"][None], h["top"], h["top_right"][None]], axis=0)
    last = jnp.concatenate([h["bottom_left"][None], h["bottom"], h["bottom_right"][None]], axis=0)
    middle = jnp.concatenate([h["left"][:, None], x, h["right"][:, None]], axis=1)
    return jnp.concatenate([first[None], middle, last[None]], axis=0)


def halo_ring(x):
    h = halo_pieces(x)
    return jnp.concatenate(
        [
            h["top_left"][None],
            h["top"],
            h["top_right"][None],
            h["bottom_left"][None],
            h["bottom"],
            h["bottom_right"][None],
            h["left"],
            h["right"],
        ],
        axis=0,
    )


def ap_kernel(near_ref, slot_ref, a_ref, p_ref, out_ref, acc_ref):
    tiles, terms = a_ref.shape[0], a_ref.shape[1]

    def one_tile(t, carry):
        acc_ref[...] = jnp.zeros(acc_ref.shape, jnp.float32)
        for k in range(terms):
            j = near_ref[t * terms + k]
            a = a_ref[t, k]
            for q in range(4):
                e = slot_ref[(t * terms + k) * 4 + q]
                keep = jnp.where(e >= 0, 1.0, 0.0).astype(jnp.float32)
                prod = jnp.dot(a, p_ref[j, q], preferred_element_type=jnp.float32)
                acc_ref[jnp.clip(e, 0, 8)] += prod * keep

        out_ref[t] = acc_ref[...].astype(out_ref.dtype)
        return carry

    lax.fori_loop(0, tiles, one_tile, 0)


def add_terms(where_ref, target_ref, ap_ref, pt_ref, acc_ref):
    def one_tile(t, carry):
        w = where_ref[t]
        for q in range(4):
            g = target_ref[t * 4 + q]

            @pl.when(g >= 0)
            def _():
                pt = pt_ref[w * 4 + q]
                for e in range(9):
                    acc_ref[g + (e // 3) * 5 + e % 3] += jnp.dot(
                        pt, ap_ref[t, e], preferred_element_type=jnp.float32
                    )

        return carry

    lax.fori_loop(0, ap_ref.shape[0], one_tile, 0)


def own_kernel(where_ref, target_ref, ap_ref, pt_ref, acc_ref):
    acc_ref[...] = jnp.zeros(acc_ref.shape, jnp.float32)
    add_terms(where_ref, target_ref, ap_ref, pt_ref, acc_ref)


def ring_kernel(where_ref, target_ref, pick_ref, ap_ref, pt_ref, part_ref, out_ref, acc_ref):
    acc_ref[...] = part_ref[...]
    add_terms(where_ref, target_ref, ap_ref, pt_ref, acc_ref)
    owned, stencil = out_ref.shape[0], out_ref.shape[1]

    def one_pick(i, carry):
        a = i // stencil
        out_ref[a, i % stencil] = acc_ref[a * stencil + pick_ref[i]].astype(out_ref.dtype)
        return carry

    lax.fori_loop(0, owned * stencil, one_pick, 0)


def ring_of(x):
    return jnp.concatenate([x[0], x[-1], x[1:-1, 0], x[1:-1, -1]], axis=0)


def body(a_blocks, a_cols, p_blocks, p_cols, c_cols):
    n_r, n_c = a_blocks.shape[0], a_blocks.shape[1]
    bs = a_blocks.shape[-1]
    terms = a_blocks.shape[2]
    grid_rows = n_r * lax.axis_size("row")
    grid_cols = n_c * lax.axis_size("col")
    coarse_rows, coarse_cols = grid_rows // 2, grid_cols // 2
    y0 = lax.axis_index("row") * n_r
    x0 = lax.axis_index("col") * n_c
    ys = y0 + jnp.arange(n_r, dtype=jnp.int32)
    xs = x0 + jnp.arange(n_c, dtype=jnp.int32)
    two = jnp.arange(2, dtype=jnp.int32)

    agg_y = mirror((ys - 1)[:, None] // 2 + two, coarse_rows)
    agg_x = mirror((xs - 1)[:, None] // 2 + two, coarse_cols)
    wanted = (agg_y[:, None, :, None] * coarse_cols + agg_x[None, :, None, :]).reshape(n_r, n_c, 4)
    match = p_cols[:, :, None, :] == wanted[:, :, :, None]
    canon = jnp.sum(
        jnp.where(match[..., None, None], p_blocks[:, :, None], jnp.zeros((), p_blocks.dtype)),
        axis=3,
        dtype=p_blocks.dtype,
    )
    p_ext = with_halo(canon)
    ext_r, ext_c = n_r + 2, n_c + 2

    near_y = a_cols // grid_cols
    near_x = a_cols % grid_cols
    near = jnp.clip(near_y - (y0 - 1), 0, ext_r - 1) * ext_c + jnp.clip(near_x - (x0 - 1), 0, ext_c - 1)
    near_agg_y = mirror((near_y - 1)[..., None] // 2 + two, coarse_rows)
    near_agg_x = mirror((near_x - 1)[..., None] // 2 + two, coarse_cols)
    slot_y = near_agg_y - (ys // 2 - 1)[:, None, None, None]
    slot_x = near_agg_x - (xs // 2 - 1)[None, :, None, None]
    slot = (slot_y[..., :, None] * 3 + slot_x[..., None, :]).reshape(n_r, n_c, terms, 4)
    slot = jnp.where((slot >= 0) & (slot < 9), slot, -1)

    ap = pl.pallas_call(
        ap_kernel,
        out_shape=jax.ShapeDtypeStruct((n_r * n_c, 9, bs, bs), jnp.bfloat16),
        in_specs=[
            pl.BlockSpec(memory_space=pltpu.SMEM),
            pl.BlockSpec(memory_space=pltpu.SMEM),
            pl.BlockSpec(memory_space=pltpu.VMEM),
            pl.BlockSpec(memory_space=pltpu.VMEM),
        ],
        out_specs=pl.BlockSpec(memory_space=pltpu.VMEM),
        scratch_shapes=[pltpu.VMEM((9, bs, bs), jnp.float32)],
    )(
        near.reshape(-1),
        slot.reshape(-1),
        a_blocks.reshape(n_r * n_c, terms, bs, bs),
        p_ext.reshape(ext_r * ext_c, 4, bs, bs),
    )
    ap = ap.reshape(n_r, n_c, 9, bs, bs)

    o_r, o_c = n_r // 2, n_c // 2
    ey = y0 - 1 + jnp.arange(ext_r, dtype=jnp.int32)
    ex = x0 - 1 + jnp.arange(ext_c, dtype=jnp.int32)
    e_agg_y = mirror((ey - 1)[:, None] // 2 + two, coarse_rows)
    e_agg_x = mirror((ex - 1)[:, None] // 2 + two, coarse_cols)
    own_y = e_agg_y - y0 // 2
    own_x = e_agg_x - x0 // 2
    off_y = (ey // 2 - 1)[:, None] - e_agg_y + 2
    off_x = (ex // 2 - 1)[:, None] - e_agg_x + 2
    ok_y = (ey >= 0)[:, None] & (ey < grid_rows)[:, None] & (own_y >= 0) & (own_y < o_r) & (off_y >= 0) & (off_y <= 2)
    ok_x = (ex >= 0)[:, None] & (ex < grid_cols)[:, None] & (own_x >= 0) & (own_x < o_c) & (off_x >= 0) & (off_x <= 2)
    target = (own_y[:, None, :, None] * o_c + own_x[None, :, None, :]) * 25 + (
        off_y[:, None, :, None] * 5 + off_x[None, :, None, :]
    )
    target = jnp.where(ok_y[:, None, :, None] & ok_x[None, :, None, :], target, -1).reshape(ext_r, ext_c, 4)
    place = jnp.arange(ext_r * ext_c, dtype=jnp.int32).reshape(ext_r, ext_c)

    cy = ys[0] // 2 + jnp.arange(o_r, dtype=jnp.int32)
    cx = xs[0] // 2 + jnp.arange(o_c, dtype=jnp.int32)
    pick = (c_cols // coarse_cols - cy[:, None, None] + 2) * 5 + (c_cols % coarse_cols - cx[None, :, None] + 2)
    pick = jnp.clip(pick, 0, 24).reshape(-1)

    p_t = jnp.swapaxes(p_ext, -1, -2).reshape(ext_r * ext_c * 4, bs, bs)
    stencil = c_cols.shape[-1]
    acc_shape = jax.ShapeDtypeStruct((o_r * o_c * 25, bs, bs), jnp.float32)
    dot_cost = 2 * bs * bs * bs * 9
    part = pl.pallas_call(
        own_kernel,
        out_shape=acc_shape,
        in_specs=[pl.BlockSpec(memory_space=pltpu.SMEM)] * 2 + [pl.BlockSpec(memory_space=pltpu.VMEM)] * 2,
        out_specs=pl.BlockSpec(memory_space=pltpu.VMEM),
        cost_estimate=pl.CostEstimate(
            flops=dot_cost * n_r * n_c * 4, bytes_accessed=4 * 1024 * 1024, transcendentals=0
        ),
    )(
        place[1:-1, 1:-1].reshape(-1),
        target[1:-1, 1:-1].reshape(-1),
        ap.reshape(n_r * n_c, 9, bs, bs),
        p_t,
    )
    ring_tiles = 2 * ext_c + 2 * n_r
    out = pl.pallas_call(
        ring_kernel,
        out_shape=jax.ShapeDtypeStruct((o_r * o_c, stencil, bs, bs), jnp.bfloat16),
        in_specs=[pl.BlockSpec(memory_space=pltpu.SMEM)] * 3 + [pl.BlockSpec(memory_space=pltpu.VMEM)] * 3,
        out_specs=pl.BlockSpec(memory_space=pltpu.VMEM),
        scratch_shapes=[pltpu.VMEM(acc_shape.shape, jnp.float32)],
        cost_estimate=pl.CostEstimate(
            flops=dot_cost * ring_tiles * 4, bytes_accessed=5 * 1024 * 1024, transcendentals=0
        ),
    )(
        ring_of(place),
        ring_of(target).reshape(-1),
        pick,
        halo_ring(ap),
        p_t,
        part,
    )
    return out.reshape(o_r, o_c, stencil, bs, bs)


def solution(mesh):
    return jax.shard_map(
        body,
        mesh=mesh,
        in_specs=(
            P("row", "col", None, None, None),
            P("row", "col", None),
            P("row", "col", None, None, None),
            P("row", "col", None),
            P("row", "col", None),
        ),
        out_specs=P("row", "col", None, None, None),
        check_vma=False,
    )
```

```python
import jax
import jax.numpy as jnp
from jax import lax
from jax.experimental import pallas as pl
from jax.experimental.pallas import tpu as pltpu
from jax.sharding import PartitionSpec as P


def mirror(values, limit):
    values = jnp.where(values < 0, -values, values)
    return jnp.where(values >= limit, 2 * (limit - 1) - values, values)


def shifted(piece, down, right):
    rows, cols = lax.axis_size("row"), lax.axis_size("col")
    if right == 0:
        pairs = [(s, s + down) for s in range(rows) if 0 <= s + down < rows]
        return lax.ppermute(piece, "row", pairs)
    if down == 0:
        pairs = [(s, s + right) for s in range(cols) if 0 <= s + right < cols]
        return lax.ppermute(piece, "col", pairs)
    pairs = []
    for sr in range(rows):
        for sc in range(cols):
            tr, tc = sr + down, sc + right
            if 0 <= tr < rows and 0 <= tc < cols:
                pairs.append((sr * cols + sc, tr * cols + tc))
    return lax.ppermute(piece, ("row", "col"), pairs)


def dense_shifted(piece, down, right):
    rows, cols = piece.shape[-2], piece.shape[-1]
    lanes = 128 if (rows * cols) % 128 == 0 and cols < 128 else cols
    packed = piece.reshape(piece.shape[:-2] + (rows * cols // lanes, lanes))
    return shifted(packed, down, right).reshape(piece.shape)


def halo_pieces(x):
    return {
        "left": dense_shifted(x[:, -1], 0, 1),
        "right": dense_shifted(x[:, 0], 0, -1),
        "top": dense_shifted(x[-1], 1, 0),
        "bottom": dense_shifted(x[0], -1, 0),
        "top_left": dense_shifted(x[-1, -1], 1, 1),
        "top_right": dense_shifted(x[-1, 0], 1, -1),
        "bottom_left": dense_shifted(x[0, -1], -1, 1),
        "bottom_right": dense_shifted(x[0, 0], -1, -1),
    }


def with_halo(x):
    h = halo_pieces(x)
    first = jnp.concatenate([h["top_left"][None], h["top"], h["top_right"][None]], axis=0)
    last = jnp.concatenate([h["bottom_left"][None], h["bottom"], h["bottom_right"][None]], axis=0)
    middle = jnp.concatenate([h["left"][:, None], x, h["right"][:, None]], axis=1)
    return jnp.concatenate([first[None], middle, last[None]], axis=0)


def halo_ring(x):
    h = halo_pieces(x)
    return jnp.concatenate(
        [
            h["top_left"][None],
            h["top"],
            h["top_right"][None],
            h["bottom_left"][None],
            h["bottom"],
            h["bottom_right"][None],
            h["left"],
            h["right"],
        ],
        axis=0,
    )


def ap_kernel(near_ref, slot_ref, a_ref, p_ref, out_ref, acc_ref):
    tiles, terms = a_ref.shape[0], a_ref.shape[1]

    def one_tile(t, carry):
        acc_ref[...] = jnp.zeros(acc_ref.shape, jnp.float32)
        for k in range(terms):
            j = near_ref[t * terms + k]
            a = a_ref[t, k]
            for q in range(4):
                e = slot_ref[(t * terms + k) * 4 + q]
                keep = jnp.where(e >= 0, 1.0, 0.0).astype(jnp.float32)
                prod = jnp.dot(a, p_ref[j, q], preferred_element_type=jnp.float32)
                acc_ref[jnp.clip(e, 0, 8)] += prod * keep

        out_ref[t] = acc_ref[...].astype(out_ref.dtype)
        return carry

    lax.fori_loop(0, tiles, one_tile, 0)


def add_terms(where_ref, target_ref, ap_ref, pt_ref, acc_ref):
    def one_tile(t, carry):
        w = where_ref[t]
        for q in range(4):
            g = target_ref[t * 4 + q]

            @pl.when(g >= 0)
            def _():
                pt = pt_ref[w * 4 + q]
                for e in range(9):
                    acc_ref[g + (e // 3) * 5 + e % 3] += jnp.dot(
                        pt, ap_ref[t, e], preferred_element_type=jnp.float32
                    )

        return carry

    lax.fori_loop(0, ap_ref.shape[0], one_tile, 0)


def coarse_kernel(
    own_where_ref, own_target_ref, ring_where_ref, ring_target_ref, pick_ref, own_ref, ring_ref, pt_ref, out_ref, acc_ref
):
    acc_ref[...] = jnp.zeros(acc_ref.shape, jnp.float32)
    add_terms(own_where_ref, own_target_ref, own_ref, pt_ref, acc_ref)
    add_terms(ring_where_ref, ring_target_ref, ring_ref, pt_ref, acc_ref)
    owned, stencil = out_ref.shape[0], out_ref.shape[1]

    def one_pick(i, carry):
        a = i // stencil
        out_ref[a, i % stencil] = acc_ref[a * stencil + pick_ref[i]].astype(out_ref.dtype)
        return carry

    lax.fori_loop(0, owned * stencil, one_pick, 0)


def ring_of(x):
    return jnp.concatenate([x[0], x[-1], x[1:-1, 0], x[1:-1, -1]], axis=0)


def body(a_blocks, a_cols, p_blocks, p_cols, c_cols):
    n_r, n_c = a_blocks.shape[0], a_blocks.shape[1]
    bs = a_blocks.shape[-1]
    terms = a_blocks.shape[2]
    grid_rows = n_r * lax.axis_size("row")
    grid_cols = n_c * lax.axis_size("col")
    coarse_rows, coarse_cols = grid_rows // 2, grid_cols // 2
    y0 = lax.axis_index("row") * n_r
    x0 = lax.axis_index("col") * n_c
    ys = y0 + jnp.arange(n_r, dtype=jnp.int32)
    xs = x0 + jnp.arange(n_c, dtype=jnp.int32)
    two = jnp.arange(2, dtype=jnp.int32)

    agg_y = mirror((ys - 1)[:, None] // 2 + two, coarse_rows)
    agg_x = mirror((xs - 1)[:, None] // 2 + two, coarse_cols)
    wanted = (agg_y[:, None, :, None] * coarse_cols + agg_x[None, :, None, :]).reshape(n_r, n_c, 4)
    match = p_cols[:, :, None, :] == wanted[:, :, :, None]
    canon = jnp.sum(
        jnp.where(match[..., None, None], p_blocks[:, :, None], jnp.zeros((), p_blocks.dtype)),
        axis=3,
        dtype=p_blocks.dtype,
    )
    p_ext = with_halo(canon)
    ext_r, ext_c = n_r + 2, n_c + 2

    near_y = a_cols // grid_cols
    near_x = a_cols % grid_cols
    near = jnp.clip(near_y - (y0 - 1), 0, ext_r - 1) * ext_c + jnp.clip(near_x - (x0 - 1), 0, ext_c - 1)
    near_agg_y = mirror((near_y - 1)[..., None] // 2 + two, coarse_rows)
    near_agg_x = mirror((near_x - 1)[..., None] // 2 + two, coarse_cols)
    slot_y = near_agg_y - (ys // 2 - 1)[:, None, None, None]
    slot_x = near_agg_x - (xs // 2 - 1)[None, :, None, None]
    slot = (slot_y[..., :, None] * 3 + slot_x[..., None, :]).reshape(n_r, n_c, terms, 4)
    slot = jnp.where((slot >= 0) & (slot < 9), slot, -1)

    ap = pl.pallas_call(
        ap_kernel,
        out_shape=jax.ShapeDtypeStruct((n_r * n_c, 9, bs, bs), jnp.bfloat16),
        in_specs=[
            pl.BlockSpec(memory_space=pltpu.SMEM),
            pl.BlockSpec(memory_space=pltpu.SMEM),
            pl.BlockSpec(memory_space=pltpu.VMEM),
            pl.BlockSpec(memory_space=pltpu.VMEM),
        ],
        out_specs=pl.BlockSpec(memory_space=pltpu.VMEM),
        scratch_shapes=[pltpu.VMEM((9, bs, bs), jnp.float32)],
    )(
        near.reshape(-1),
        slot.reshape(-1),
        a_blocks.reshape(n_r * n_c, terms, bs, bs),
        p_ext.reshape(ext_r * ext_c, 4, bs, bs),
    )
    ap = ap.reshape(n_r, n_c, 9, bs, bs)

    o_r, o_c = n_r // 2, n_c // 2
    ey = y0 - 1 + jnp.arange(ext_r, dtype=jnp.int32)
    ex = x0 - 1 + jnp.arange(ext_c, dtype=jnp.int32)
    e_agg_y = mirror((ey - 1)[:, None] // 2 + two, coarse_rows)
    e_agg_x = mirror((ex - 1)[:, None] // 2 + two, coarse_cols)
    own_y = e_agg_y - y0 // 2
    own_x = e_agg_x - x0 // 2
    off_y = (ey // 2 - 1)[:, None] - e_agg_y + 2
    off_x = (ex // 2 - 1)[:, None] - e_agg_x + 2
    ok_y = (ey >= 0)[:, None] & (ey < grid_rows)[:, None] & (own_y >= 0) & (own_y < o_r) & (off_y >= 0) & (off_y <= 2)
    ok_x = (ex >= 0)[:, None] & (ex < grid_cols)[:, None] & (own_x >= 0) & (own_x < o_c) & (off_x >= 0) & (off_x <= 2)
    target = (own_y[:, None, :, None] * o_c + own_x[None, :, None, :]) * 25 + (
        off_y[:, None, :, None] * 5 + off_x[None, :, None, :]
    )
    target = jnp.where(ok_y[:, None, :, None] & ok_x[None, :, None, :], target, -1).reshape(ext_r, ext_c, 4)
    place = jnp.arange(ext_r * ext_c, dtype=jnp.int32).reshape(ext_r, ext_c)

    cy = ys[0] // 2 + jnp.arange(o_r, dtype=jnp.int32)
    cx = xs[0] // 2 + jnp.arange(o_c, dtype=jnp.int32)
    pick = (c_cols // coarse_cols - cy[:, None, None] + 2) * 5 + (c_cols % coarse_cols - cx[None, :, None] + 2)
    pick = jnp.clip(pick, 0, 24).reshape(-1)

    p_t = jnp.swapaxes(p_ext, -1, -2).reshape(ext_r * ext_c * 4, bs, bs)
    stencil = c_cols.shape[-1]
    ring_tiles = 2 * ext_c + 2 * n_r
    out = pl.pallas_call(
        coarse_kernel,
        out_shape=jax.ShapeDtypeStruct((o_r * o_c, stencil, bs, bs), jnp.bfloat16),
        in_specs=[pl.BlockSpec(memory_space=pltpu.SMEM)] * 5 + [pl.BlockSpec(memory_space=pltpu.VMEM)] * 3,
        out_specs=pl.BlockSpec(memory_space=pltpu.VMEM),
        scratch_shapes=[pltpu.VMEM((o_r * o_c * 25, bs, bs), jnp.float32)],
    )(
        place[1:-1, 1:-1].reshape(-1),
        target[1:-1, 1:-1].reshape(-1),
        ring_of(place),
        ring_of(target).reshape(-1),
        pick,
        ap.reshape(n_r * n_c, 9, bs, bs),
        halo_ring(ap),
        p_t,
    )
    return out.reshape(o_r, o_c, stencil, bs, bs)


def solution(mesh):
    return jax.shard_map(
        body,
        mesh=mesh,
        in_specs=(
            P("row", "col", None, None, None),
            P("row", "col", None),
            P("row", "col", None, None, None),
            P("row", "col", None),
            P("row", "col", None),
        ),
        out_specs=P("row", "col", None, None, None),
        check_vma=False,
    )
```

```python
import jax
import jax.numpy as jnp
from jax import lax
from jax.experimental import pallas as pl
from jax.experimental.pallas import tpu as pltpu
from jax.sharding import PartitionSpec as P


def mirror(values, limit):
    values = jnp.where(values < 0, -values, values)
    return jnp.where(values >= limit, 2 * (limit - 1) - values, values)


def shifted(piece, down, right):
    rows, cols = lax.axis_size("row"), lax.axis_size("col")
    if right == 0:
        pairs = [(s, s + down) for s in range(rows) if 0 <= s + down < rows]
        return lax.ppermute(piece, "row", pairs)
    if down == 0:
        pairs = [(s, s + right) for s in range(cols) if 0 <= s + right < cols]
        return lax.ppermute(piece, "col", pairs)
    pairs = []
    for sr in range(rows):
        for sc in range(cols):
            tr, tc = sr + down, sc + right
            if 0 <= tr < rows and 0 <= tc < cols:
                pairs.append((sr * cols + sc, tr * cols + tc))
    return lax.ppermute(piece, ("row", "col"), pairs)


def dense_shifted(piece, down, right):
    rows, cols = piece.shape[-2], piece.shape[-1]
    lanes = 128 if (rows * cols) % 128 == 0 and cols < 128 else cols
    packed = piece.reshape(piece.shape[:-2] + (rows * cols // lanes, lanes))
    return shifted(packed, down, right).reshape(piece.shape)


def halo_pieces(x):
    return {
        "left": dense_shifted(x[:, -1], 0, 1),
        "right": dense_shifted(x[:, 0], 0, -1),
        "top": dense_shifted(x[-1], 1, 0),
        "bottom": dense_shifted(x[0], -1, 0),
        "top_left": dense_shifted(x[-1, -1], 1, 1),
        "top_right": dense_shifted(x[-1, 0], 1, -1),
        "bottom_left": dense_shifted(x[0, -1], -1, 1),
        "bottom_right": dense_shifted(x[0, 0], -1, -1),
    }


def with_halo(x):
    h = halo_pieces(x)
    first = jnp.concatenate([h["top_left"][None], h["top"], h["top_right"][None]], axis=0)
    last = jnp.concatenate([h["bottom_left"][None], h["bottom"], h["bottom_right"][None]], axis=0)
    middle = jnp.concatenate([h["left"][:, None], x, h["right"][:, None]], axis=1)
    return jnp.concatenate([first[None], middle, last[None]], axis=0)


def halo_ring(x):
    h = halo_pieces(x)
    return jnp.concatenate(
        [
            h["top_left"][None],
            h["top"],
            h["top_right"][None],
            h["bottom_left"][None],
            h["bottom"],
            h["bottom_right"][None],
            h["left"],
            h["right"],
        ],
        axis=0,
    )


def ap_kernel(near_ref, slot_ref, a_ref, p_ref, out_ref, dense_ref, acc_ref):
    tiles, terms = a_ref.shape[0], a_ref.shape[1]

    def one_tile(t, carry):
        acc_ref[...] = jnp.zeros(acc_ref.shape, jnp.float32)
        for k in range(terms):
            j = near_ref[t * terms + k]
            a = a_ref[t, k]
            for q in range(4):
                e = slot_ref[(t * terms + k) * 4 + q]
                keep = jnp.where(e >= 0, 1.0, 0.0).astype(jnp.float32)
                prod = jnp.dot(a, p_ref[j, q], preferred_element_type=jnp.float32)
                acc_ref[jnp.clip(e, 0, 8)] += prod * keep

        ap = acc_ref[...].astype(out_ref.dtype)
        out_ref[t] = ap
        dense_ref[t] = ap.reshape(dense_ref.shape[1:])
        return carry

    lax.fori_loop(0, tiles, one_tile, 0)


def add_terms(where_ref, target_ref, ap_ref, pt_ref, acc_ref):
    def one_tile(t, carry):
        w = where_ref[t]
        for q in range(4):
            g = target_ref[t * 4 + q]

            @pl.when(g >= 0)
            def _():
                pt = pt_ref[w * 4 + q]
                for e in range(9):
                    block = ap_ref[t, e].reshape(pt.shape)
                    acc_ref[g + (e // 3) * 5 + e % 3] += jnp.dot(pt, block, preferred_element_type=jnp.float32)

        return carry

    lax.fori_loop(0, ap_ref.shape[0], one_tile, 0)


def coarse_kernel(
    own_where_ref, own_target_ref, ring_where_ref, ring_target_ref, pick_ref, own_ref, ring_ref, pt_ref, out_ref, acc_ref
):
    acc_ref[...] = jnp.zeros(acc_ref.shape, jnp.float32)
    add_terms(own_where_ref, own_target_ref, own_ref, pt_ref, acc_ref)
    add_terms(ring_where_ref, ring_target_ref, ring_ref, pt_ref, acc_ref)
    owned, stencil = out_ref.shape[0], out_ref.shape[1]

    def one_pick(i, carry):
        a = i // stencil
        out_ref[a, i % stencil] = acc_ref[a * stencil + pick_ref[i]].astype(out_ref.dtype)
        return carry

    lax.fori_loop(0, owned * stencil, one_pick, 0)


def ring_of(x):
    return jnp.concatenate([x[0], x[-1], x[1:-1, 0], x[1:-1, -1]], axis=0)


def body(a_blocks, a_cols, p_blocks, p_cols, c_cols):
    n_r, n_c = a_blocks.shape[0], a_blocks.shape[1]
    bs = a_blocks.shape[-1]
    terms = a_blocks.shape[2]
    grid_rows = n_r * lax.axis_size("row")
    grid_cols = n_c * lax.axis_size("col")
    coarse_rows, coarse_cols = grid_rows // 2, grid_cols // 2
    y0 = lax.axis_index("row") * n_r
    x0 = lax.axis_index("col") * n_c
    ys = y0 + jnp.arange(n_r, dtype=jnp.int32)
    xs = x0 + jnp.arange(n_c, dtype=jnp.int32)
    two = jnp.arange(2, dtype=jnp.int32)

    agg_y = mirror((ys - 1)[:, None] // 2 + two, coarse_rows)
    agg_x = mirror((xs - 1)[:, None] // 2 + two, coarse_cols)
    wanted = (agg_y[:, None, :, None] * coarse_cols + agg_x[None, :, None, :]).reshape(n_r, n_c, 4)
    match = p_cols[:, :, None, :] == wanted[:, :, :, None]
    canon = jnp.sum(
        jnp.where(match[..., None, None], p_blocks[:, :, None], jnp.zeros((), p_blocks.dtype)),
        axis=3,
        dtype=p_blocks.dtype,
    )
    p_ext = with_halo(canon)
    ext_r, ext_c = n_r + 2, n_c + 2

    near_y = a_cols // grid_cols
    near_x = a_cols % grid_cols
    near = jnp.clip(near_y - (y0 - 1), 0, ext_r - 1) * ext_c + jnp.clip(near_x - (x0 - 1), 0, ext_c - 1)
    near_agg_y = mirror((near_y - 1)[..., None] // 2 + two, coarse_rows)
    near_agg_x = mirror((near_x - 1)[..., None] // 2 + two, coarse_cols)
    slot_y = near_agg_y - (ys // 2 - 1)[:, None, None, None]
    slot_x = near_agg_x - (xs // 2 - 1)[None, :, None, None]
    slot = (slot_y[..., :, None] * 3 + slot_x[..., None, :]).reshape(n_r, n_c, terms, 4)
    slot = jnp.where((slot >= 0) & (slot < 9), slot, -1)

    ap, ap_dense = pl.pallas_call(
        ap_kernel,
        out_shape=(
            jax.ShapeDtypeStruct((n_r * n_c, 9, bs, bs), jnp.bfloat16),
            jax.ShapeDtypeStruct((n_r * n_c, 9, bs * bs // 128, 128), jnp.bfloat16),
        ),
        in_specs=[
            pl.BlockSpec(memory_space=pltpu.SMEM),
            pl.BlockSpec(memory_space=pltpu.SMEM),
            pl.BlockSpec(memory_space=pltpu.VMEM),
            pl.BlockSpec(memory_space=pltpu.VMEM),
        ],
        out_specs=(pl.BlockSpec(memory_space=pltpu.VMEM), pl.BlockSpec(memory_space=pltpu.VMEM)),
        scratch_shapes=[pltpu.VMEM((9, bs, bs), jnp.float32)],
    )(
        near.reshape(-1),
        slot.reshape(-1),
        a_blocks.reshape(n_r * n_c, terms, bs, bs),
        p_ext.reshape(ext_r * ext_c, 4, bs, bs),
    )
    ap = ap.reshape(n_r, n_c, 9, bs, bs)
    ap_dense = ap_dense.reshape((n_r, n_c) + ap_dense.shape[1:])

    o_r, o_c = n_r // 2, n_c // 2
    ey = y0 - 1 + jnp.arange(ext_r, dtype=jnp.int32)
    ex = x0 - 1 + jnp.arange(ext_c, dtype=jnp.int32)
    e_agg_y = mirror((ey - 1)[:, None] // 2 + two, coarse_rows)
    e_agg_x = mirror((ex - 1)[:, None] // 2 + two, coarse_cols)
    own_y = e_agg_y - y0 // 2
    own_x = e_agg_x - x0 // 2
    off_y = (ey // 2 - 1)[:, None] - e_agg_y + 2
    off_x = (ex // 2 - 1)[:, None] - e_agg_x + 2
    ok_y = (ey >= 0)[:, None] & (ey < grid_rows)[:, None] & (own_y >= 0) & (own_y < o_r) & (off_y >= 0) & (off_y <= 2)
    ok_x = (ex >= 0)[:, None] & (ex < grid_cols)[:, None] & (own_x >= 0) & (own_x < o_c) & (off_x >= 0) & (off_x <= 2)
    target = (own_y[:, None, :, None] * o_c + own_x[None, :, None, :]) * 25 + (
        off_y[:, None, :, None] * 5 + off_x[None, :, None, :]
    )
    target = jnp.where(ok_y[:, None, :, None] & ok_x[None, :, None, :], target, -1).reshape(ext_r, ext_c, 4)
    place = jnp.arange(ext_r * ext_c, dtype=jnp.int32).reshape(ext_r, ext_c)

    cy = ys[0] // 2 + jnp.arange(o_r, dtype=jnp.int32)
    cx = xs[0] // 2 + jnp.arange(o_c, dtype=jnp.int32)
    pick = (c_cols // coarse_cols - cy[:, None, None] + 2) * 5 + (c_cols % coarse_cols - cx[None, :, None] + 2)
    pick = jnp.clip(pick, 0, 24).reshape(-1)

    p_t = jnp.swapaxes(p_ext, -1, -2).reshape(ext_r * ext_c * 4, bs, bs)
    stencil = c_cols.shape[-1]
    ring_tiles = 2 * ext_c + 2 * n_r
    out = pl.pallas_call(
        coarse_kernel,
        out_shape=jax.ShapeDtypeStruct((o_r * o_c, stencil, bs, bs), jnp.bfloat16),
        in_specs=[pl.BlockSpec(memory_space=pltpu.SMEM)] * 5 + [pl.BlockSpec(memory_space=pltpu.VMEM)] * 3,
        out_specs=pl.BlockSpec(memory_space=pltpu.VMEM),
        scratch_shapes=[pltpu.VMEM((o_r * o_c * 25, bs, bs), jnp.float32)],
    )(
        place[1:-1, 1:-1].reshape(-1),
        target[1:-1, 1:-1].reshape(-1),
        ring_of(place),
        ring_of(target).reshape(-1),
        pick,
        ap.reshape(n_r * n_c, 9, bs, bs),
        halo_ring(ap_dense),
        p_t,
    )
    return out.reshape(o_r, o_c, stencil, bs, bs)


def solution(mesh):
    return jax.shard_map(
        body,
        mesh=mesh,
        in_specs=(
            P("row", "col", None, None, None),
            P("row", "col", None),
            P("row", "col", None, None, None),
            P("row", "col", None),
            P("row", "col", None),
        ),
        out_specs=P("row", "col", None, None, None),
        check_vma=False,
    )
```

```python
import jax
import jax.numpy as jnp
from jax import lax
from jax.experimental import pallas as pl
from jax.experimental.pallas import tpu as pltpu
from jax.sharding import PartitionSpec as P


def mirror(values, limit):
    values = jnp.where(values < 0, -values, values)
    return jnp.where(values >= limit, 2 * (limit - 1) - values, values)


def shifted(piece, down, right):
    rows, cols = lax.axis_size("row"), lax.axis_size("col")
    if right == 0:
        pairs = [(s, s + down) for s in range(rows) if 0 <= s + down < rows]
        return lax.ppermute(piece, "row", pairs)
    if down == 0:
        pairs = [(s, s + right) for s in range(cols) if 0 <= s + right < cols]
        return lax.ppermute(piece, "col", pairs)
    pairs = []
    for sr in range(rows):
        for sc in range(cols):
            tr, tc = sr + down, sc + right
            if 0 <= tr < rows and 0 <= tc < cols:
                pairs.append((sr * cols + sc, tr * cols + tc))
    return lax.ppermute(piece, ("row", "col"), pairs)


def dense_shifted(piece, down, right):
    rows, cols = piece.shape[-2], piece.shape[-1]
    lanes = 128 if (rows * cols) % 128 == 0 and cols < 128 else cols
    packed = piece.reshape(piece.shape[:-2] + (rows * cols // lanes, lanes))
    return shifted(packed, down, right).reshape(piece.shape)


def halo_pieces(x):
    return {
        "left": dense_shifted(x[:, -1], 0, 1),
        "right": dense_shifted(x[:, 0], 0, -1),
        "top": dense_shifted(x[-1], 1, 0),
        "bottom": dense_shifted(x[0], -1, 0),
        "top_left": dense_shifted(x[-1, -1], 1, 1),
        "top_right": dense_shifted(x[-1, 0], 1, -1),
        "bottom_left": dense_shifted(x[0, -1], -1, 1),
        "bottom_right": dense_shifted(x[0, 0], -1, -1),
    }


def with_halo(x):
    h = halo_pieces(x)
    first = jnp.concatenate([h["top_left"][None], h["top"], h["top_right"][None]], axis=0)
    last = jnp.concatenate([h["bottom_left"][None], h["bottom"], h["bottom_right"][None]], axis=0)
    middle = jnp.concatenate([h["left"][:, None], x, h["right"][:, None]], axis=1)
    return jnp.concatenate([first[None], middle, last[None]], axis=0)


def halo_ring(x):
    h = halo_pieces(x)
    return jnp.concatenate(
        [
            h["top_left"][None],
            h["top"],
            h["top_right"][None],
            h["bottom_left"][None],
            h["bottom"],
            h["bottom_right"][None],
            h["left"],
            h["right"],
        ],
        axis=0,
    )


def ap_kernel(near_ref, slot_ref, a_ref, p_ref, out_ref, dense_ref, acc_ref):
    tiles, terms = a_ref.shape[0], a_ref.shape[1]

    def one_tile(t, carry):
        acc_ref[...] = jnp.zeros(acc_ref.shape, jnp.float32)
        for k in range(terms):
            j = near_ref[t * terms + k]
            a = a_ref[t, k]
            for q in range(4):
                e = slot_ref[(t * terms + k) * 4 + q]
                keep = jnp.where(e >= 0, 1.0, 0.0).astype(jnp.float32)
                prod = jnp.dot(a, p_ref[j, q], preferred_element_type=jnp.float32)
                acc_ref[jnp.clip(e, 0, 8)] += prod * keep

        ap = acc_ref[...].astype(out_ref.dtype)
        out_ref[t] = ap
        dense_ref[t] = ap.reshape(dense_ref.shape[1:])
        return carry

    lax.fori_loop(0, tiles, one_tile, 0)


def add_terms(where_ref, target_ref, ap_ref, pt_ref, acc_ref):
    def one_tile(t, carry):
        w = where_ref[t]
        blocks = [ap_ref[t, e].reshape(pt_ref.shape[1:]) for e in range(9)]
        for q in range(4):
            g = target_ref[t * 4 + q]

            @pl.when(g >= 0)
            def _():
                pt = pt_ref[w * 4 + q]
                for e in range(9):
                    acc_ref[g + (e // 3) * 5 + e % 3] += jnp.dot(pt, blocks[e], preferred_element_type=jnp.float32)

        return carry

    lax.fori_loop(0, ap_ref.shape[0], one_tile, 0)


def coarse_kernel(
    own_where_ref, own_target_ref, ring_where_ref, ring_target_ref, pick_ref, own_ref, ring_ref, pt_ref, out_ref, acc_ref
):
    acc_ref[...] = jnp.zeros(acc_ref.shape, jnp.float32)
    add_terms(own_where_ref, own_target_ref, own_ref, pt_ref, acc_ref)
    add_terms(ring_where_ref, ring_target_ref, ring_ref, pt_ref, acc_ref)
    owned, stencil = out_ref.shape[0], out_ref.shape[1]

    def one_pick(i, carry):
        a = i // stencil
        out_ref[a, i % stencil] = acc_ref[a * stencil + pick_ref[i]].astype(out_ref.dtype)
        return carry

    lax.fori_loop(0, owned * stencil, one_pick, 0)


def ring_of(x):
    return jnp.concatenate([x[0], x[-1], x[1:-1, 0], x[1:-1, -1]], axis=0)


def body(a_blocks, a_cols, p_blocks, p_cols, c_cols):
    n_r, n_c = a_blocks.shape[0], a_blocks.shape[1]
    bs = a_blocks.shape[-1]
    terms = a_blocks.shape[2]
    grid_rows = n_r * lax.axis_size("row")
    grid_cols = n_c * lax.axis_size("col")
    coarse_rows, coarse_cols = grid_rows // 2, grid_cols // 2
    y0 = lax.axis_index("row") * n_r
    x0 = lax.axis_index("col") * n_c
    ys = y0 + jnp.arange(n_r, dtype=jnp.int32)
    xs = x0 + jnp.arange(n_c, dtype=jnp.int32)
    two = jnp.arange(2, dtype=jnp.int32)

    agg_y = mirror((ys - 1)[:, None] // 2 + two, coarse_rows)
    agg_x = mirror((xs - 1)[:, None] // 2 + two, coarse_cols)
    wanted = (agg_y[:, None, :, None] * coarse_cols + agg_x[None, :, None, :]).reshape(n_r, n_c, 4)
    match = p_cols[:, :, None, :] == wanted[:, :, :, None]
    canon = jnp.sum(
        jnp.where(match[..., None, None], p_blocks[:, :, None], jnp.zeros((), p_blocks.dtype)),
        axis=3,
        dtype=p_blocks.dtype,
    )
    p_ext = with_halo(canon)
    ext_r, ext_c = n_r + 2, n_c + 2

    near_y = a_cols // grid_cols
    near_x = a_cols % grid_cols
    near = jnp.clip(near_y - (y0 - 1), 0, ext_r - 1) * ext_c + jnp.clip(near_x - (x0 - 1), 0, ext_c - 1)
    near_agg_y = mirror((near_y - 1)[..., None] // 2 + two, coarse_rows)
    near_agg_x = mirror((near_x - 1)[..., None] // 2 + two, coarse_cols)
    slot_y = near_agg_y - (ys // 2 - 1)[:, None, None, None]
    slot_x = near_agg_x - (xs // 2 - 1)[None, :, None, None]
    slot = (slot_y[..., :, None] * 3 + slot_x[..., None, :]).reshape(n_r, n_c, terms, 4)
    slot = jnp.where((slot >= 0) & (slot < 9), slot, -1)

    ap, ap_dense = pl.pallas_call(
        ap_kernel,
        out_shape=(
            jax.ShapeDtypeStruct((n_r * n_c, 9, bs, bs), jnp.bfloat16),
            jax.ShapeDtypeStruct((n_r * n_c, 9, bs * bs // 128, 128), jnp.bfloat16),
        ),
        in_specs=[
            pl.BlockSpec(memory_space=pltpu.SMEM),
            pl.BlockSpec(memory_space=pltpu.SMEM),
            pl.BlockSpec(memory_space=pltpu.VMEM),
            pl.BlockSpec(memory_space=pltpu.VMEM),
        ],
        out_specs=(pl.BlockSpec(memory_space=pltpu.VMEM), pl.BlockSpec(memory_space=pltpu.VMEM)),
        scratch_shapes=[pltpu.VMEM((9, bs, bs), jnp.float32)],
    )(
        near.reshape(-1),
        slot.reshape(-1),
        a_blocks.reshape(n_r * n_c, terms, bs, bs),
        p_ext.reshape(ext_r * ext_c, 4, bs, bs),
    )
    ap = ap.reshape(n_r, n_c, 9, bs, bs)
    ap_dense = ap_dense.reshape((n_r, n_c) + ap_dense.shape[1:])

    o_r, o_c = n_r // 2, n_c // 2
    ey = y0 - 1 + jnp.arange(ext_r, dtype=jnp.int32)
    ex = x0 - 1 + jnp.arange(ext_c, dtype=jnp.int32)
    e_agg_y = mirror((ey - 1)[:, None] // 2 + two, coarse_rows)
    e_agg_x = mirror((ex - 1)[:, None] // 2 + two, coarse_cols)
    own_y = e_agg_y - y0 // 2
    own_x = e_agg_x - x0 // 2
    off_y = (ey // 2 - 1)[:, None] - e_agg_y + 2
    off_x = (ex // 2 - 1)[:, None] - e_agg_x + 2
    ok_y = (ey >= 0)[:, None] & (ey < grid_rows)[:, None] & (own_y >= 0) & (own_y < o_r) & (off_y >= 0) & (off_y <= 2)
    ok_x = (ex >= 0)[:, None] & (ex < grid_cols)[:, None] & (own_x >= 0) & (own_x < o_c) & (off_x >= 0) & (off_x <= 2)
    target = (own_y[:, None, :, None] * o_c + own_x[None, :, None, :]) * 25 + (
        off_y[:, None, :, None] * 5 + off_x[None, :, None, :]
    )
    target = jnp.where(ok_y[:, None, :, None] & ok_x[None, :, None, :], target, -1).reshape(ext_r, ext_c, 4)
    place = jnp.arange(ext_r * ext_c, dtype=jnp.int32).reshape(ext_r, ext_c)

    cy = ys[0] // 2 + jnp.arange(o_r, dtype=jnp.int32)
    cx = xs[0] // 2 + jnp.arange(o_c, dtype=jnp.int32)
    pick = (c_cols // coarse_cols - cy[:, None, None] + 2) * 5 + (c_cols % coarse_cols - cx[None, :, None] + 2)
    pick = jnp.clip(pick, 0, 24).reshape(-1)

    p_t = jnp.swapaxes(p_ext, -1, -2).reshape(ext_r * ext_c * 4, bs, bs)
    stencil = c_cols.shape[-1]
    ring_tiles = 2 * ext_c + 2 * n_r
    out = pl.pallas_call(
        coarse_kernel,
        out_shape=jax.ShapeDtypeStruct((o_r * o_c, stencil, bs, bs), jnp.bfloat16),
        in_specs=[pl.BlockSpec(memory_space=pltpu.SMEM)] * 5 + [pl.BlockSpec(memory_space=pltpu.VMEM)] * 3,
        out_specs=pl.BlockSpec(memory_space=pltpu.VMEM),
        scratch_shapes=[pltpu.VMEM((o_r * o_c * 25, bs, bs), jnp.float32)],
    )(
        place[1:-1, 1:-1].reshape(-1),
        target[1:-1, 1:-1].reshape(-1),
        ring_of(place),
        ring_of(target).reshape(-1),
        pick,
        ap.reshape(n_r * n_c, 9, bs, bs),
        halo_ring(ap_dense),
        p_t,
    )
    return out.reshape(o_r, o_c, stencil, bs, bs)


def solution(mesh):
    return jax.shard_map(
        body,
        mesh=mesh,
        in_specs=(
            P("row", "col", None, None, None),
            P("row", "col", None),
            P("row", "col", None, None, None),
            P("row", "col", None),
            P("row", "col", None),
        ),
        out_specs=P("row", "col", None, None, None),
        check_vma=False,
    )
```

```python
import jax
import jax.numpy as jnp
from jax import lax
from jax.experimental import pallas as pl
from jax.experimental.pallas import tpu as pltpu
from jax.sharding import PartitionSpec as P


def mirror(values, limit):
    values = jnp.where(values < 0, -values, values)
    return jnp.where(values >= limit, 2 * (limit - 1) - values, values)


def shifted(piece, down, right):
    rows, cols = lax.axis_size("row"), lax.axis_size("col")
    if right == 0:
        pairs = [(s, s + down) for s in range(rows) if 0 <= s + down < rows]
        return lax.ppermute(piece, "row", pairs)
    if down == 0:
        pairs = [(s, s + right) for s in range(cols) if 0 <= s + right < cols]
        return lax.ppermute(piece, "col", pairs)
    pairs = []
    for sr in range(rows):
        for sc in range(cols):
            tr, tc = sr + down, sc + right
            if 0 <= tr < rows and 0 <= tc < cols:
                pairs.append((sr * cols + sc, tr * cols + tc))
    return lax.ppermute(piece, ("row", "col"), pairs)


def dense_shifted(piece, down, right):
    rows, cols = piece.shape[-2], piece.shape[-1]
    lanes = 128 if (rows * cols) % 128 == 0 and cols < 128 else cols
    packed = piece.reshape(piece.shape[:-2] + (rows * cols // lanes, lanes))
    return shifted(packed, down, right).reshape(piece.shape)


def halo_pieces(x):
    return {
        "left": dense_shifted(x[:, -1], 0, 1),
        "right": dense_shifted(x[:, 0], 0, -1),
        "top": dense_shifted(x[-1], 1, 0),
        "bottom": dense_shifted(x[0], -1, 0),
        "top_left": dense_shifted(x[-1, -1], 1, 1),
        "top_right": dense_shifted(x[-1, 0], 1, -1),
        "bottom_left": dense_shifted(x[0, -1], -1, 1),
        "bottom_right": dense_shifted(x[0, 0], -1, -1),
    }


def with_halo(x):
    h = halo_pieces(x)
    first = jnp.concatenate([h["top_left"][None], h["top"], h["top_right"][None]], axis=0)
    last = jnp.concatenate([h["bottom_left"][None], h["bottom"], h["bottom_right"][None]], axis=0)
    middle = jnp.concatenate([h["left"][:, None], x, h["right"][:, None]], axis=1)
    return jnp.concatenate([first[None], middle, last[None]], axis=0)


def halo_ring(top, bottom, left, right):
    return jnp.concatenate(
        [
            dense_shifted(bottom[-1], 1, 1)[None],
            dense_shifted(bottom, 1, 0),
            dense_shifted(bottom[0], 1, -1)[None],
            dense_shifted(top[-1], -1, 1)[None],
            dense_shifted(top, -1, 0),
            dense_shifted(top[0], -1, -1)[None],
            dense_shifted(right, 0, 1),
            dense_shifted(left, 0, -1),
        ],
        axis=0,
    )


def ap_kernel(near_ref, slot_ref, a_ref, p_ref, out_ref, top_ref, bottom_ref, left_ref, right_ref, acc_ref):
    tiles, terms = a_ref.shape[0], a_ref.shape[1]
    n_c = top_ref.shape[0]
    n_r = left_ref.shape[0]
    dense = top_ref.shape[1:]

    def one_tile(t, carry):
        acc_ref[...] = jnp.zeros(acc_ref.shape, jnp.float32)
        for k in range(terms):
            j = near_ref[t * terms + k]
            a = a_ref[t, k]
            for q in range(4):
                e = slot_ref[(t * terms + k) * 4 + q]
                keep = jnp.where(e >= 0, 1.0, 0.0).astype(jnp.float32)
                prod = jnp.dot(a, p_ref[j, q], preferred_element_type=jnp.float32)
                acc_ref[jnp.clip(e, 0, 8)] += prod * keep

        out_ref[t] = acc_ref[...].astype(out_ref.dtype)
        row, col = t // n_c, t % n_c
        for ref, at, index in (
            (top_ref, row == 0, col),
            (bottom_ref, row == n_r - 1, col),
            (left_ref, col == 0, row),
            (right_ref, col == n_c - 1, row),
        ):

            @pl.when(at)
            def _():
                ref[index] = out_ref[t].reshape(dense)

        return carry

    lax.fori_loop(0, tiles, one_tile, 0)


def add_terms(where_ref, target_ref, ap_ref, pt_ref, acc_ref):
    def one_tile(t, carry):
        w = where_ref[t]
        blocks = [ap_ref[t, e].reshape(pt_ref.shape[1:]) for e in range(9)]
        for q in range(4):
            g = target_ref[t * 4 + q]

            @pl.when(g >= 0)
            def _():
                pt = pt_ref[w * 4 + q]
                for e in range(9):
                    acc_ref[g + (e // 3) * 5 + e % 3] += jnp.dot(pt, blocks[e], preferred_element_type=jnp.float32)

        return carry

    lax.fori_loop(0, ap_ref.shape[0], one_tile, 0)


def coarse_kernel(
    own_where_ref, own_target_ref, ring_where_ref, ring_target_ref, pick_ref, own_ref, ring_ref, pt_ref, out_ref, acc_ref
):
    acc_ref[...] = jnp.zeros(acc_ref.shape, jnp.float32)
    add_terms(own_where_ref, own_target_ref, own_ref, pt_ref, acc_ref)
    add_terms(ring_where_ref, ring_target_ref, ring_ref, pt_ref, acc_ref)
    owned, stencil = out_ref.shape[0], out_ref.shape[1]

    def one_pick(i, carry):
        a = i // stencil
        out_ref[a, i % stencil] = acc_ref[a * stencil + pick_ref[i]].astype(out_ref.dtype)
        return carry

    lax.fori_loop(0, owned * stencil, one_pick, 0)


def ring_of(x):
    return jnp.concatenate([x[0], x[-1], x[1:-1, 0], x[1:-1, -1]], axis=0)


def body(a_blocks, a_cols, p_blocks, p_cols, c_cols):
    n_r, n_c = a_blocks.shape[0], a_blocks.shape[1]
    bs = a_blocks.shape[-1]
    terms = a_blocks.shape[2]
    grid_rows = n_r * lax.axis_size("row")
    grid_cols = n_c * lax.axis_size("col")
    coarse_rows, coarse_cols = grid_rows // 2, grid_cols // 2
    y0 = lax.axis_index("row") * n_r
    x0 = lax.axis_index("col") * n_c
    ys = y0 + jnp.arange(n_r, dtype=jnp.int32)
    xs = x0 + jnp.arange(n_c, dtype=jnp.int32)
    two = jnp.arange(2, dtype=jnp.int32)

    agg_y = mirror((ys - 1)[:, None] // 2 + two, coarse_rows)
    agg_x = mirror((xs - 1)[:, None] // 2 + two, coarse_cols)
    wanted = (agg_y[:, None, :, None] * coarse_cols + agg_x[None, :, None, :]).reshape(n_r, n_c, 4)
    match = p_cols[:, :, None, :] == wanted[:, :, :, None]
    canon = jnp.sum(
        jnp.where(match[..., None, None], p_blocks[:, :, None], jnp.zeros((), p_blocks.dtype)),
        axis=3,
        dtype=p_blocks.dtype,
    )
    p_ext = with_halo(canon)
    ext_r, ext_c = n_r + 2, n_c + 2

    near_y = a_cols // grid_cols
    near_x = a_cols % grid_cols
    near = jnp.clip(near_y - (y0 - 1), 0, ext_r - 1) * ext_c + jnp.clip(near_x - (x0 - 1), 0, ext_c - 1)
    near_agg_y = mirror((near_y - 1)[..., None] // 2 + two, coarse_rows)
    near_agg_x = mirror((near_x - 1)[..., None] // 2 + two, coarse_cols)
    slot_y = near_agg_y - (ys // 2 - 1)[:, None, None, None]
    slot_x = near_agg_x - (xs // 2 - 1)[None, :, None, None]
    slot = (slot_y[..., :, None] * 3 + slot_x[..., None, :]).reshape(n_r, n_c, terms, 4)
    slot = jnp.where((slot >= 0) & (slot < 9), slot, -1)

    dense = (9, bs * bs // 128, 128)
    ap, top, bottom, left, right = pl.pallas_call(
        ap_kernel,
        out_shape=(
            jax.ShapeDtypeStruct((n_r * n_c, 9, bs, bs), jnp.bfloat16),
            jax.ShapeDtypeStruct((n_c,) + dense, jnp.bfloat16),
            jax.ShapeDtypeStruct((n_c,) + dense, jnp.bfloat16),
            jax.ShapeDtypeStruct((n_r,) + dense, jnp.bfloat16),
            jax.ShapeDtypeStruct((n_r,) + dense, jnp.bfloat16),
        ),
        in_specs=[
            pl.BlockSpec(memory_space=pltpu.SMEM),
            pl.BlockSpec(memory_space=pltpu.SMEM),
            pl.BlockSpec(memory_space=pltpu.VMEM),
            pl.BlockSpec(memory_space=pltpu.VMEM),
        ],
        out_specs=tuple(pl.BlockSpec(memory_space=pltpu.VMEM) for _ in range(5)),
        scratch_shapes=[pltpu.VMEM((9, bs, bs), jnp.float32)],
    )(
        near.reshape(-1),
        slot.reshape(-1),
        a_blocks.reshape(n_r * n_c, terms, bs, bs),
        p_ext.reshape(ext_r * ext_c, 4, bs, bs),
    )
    ap = ap.reshape(n_r, n_c, 9, bs, bs)

    o_r, o_c = n_r // 2, n_c // 2
    ey = y0 - 1 + jnp.arange(ext_r, dtype=jnp.int32)
    ex = x0 - 1 + jnp.arange(ext_c, dtype=jnp.int32)
    e_agg_y = mirror((ey - 1)[:, None] // 2 + two, coarse_rows)
    e_agg_x = mirror((ex - 1)[:, None] // 2 + two, coarse_cols)
    own_y = e_agg_y - y0 // 2
    own_x = e_agg_x - x0 // 2
    off_y = (ey // 2 - 1)[:, None] - e_agg_y + 2
    off_x = (ex // 2 - 1)[:, None] - e_agg_x + 2
    ok_y = (ey >= 0)[:, None] & (ey < grid_rows)[:, None] & (own_y >= 0) & (own_y < o_r) & (off_y >= 0) & (off_y <= 2)
    ok_x = (ex >= 0)[:, None] & (ex < grid_cols)[:, None] & (own_x >= 0) & (own_x < o_c) & (off_x >= 0) & (off_x <= 2)
    target = (own_y[:, None, :, None] * o_c + own_x[None, :, None, :]) * 25 + (
        off_y[:, None, :, None] * 5 + off_x[None, :, None, :]
    )
    target = jnp.where(ok_y[:, None, :, None] & ok_x[None, :, None, :], target, -1).reshape(ext_r, ext_c, 4)
    place = jnp.arange(ext_r * ext_c, dtype=jnp.int32).reshape(ext_r, ext_c)

    cy = ys[0] // 2 + jnp.arange(o_r, dtype=jnp.int32)
    cx = xs[0] // 2 + jnp.arange(o_c, dtype=jnp.int32)
    pick = (c_cols // coarse_cols - cy[:, None, None] + 2) * 5 + (c_cols % coarse_cols - cx[None, :, None] + 2)
    pick = jnp.clip(pick, 0, 24).reshape(-1)

    p_t = jnp.swapaxes(p_ext, -1, -2).reshape(ext_r * ext_c * 4, bs, bs)
    stencil = c_cols.shape[-1]
    ring_tiles = 2 * ext_c + 2 * n_r
    out = pl.pallas_call(
        coarse_kernel,
        out_shape=jax.ShapeDtypeStruct((o_r * o_c, stencil, bs, bs), jnp.bfloat16),
        in_specs=[pl.BlockSpec(memory_space=pltpu.SMEM)] * 5 + [pl.BlockSpec(memory_space=pltpu.VMEM)] * 3,
        out_specs=pl.BlockSpec(memory_space=pltpu.VMEM),
        scratch_shapes=[pltpu.VMEM((o_r * o_c * 25, bs, bs), jnp.float32)],
    )(
        place[1:-1, 1:-1].reshape(-1),
        target[1:-1, 1:-1].reshape(-1),
        ring_of(place),
        ring_of(target).reshape(-1),
        pick,
        ap.reshape(n_r * n_c, 9, bs, bs),
        halo_ring(top, bottom, left, right),
        p_t,
    )
    return out.reshape(o_r, o_c, stencil, bs, bs)


def solution(mesh):
    return jax.shard_map(
        body,
        mesh=mesh,
        in_specs=(
            P("row", "col", None, None, None),
            P("row", "col", None),
            P("row", "col", None, None, None),
            P("row", "col", None),
            P("row", "col", None),
        ),
        out_specs=P("row", "col", None, None, None),
        check_vma=False,
    )
```

```python
import jax
import jax.numpy as jnp
from jax import lax
from jax.experimental import pallas as pl
from jax.experimental.pallas import tpu as pltpu
from jax.sharding import PartitionSpec as P


def mirror(values, limit):
    values = jnp.where(values < 0, -values, values)
    return jnp.where(values >= limit, 2 * (limit - 1) - values, values)


def shifted(piece, down, right):
    rows, cols = lax.axis_size("row"), lax.axis_size("col")
    if right == 0:
        pairs = [(s, s + down) for s in range(rows) if 0 <= s + down < rows]
        return lax.ppermute(piece, "row", pairs)
    if down == 0:
        pairs = [(s, s + right) for s in range(cols) if 0 <= s + right < cols]
        return lax.ppermute(piece, "col", pairs)
    pairs = []
    for sr in range(rows):
        for sc in range(cols):
            tr, tc = sr + down, sc + right
            if 0 <= tr < rows and 0 <= tc < cols:
                pairs.append((sr * cols + sc, tr * cols + tc))
    return lax.ppermute(piece, ("row", "col"), pairs)


def dense_shifted(piece, down, right):
    rows, cols = piece.shape[-2], piece.shape[-1]
    lanes = 128 if (rows * cols) % 128 == 0 and cols < 128 else cols
    packed = piece.reshape(piece.shape[:-2] + (rows * cols // lanes, lanes))
    return shifted(packed, down, right).reshape(piece.shape)


def halo_sides(x):
    top = dense_shifted(x[-1], 1, 0)
    bottom = dense_shifted(x[0], -1, 0)
    left = dense_shifted(jnp.concatenate([top[-1:], x[:, -1], bottom[-1:]], axis=0), 0, 1)
    right = dense_shifted(jnp.concatenate([top[:1], x[:, 0], bottom[:1]], axis=0), 0, -1)
    return top, bottom, left, right


def with_halo(x):
    top, bottom, left, right = halo_sides(x)
    middle = jnp.concatenate([top[None], x, bottom[None]], axis=0)
    return jnp.concatenate([left[:, None], middle, right[:, None]], axis=1)


def halo_ring(x):
    top, bottom, left, right = halo_sides(x)
    return jnp.concatenate(
        [left[:1], top, right[:1], left[-1:], bottom, right[-1:], left[1:-1], right[1:-1]], axis=0
    )


def ap_kernel(near_ref, slot_ref, a_ref, p_ref, out_ref, dense_ref, acc_ref):
    tiles, terms = a_ref.shape[0], a_ref.shape[1]

    def one_tile(t, carry):
        acc_ref[...] = jnp.zeros(acc_ref.shape, jnp.float32)
        for k in range(terms):
            j = near_ref[t * terms + k]
            a = a_ref[t, k]
            for q in range(4):
                e = slot_ref[(t * terms + k) * 4 + q]
                keep = jnp.where(e >= 0, 1.0, 0.0).astype(jnp.float32)
                prod = jnp.dot(a, p_ref[j, q], preferred_element_type=jnp.float32)
                acc_ref[jnp.clip(e, 0, 8)] += prod * keep

        ap = acc_ref[...].astype(out_ref.dtype)
        out_ref[t] = ap
        dense_ref[t] = ap.reshape(dense_ref.shape[1:])
        return carry

    lax.fori_loop(0, tiles, one_tile, 0)


def add_terms(where_ref, target_ref, ap_ref, pt_ref, acc_ref):
    def one_tile(t, carry):
        w = where_ref[t]
        blocks = [ap_ref[t, e].reshape(pt_ref.shape[1:]) for e in range(9)]
        for q in range(4):
            g = target_ref[t * 4 + q]

            @pl.when(g >= 0)
            def _():
                pt = pt_ref[w * 4 + q]
                for e in range(9):
                    acc_ref[g + (e // 3) * 5 + e % 3] += jnp.dot(pt, blocks[e], preferred_element_type=jnp.float32)

        return carry

    lax.fori_loop(0, ap_ref.shape[0], one_tile, 0)


def coarse_kernel(
    own_where_ref, own_target_ref, ring_where_ref, ring_target_ref, pick_ref, own_ref, ring_ref, pt_ref, out_ref, acc_ref
):
    acc_ref[...] = jnp.zeros(acc_ref.shape, jnp.float32)
    add_terms(own_where_ref, own_target_ref, own_ref, pt_ref, acc_ref)
    add_terms(ring_where_ref, ring_target_ref, ring_ref, pt_ref, acc_ref)
    owned, stencil = out_ref.shape[0], out_ref.shape[1]

    def one_pick(i, carry):
        a = i // stencil
        out_ref[a, i % stencil] = acc_ref[a * stencil + pick_ref[i]].astype(out_ref.dtype)
        return carry

    lax.fori_loop(0, owned * stencil, one_pick, 0)


def ring_of(x):
    return jnp.concatenate([x[0], x[-1], x[1:-1, 0], x[1:-1, -1]], axis=0)


def body(a_blocks, a_cols, p_blocks, p_cols, c_cols):
    n_r, n_c = a_blocks.shape[0], a_blocks.shape[1]
    bs = a_blocks.shape[-1]
    terms = a_blocks.shape[2]
    grid_rows = n_r * lax.axis_size("row")
    grid_cols = n_c * lax.axis_size("col")
    coarse_rows, coarse_cols = grid_rows // 2, grid_cols // 2
    y0 = lax.axis_index("row") * n_r
    x0 = lax.axis_index("col") * n_c
    ys = y0 + jnp.arange(n_r, dtype=jnp.int32)
    xs = x0 + jnp.arange(n_c, dtype=jnp.int32)
    two = jnp.arange(2, dtype=jnp.int32)

    agg_y = mirror((ys - 1)[:, None] // 2 + two, coarse_rows)
    agg_x = mirror((xs - 1)[:, None] // 2 + two, coarse_cols)
    wanted = (agg_y[:, None, :, None] * coarse_cols + agg_x[None, :, None, :]).reshape(n_r, n_c, 4)
    match = p_cols[:, :, None, :] == wanted[:, :, :, None]
    canon = jnp.sum(
        jnp.where(match[..., None, None], p_blocks[:, :, None], jnp.zeros((), p_blocks.dtype)),
        axis=3,
        dtype=p_blocks.dtype,
    )
    p_ext = with_halo(canon)
    ext_r, ext_c = n_r + 2, n_c + 2

    near_y = a_cols // grid_cols
    near_x = a_cols % grid_cols
    near = jnp.clip(near_y - (y0 - 1), 0, ext_r - 1) * ext_c + jnp.clip(near_x - (x0 - 1), 0, ext_c - 1)
    near_agg_y = mirror((near_y - 1)[..., None] // 2 + two, coarse_rows)
    near_agg_x = mirror((near_x - 1)[..., None] // 2 + two, coarse_cols)
    slot_y = near_agg_y - (ys // 2 - 1)[:, None, None, None]
    slot_x = near_agg_x - (xs // 2 - 1)[None, :, None, None]
    slot = (slot_y[..., :, None] * 3 + slot_x[..., None, :]).reshape(n_r, n_c, terms, 4)
    slot = jnp.where((slot >= 0) & (slot < 9), slot, -1)

    ap, ap_dense = pl.pallas_call(
        ap_kernel,
        out_shape=(
            jax.ShapeDtypeStruct((n_r * n_c, 9, bs, bs), jnp.bfloat16),
            jax.ShapeDtypeStruct((n_r * n_c, 9, bs * bs // 128, 128), jnp.bfloat16),
        ),
        in_specs=[
            pl.BlockSpec(memory_space=pltpu.SMEM),
            pl.BlockSpec(memory_space=pltpu.SMEM),
            pl.BlockSpec(memory_space=pltpu.VMEM),
            pl.BlockSpec(memory_space=pltpu.VMEM),
        ],
        out_specs=(pl.BlockSpec(memory_space=pltpu.VMEM), pl.BlockSpec(memory_space=pltpu.VMEM)),
        scratch_shapes=[pltpu.VMEM((9, bs, bs), jnp.float32)],
    )(
        near.reshape(-1),
        slot.reshape(-1),
        a_blocks.reshape(n_r * n_c, terms, bs, bs),
        p_ext.reshape(ext_r * ext_c, 4, bs, bs),
    )
    ap = ap.reshape(n_r, n_c, 9, bs, bs)
    ap_dense = ap_dense.reshape((n_r, n_c) + ap_dense.shape[1:])

    o_r, o_c = n_r // 2, n_c // 2
    ey = y0 - 1 + jnp.arange(ext_r, dtype=jnp.int32)
    ex = x0 - 1 + jnp.arange(ext_c, dtype=jnp.int32)
    e_agg_y = mirror((ey - 1)[:, None] // 2 + two, coarse_rows)
    e_agg_x = mirror((ex - 1)[:, None] // 2 + two, coarse_cols)
    own_y = e_agg_y - y0 // 2
    own_x = e_agg_x - x0 // 2
    off_y = (ey // 2 - 1)[:, None] - e_agg_y + 2
    off_x = (ex // 2 - 1)[:, None] - e_agg_x + 2
    ok_y = (ey >= 0)[:, None] & (ey < grid_rows)[:, None] & (own_y >= 0) & (own_y < o_r) & (off_y >= 0) & (off_y <= 2)
    ok_x = (ex >= 0)[:, None] & (ex < grid_cols)[:, None] & (own_x >= 0) & (own_x < o_c) & (off_x >= 0) & (off_x <= 2)
    target = (own_y[:, None, :, None] * o_c + own_x[None, :, None, :]) * 25 + (
        off_y[:, None, :, None] * 5 + off_x[None, :, None, :]
    )
    target = jnp.where(ok_y[:, None, :, None] & ok_x[None, :, None, :], target, -1).reshape(ext_r, ext_c, 4)
    place = jnp.arange(ext_r * ext_c, dtype=jnp.int32).reshape(ext_r, ext_c)

    cy = ys[0] // 2 + jnp.arange(o_r, dtype=jnp.int32)
    cx = xs[0] // 2 + jnp.arange(o_c, dtype=jnp.int32)
    pick = (c_cols // coarse_cols - cy[:, None, None] + 2) * 5 + (c_cols % coarse_cols - cx[None, :, None] + 2)
    pick = jnp.clip(pick, 0, 24).reshape(-1)

    p_t = jnp.swapaxes(p_ext, -1, -2).reshape(ext_r * ext_c * 4, bs, bs)
    stencil = c_cols.shape[-1]
    ring_tiles = 2 * ext_c + 2 * n_r
    out = pl.pallas_call(
        coarse_kernel,
        out_shape=jax.ShapeDtypeStruct((o_r * o_c, stencil, bs, bs), jnp.bfloat16),
        in_specs=[pl.BlockSpec(memory_space=pltpu.SMEM)] * 5 + [pl.BlockSpec(memory_space=pltpu.VMEM)] * 3,
        out_specs=pl.BlockSpec(memory_space=pltpu.VMEM),
        scratch_shapes=[pltpu.VMEM((o_r * o_c * 25, bs, bs), jnp.float32)],
    )(
        place[1:-1, 1:-1].reshape(-1),
        target[1:-1, 1:-1].reshape(-1),
        ring_of(place),
        ring_of(target).reshape(-1),
        pick,
        ap.reshape(n_r * n_c, 9, bs, bs),
        halo_ring(ap_dense),
        p_t,
    )
    return out.reshape(o_r, o_c, stencil, bs, bs)


def solution(mesh):
    return jax.shard_map(
        body,
        mesh=mesh,
        in_specs=(
            P("row", "col", None, None, None),
            P("row", "col", None),
            P("row", "col", None, None, None),
            P("row", "col", None),
            P("row", "col", None),
        ),
        out_specs=P("row", "col", None, None, None),
        check_vma=False,
    )
```

```python
import jax
import jax.numpy as jnp
from jax import lax
from jax.experimental import pallas as pl
from jax.experimental.pallas import tpu as pltpu
from jax.sharding import PartitionSpec as P


def mirror(values, limit):
    values = jnp.where(values < 0, -values, values)
    return jnp.where(values >= limit, 2 * (limit - 1) - values, values)


def shifted(piece, down, right):
    rows, cols = lax.axis_size("row"), lax.axis_size("col")
    if right == 0:
        pairs = [(s, s + down) for s in range(rows) if 0 <= s + down < rows]
        return lax.ppermute(piece, "row", pairs)
    if down == 0:
        pairs = [(s, s + right) for s in range(cols) if 0 <= s + right < cols]
        return lax.ppermute(piece, "col", pairs)
    pairs = []
    for sr in range(rows):
        for sc in range(cols):
            tr, tc = sr + down, sc + right
            if 0 <= tr < rows and 0 <= tc < cols:
                pairs.append((sr * cols + sc, tr * cols + tc))
    return lax.ppermute(piece, ("row", "col"), pairs)


def dense_shifted(piece, down, right):
    rows, cols = piece.shape[-2], piece.shape[-1]
    lanes = 128 if (rows * cols) % 128 == 0 and cols < 128 else cols
    packed = piece.reshape(piece.shape[:-2] + (rows * cols // lanes, lanes))
    return shifted(packed, down, right).reshape(piece.shape)


def halo_sides(x):
    top = dense_shifted(x[-1], 1, 0)
    bottom = dense_shifted(x[0], -1, 0)
    left = dense_shifted(jnp.concatenate([top[-1:], x[:, -1], bottom[-1:]], axis=0), 0, 1)
    right = dense_shifted(jnp.concatenate([top[:1], x[:, 0], bottom[:1]], axis=0), 0, -1)
    return top, bottom, left, right


def with_halo(x):
    top, bottom, left, right = halo_sides(x)
    middle = jnp.concatenate([top[None], x, bottom[None]], axis=0)
    return jnp.concatenate([left[:, None], middle, right[:, None]], axis=1)


def halo_ring(x):
    top, bottom, left, right = halo_sides(x)
    return jnp.concatenate(
        [left[:1], top, right[:1], left[-1:], bottom, right[-1:], left[1:-1], right[1:-1]], axis=0
    )


def ap_kernel(near_ref, slot_ref, a_ref, p_ref, out_ref, dense_ref, acc_ref):
    tiles, terms = a_ref.shape[0], a_ref.shape[1]

    def one_tile(t, carry):
        acc_ref[...] = jnp.zeros(acc_ref.shape, jnp.float32)
        for k in range(terms):
            j = near_ref[t * terms + k]
            a = a_ref[t, k]
            for q in range(4):
                e = slot_ref[(t * terms + k) * 4 + q]
                keep = jnp.where(e >= 0, 1.0, 0.0).astype(jnp.float32)
                prod = jnp.dot(a, p_ref[j, q], preferred_element_type=jnp.float32)
                acc_ref[jnp.clip(e, 0, 8)] += prod * keep

        ap = acc_ref[...].astype(out_ref.dtype)
        out_ref[t] = ap
        dense_ref[t] = ap.reshape(dense_ref.shape[1:])
        return carry

    lax.fori_loop(0, tiles, one_tile, 0)


def add_terms(where_ref, target_ref, ap_ref, pt_ref, acc_ref):
    def one_tile(t, carry):
        w = where_ref[t]
        blocks = [ap_ref[t, e].reshape(pt_ref.shape[1:]) for e in range(9)]
        for q in range(4):
            g = target_ref[t * 4 + q]

            @pl.when(g >= 0)
            def _():
                pt = pt_ref[w * 4 + q]
                for e in range(9):
                    acc_ref[g + (e // 3) * 5 + e % 3] += jnp.dot(pt, blocks[e], preferred_element_type=jnp.float32)

        return carry

    lax.fori_loop(0, ap_ref.shape[0], one_tile, 0)


def coarse_kernel(*refs):
    groups = (len(refs) - 4) // 3
    tables, pick_ref = refs[: 2 * groups], refs[2 * groups]
    blocks, pt_ref, out_ref, acc_ref = refs[2 * groups + 1 : 3 * groups + 1], refs[-3], refs[-2], refs[-1]
    acc_ref[...] = jnp.zeros(acc_ref.shape, jnp.float32)
    for i in range(groups):
        add_terms(tables[2 * i], tables[2 * i + 1], blocks[i], pt_ref, acc_ref)
    owned, stencil = out_ref.shape[0], out_ref.shape[1]

    def one_pick(i, carry):
        a = i // stencil
        out_ref[a, i % stencil] = acc_ref[a * stencil + pick_ref[i]].astype(out_ref.dtype)
        return carry

    lax.fori_loop(0, owned * stencil, one_pick, 0)


def ring_of(x):
    return jnp.concatenate([x[0], x[-1], x[1:-1, 0], x[1:-1, -1]], axis=0)


def body(a_blocks, a_cols, p_blocks, p_cols, c_cols):
    n_r, n_c = a_blocks.shape[0], a_blocks.shape[1]
    bs = a_blocks.shape[-1]
    terms = a_blocks.shape[2]
    grid_rows = n_r * lax.axis_size("row")
    grid_cols = n_c * lax.axis_size("col")
    coarse_rows, coarse_cols = grid_rows // 2, grid_cols // 2
    y0 = lax.axis_index("row") * n_r
    x0 = lax.axis_index("col") * n_c
    ys = y0 + jnp.arange(n_r, dtype=jnp.int32)
    xs = x0 + jnp.arange(n_c, dtype=jnp.int32)
    two = jnp.arange(2, dtype=jnp.int32)

    agg_y = mirror((ys - 1)[:, None] // 2 + two, coarse_rows)
    agg_x = mirror((xs - 1)[:, None] // 2 + two, coarse_cols)
    wanted = (agg_y[:, None, :, None] * coarse_cols + agg_x[None, :, None, :]).reshape(n_r, n_c, 4)
    match = p_cols[:, :, None, :] == wanted[:, :, :, None]
    canon = jnp.sum(
        jnp.where(match[..., None, None], p_blocks[:, :, None], jnp.zeros((), p_blocks.dtype)),
        axis=3,
        dtype=p_blocks.dtype,
    )
    p_ext = with_halo(canon)
    ext_r, ext_c = n_r + 2, n_c + 2

    near_y = a_cols // grid_cols
    near_x = a_cols % grid_cols
    near = jnp.clip(near_y - (y0 - 1), 0, ext_r - 1) * ext_c + jnp.clip(near_x - (x0 - 1), 0, ext_c - 1)
    near_agg_y = mirror((near_y - 1)[..., None] // 2 + two, coarse_rows)
    near_agg_x = mirror((near_x - 1)[..., None] // 2 + two, coarse_cols)
    slot_y = near_agg_y - (ys // 2 - 1)[:, None, None, None]
    slot_x = near_agg_x - (xs // 2 - 1)[None, :, None, None]
    slot = (slot_y[..., :, None] * 3 + slot_x[..., None, :]).reshape(n_r, n_c, terms, 4)
    slot = jnp.where((slot >= 0) & (slot < 9), slot, -1)

    ap, ap_dense = pl.pallas_call(
        ap_kernel,
        out_shape=(
            jax.ShapeDtypeStruct((n_r * n_c, 9, bs, bs), jnp.bfloat16),
            jax.ShapeDtypeStruct((n_r * n_c, 9, bs * bs // 128, 128), jnp.bfloat16),
        ),
        in_specs=[
            pl.BlockSpec(memory_space=pltpu.SMEM),
            pl.BlockSpec(memory_space=pltpu.SMEM),
            pl.BlockSpec(memory_space=pltpu.VMEM),
            pl.BlockSpec(memory_space=pltpu.VMEM),
        ],
        out_specs=(pl.BlockSpec(memory_space=pltpu.VMEM), pl.BlockSpec(memory_space=pltpu.VMEM)),
        scratch_shapes=[pltpu.VMEM((9, bs, bs), jnp.float32)],
    )(
        near.reshape(-1),
        slot.reshape(-1),
        a_blocks.reshape(n_r * n_c, terms, bs, bs),
        p_ext.reshape(ext_r * ext_c, 4, bs, bs),
    )
    ap = ap.reshape(n_r, n_c, 9, bs, bs)
    ap_dense = ap_dense.reshape((n_r, n_c) + ap_dense.shape[1:])

    o_r, o_c = n_r // 2, n_c // 2
    ey = y0 - 1 + jnp.arange(ext_r, dtype=jnp.int32)
    ex = x0 - 1 + jnp.arange(ext_c, dtype=jnp.int32)
    e_agg_y = mirror((ey - 1)[:, None] // 2 + two, coarse_rows)
    e_agg_x = mirror((ex - 1)[:, None] // 2 + two, coarse_cols)
    own_y = e_agg_y - y0 // 2
    own_x = e_agg_x - x0 // 2
    off_y = (ey // 2 - 1)[:, None] - e_agg_y + 2
    off_x = (ex // 2 - 1)[:, None] - e_agg_x + 2
    ok_y = (ey >= 0)[:, None] & (ey < grid_rows)[:, None] & (own_y >= 0) & (own_y < o_r) & (off_y >= 0) & (off_y <= 2)
    ok_x = (ex >= 0)[:, None] & (ex < grid_cols)[:, None] & (own_x >= 0) & (own_x < o_c) & (off_x >= 0) & (off_x <= 2)
    target = (own_y[:, None, :, None] * o_c + own_x[None, :, None, :]) * 25 + (
        off_y[:, None, :, None] * 5 + off_x[None, :, None, :]
    )
    target = jnp.where(ok_y[:, None, :, None] & ok_x[None, :, None, :], target, -1).reshape(ext_r, ext_c, 4)
    place = jnp.arange(ext_r * ext_c, dtype=jnp.int32).reshape(ext_r, ext_c)

    cy = ys[0] // 2 + jnp.arange(o_r, dtype=jnp.int32)
    cx = xs[0] // 2 + jnp.arange(o_c, dtype=jnp.int32)
    pick = (c_cols // coarse_cols - cy[:, None, None] + 2) * 5 + (c_cols % coarse_cols - cx[None, :, None] + 2)
    pick = jnp.clip(pick, 0, 24).reshape(-1)

    p_t = jnp.swapaxes(p_ext, -1, -2).reshape(ext_r * ext_c * 4, bs, bs)
    stencil = c_cols.shape[-1]
    top, bottom, left, right = halo_sides(ap_dense)
    parts = [
        (place[1:-1, 1:-1], target[1:-1, 1:-1], ap.reshape(n_r * n_c, 9, bs, bs)),
        (place[0, 1:-1], target[0, 1:-1], top),
        (place[-1, 1:-1], target[-1, 1:-1], bottom),
        (place[:, 0], target[:, 0], left),
        (place[:, -1], target[:, -1], right),
    ]
    out = pl.pallas_call(
        coarse_kernel,
        out_shape=jax.ShapeDtypeStruct((o_r * o_c, stencil, bs, bs), jnp.bfloat16),
        in_specs=[pl.BlockSpec(memory_space=pltpu.SMEM)] * (2 * len(parts) + 1)
        + [pl.BlockSpec(memory_space=pltpu.VMEM)] * (len(parts) + 1),
        out_specs=pl.BlockSpec(memory_space=pltpu.VMEM),
        scratch_shapes=[pltpu.VMEM((o_r * o_c * 25, bs, bs), jnp.float32)],
    )(
        *[t for w, g, _ in parts for t in (w.reshape(-1), g.reshape(-1))],
        pick,
        *[b for _, _, b in parts],
        p_t,
    )
    return out.reshape(o_r, o_c, stencil, bs, bs)


def solution(mesh):
    return jax.shard_map(
        body,
        mesh=mesh,
        in_specs=(
            P("row", "col", None, None, None),
            P("row", "col", None),
            P("row", "col", None, None, None),
            P("row", "col", None),
            P("row", "col", None),
        ),
        out_specs=P("row", "col", None, None, None),
        check_vma=False,
    )
```

```python
import jax
import jax.numpy as jnp
from jax import lax
from jax.experimental import pallas as pl
from jax.experimental.pallas import tpu as pltpu
from jax.sharding import PartitionSpec as P


def mirror(values, limit):
    values = jnp.where(values < 0, -values, values)
    return jnp.where(values >= limit, 2 * (limit - 1) - values, values)


def shifted(piece, down, right):
    rows, cols = lax.axis_size("row"), lax.axis_size("col")
    if right == 0:
        pairs = [(s, s + down) for s in range(rows) if 0 <= s + down < rows]
        return lax.ppermute(piece, "row", pairs)
    if down == 0:
        pairs = [(s, s + right) for s in range(cols) if 0 <= s + right < cols]
        return lax.ppermute(piece, "col", pairs)
    pairs = []
    for sr in range(rows):
        for sc in range(cols):
            tr, tc = sr + down, sc + right
            if 0 <= tr < rows and 0 <= tc < cols:
                pairs.append((sr * cols + sc, tr * cols + tc))
    return lax.ppermute(piece, ("row", "col"), pairs)


def dense_shifted(piece, down, right):
    rows, cols = piece.shape[-2], piece.shape[-1]
    lanes = 128 if (rows * cols) % 128 == 0 and cols < 128 else cols
    packed = piece.reshape(piece.shape[:-2] + (rows * cols // lanes, lanes))
    return shifted(packed, down, right).reshape(piece.shape)


def halo_sides(x):
    top = dense_shifted(x[-1], 1, 0)
    bottom = dense_shifted(x[0], -1, 0)
    left = dense_shifted(jnp.concatenate([top[-1:], x[:, -1], bottom[-1:]], axis=0), 0, 1)
    right = dense_shifted(jnp.concatenate([top[:1], x[:, 0], bottom[:1]], axis=0), 0, -1)
    return top, bottom, left, right


def with_halo(x):
    top, bottom, left, right = halo_sides(x)
    middle = jnp.concatenate([top[None], x, bottom[None]], axis=0)
    return jnp.concatenate([left[:, None], middle, right[:, None]], axis=1)


def halo_ring(x):
    top, bottom, left, right = halo_sides(x)
    return jnp.concatenate(
        [left[:1], top, right[:1], left[-1:], bottom, right[-1:], left[1:-1], right[1:-1]], axis=0
    )


def ap_kernel(near_ref, slot_ref, a_ref, p_ref, out_ref, dense_ref, acc_ref):
    tiles, terms = a_ref.shape[0], a_ref.shape[1]

    def one_tile(t, carry):
        acc_ref[...] = jnp.zeros(acc_ref.shape, jnp.float32)
        for k in range(terms):
            j = near_ref[t * terms + k]
            a = a_ref[t, k]
            for q in range(4):
                e = slot_ref[(t * terms + k) * 4 + q]
                keep = jnp.where(e >= 0, 1.0, 0.0).astype(jnp.float32)
                prod = jnp.dot(a, p_ref[j, q], preferred_element_type=jnp.float32)
                acc_ref[jnp.clip(e, 0, 8)] += prod * keep

        ap = acc_ref[...].astype(out_ref.dtype)
        out_ref[t] = ap
        dense_ref[t] = ap.reshape(dense_ref.shape[1:])
        return carry

    lax.fori_loop(0, tiles, one_tile, 0)


def add_terms(where_ref, target_ref, ap_ref, pt_ref, acc_ref):
    def one_tile(t, carry):
        w = where_ref[t]
        blocks = [ap_ref[t, e].reshape(pt_ref.shape[1:]) for e in range(9)]
        for q in range(4):
            g = target_ref[t * 4 + q]

            @pl.when(g >= 0)
            def _():
                pt = pt_ref[w * 4 + q]
                for e in range(9):
                    acc_ref[g + (e // 3) * 5 + e % 3] += jnp.dot(pt, blocks[e], preferred_element_type=jnp.float32)

        return carry

    lax.fori_loop(0, ap_ref.shape[0], one_tile, 0)


def own_kernel(where_ref, target_ref, ap_ref, pt_ref, acc_ref):
    acc_ref[...] = jnp.zeros(acc_ref.shape, jnp.float32)
    add_terms(where_ref, target_ref, ap_ref, pt_ref, acc_ref)


def coarse_kernel(*refs):
    groups = (len(refs) - 5) // 3
    tables, pick_ref = refs[: 2 * groups], refs[2 * groups]
    blocks = refs[2 * groups + 1 : 3 * groups + 1]
    pt_ref, part_ref, out_ref, acc_ref = refs[-4], refs[-3], refs[-2], refs[-1]
    acc_ref[...] = part_ref[...]
    for i in range(groups):
        add_terms(tables[2 * i], tables[2 * i + 1], blocks[i], pt_ref, acc_ref)
    owned, stencil = out_ref.shape[0], out_ref.shape[1]

    def one_pick(i, carry):
        a = i // stencil
        out_ref[a, i % stencil] = acc_ref[a * stencil + pick_ref[i]].astype(out_ref.dtype)
        return carry

    lax.fori_loop(0, owned * stencil, one_pick, 0)


def ring_of(x):
    return jnp.concatenate([x[0], x[-1], x[1:-1, 0], x[1:-1, -1]], axis=0)


def body(a_blocks, a_cols, p_blocks, p_cols, c_cols):
    n_r, n_c = a_blocks.shape[0], a_blocks.shape[1]
    bs = a_blocks.shape[-1]
    terms = a_blocks.shape[2]
    grid_rows = n_r * lax.axis_size("row")
    grid_cols = n_c * lax.axis_size("col")
    coarse_rows, coarse_cols = grid_rows // 2, grid_cols // 2
    y0 = lax.axis_index("row") * n_r
    x0 = lax.axis_index("col") * n_c
    ys = y0 + jnp.arange(n_r, dtype=jnp.int32)
    xs = x0 + jnp.arange(n_c, dtype=jnp.int32)
    two = jnp.arange(2, dtype=jnp.int32)

    agg_y = mirror((ys - 1)[:, None] // 2 + two, coarse_rows)
    agg_x = mirror((xs - 1)[:, None] // 2 + two, coarse_cols)
    wanted = (agg_y[:, None, :, None] * coarse_cols + agg_x[None, :, None, :]).reshape(n_r, n_c, 4)
    match = p_cols[:, :, None, :] == wanted[:, :, :, None]
    canon = jnp.sum(
        jnp.where(match[..., None, None], p_blocks[:, :, None], jnp.zeros((), p_blocks.dtype)),
        axis=3,
        dtype=p_blocks.dtype,
    )
    p_ext = with_halo(canon)
    ext_r, ext_c = n_r + 2, n_c + 2

    near_y = a_cols // grid_cols
    near_x = a_cols % grid_cols
    near = jnp.clip(near_y - (y0 - 1), 0, ext_r - 1) * ext_c + jnp.clip(near_x - (x0 - 1), 0, ext_c - 1)
    near_agg_y = mirror((near_y - 1)[..., None] // 2 + two, coarse_rows)
    near_agg_x = mirror((near_x - 1)[..., None] // 2 + two, coarse_cols)
    slot_y = near_agg_y - (ys // 2 - 1)[:, None, None, None]
    slot_x = near_agg_x - (xs // 2 - 1)[None, :, None, None]
    slot = (slot_y[..., :, None] * 3 + slot_x[..., None, :]).reshape(n_r, n_c, terms, 4)
    slot = jnp.where((slot >= 0) & (slot < 9), slot, -1)

    ap, ap_dense = pl.pallas_call(
        ap_kernel,
        out_shape=(
            jax.ShapeDtypeStruct((n_r * n_c, 9, bs, bs), jnp.bfloat16),
            jax.ShapeDtypeStruct((n_r * n_c, 9, bs * bs // 128, 128), jnp.bfloat16),
        ),
        in_specs=[
            pl.BlockSpec(memory_space=pltpu.SMEM),
            pl.BlockSpec(memory_space=pltpu.SMEM),
            pl.BlockSpec(memory_space=pltpu.VMEM),
            pl.BlockSpec(memory_space=pltpu.VMEM),
        ],
        out_specs=(pl.BlockSpec(memory_space=pltpu.VMEM), pl.BlockSpec(memory_space=pltpu.VMEM)),
        scratch_shapes=[pltpu.VMEM((9, bs, bs), jnp.float32)],
    )(
        near.reshape(-1),
        slot.reshape(-1),
        a_blocks.reshape(n_r * n_c, terms, bs, bs),
        p_ext.reshape(ext_r * ext_c, 4, bs, bs),
    )
    ap = ap.reshape(n_r, n_c, 9, bs, bs)
    ap_dense = ap_dense.reshape((n_r, n_c) + ap_dense.shape[1:])

    o_r, o_c = n_r // 2, n_c // 2
    ey = y0 - 1 + jnp.arange(ext_r, dtype=jnp.int32)
    ex = x0 - 1 + jnp.arange(ext_c, dtype=jnp.int32)
    e_agg_y = mirror((ey - 1)[:, None] // 2 + two, coarse_rows)
    e_agg_x = mirror((ex - 1)[:, None] // 2 + two, coarse_cols)
    own_y = e_agg_y - y0 // 2
    own_x = e_agg_x - x0 // 2
    off_y = (ey // 2 - 1)[:, None] - e_agg_y + 2
    off_x = (ex // 2 - 1)[:, None] - e_agg_x + 2
    ok_y = (ey >= 0)[:, None] & (ey < grid_rows)[:, None] & (own_y >= 0) & (own_y < o_r) & (off_y >= 0) & (off_y <= 2)
    ok_x = (ex >= 0)[:, None] & (ex < grid_cols)[:, None] & (own_x >= 0) & (own_x < o_c) & (off_x >= 0) & (off_x <= 2)
    target = (own_y[:, None, :, None] * o_c + own_x[None, :, None, :]) * 25 + (
        off_y[:, None, :, None] * 5 + off_x[None, :, None, :]
    )
    target = jnp.where(ok_y[:, None, :, None] & ok_x[None, :, None, :], target, -1).reshape(ext_r, ext_c, 4)
    place = jnp.arange(ext_r * ext_c, dtype=jnp.int32).reshape(ext_r, ext_c)

    cy = ys[0] // 2 + jnp.arange(o_r, dtype=jnp.int32)
    cx = xs[0] // 2 + jnp.arange(o_c, dtype=jnp.int32)
    pick = (c_cols // coarse_cols - cy[:, None, None] + 2) * 5 + (c_cols % coarse_cols - cx[None, :, None] + 2)
    pick = jnp.clip(pick, 0, 24).reshape(-1)

    p_t = jnp.swapaxes(p_ext, -1, -2).reshape(ext_r * ext_c * 4, bs, bs)
    stencil = c_cols.shape[-1]
    smem = pl.BlockSpec(memory_space=pltpu.SMEM)
    vmem = pl.BlockSpec(memory_space=pltpu.VMEM)
    acc_shape = (o_r * o_c * 25, bs, bs)
    part = pl.pallas_call(
        own_kernel,
        out_shape=jax.ShapeDtypeStruct(acc_shape, jnp.float32),
        in_specs=[smem, smem, vmem, vmem],
        out_specs=vmem,
        cost_estimate=pl.CostEstimate(
            flops=2 * bs * bs * bs * 9 * n_r * n_c * 4, bytes_accessed=6 * 1024 * 1024, transcendentals=0
        ),
    )(place[1:-1, 1:-1].reshape(-1), target[1:-1, 1:-1].reshape(-1), ap.reshape(n_r * n_c, 9, bs, bs), p_t)
    top, bottom, left, right = halo_sides(ap_dense)
    parts = [
        (place[0, 1:-1], target[0, 1:-1], top),
        (place[-1, 1:-1], target[-1, 1:-1], bottom),
        (place[:, 0], target[:, 0], left),
        (place[:, -1], target[:, -1], right),
    ]
    out = pl.pallas_call(
        coarse_kernel,
        out_shape=jax.ShapeDtypeStruct((o_r * o_c, stencil, bs, bs), jnp.bfloat16),
        in_specs=[smem] * (2 * len(parts) + 1) + [vmem] * (len(parts) + 2),
        out_specs=vmem,
        scratch_shapes=[pltpu.VMEM(acc_shape, jnp.float32)],
    )(
        *[t for w, g, _ in parts for t in (w.reshape(-1), g.reshape(-1))],
        pick,
        *[b for _, _, b in parts],
        p_t,
        part,
    )
    return out.reshape(o_r, o_c, stencil, bs, bs)


def solution(mesh):
    return jax.shard_map(
        body,
        mesh=mesh,
        in_specs=(
            P("row", "col", None, None, None),
            P("row", "col", None),
            P("row", "col", None, None, None),
            P("row", "col", None),
            P("row", "col", None),
        ),
        out_specs=P("row", "col", None, None, None),
        check_vma=False,
    )
```

```python
import functools

import jax
import jax.numpy as jnp
from jax import lax
from jax.experimental import pallas as pl
from jax.experimental.pallas import tpu as pltpu
from jax.sharding import PartitionSpec as P


def mirror(values, limit):
    values = jnp.where(values < 0, -values, values)
    return jnp.where(values >= limit, 2 * (limit - 1) - values, values)


def shifted(piece, down, right):
    rows, cols = lax.axis_size("row"), lax.axis_size("col")
    if right == 0:
        pairs = [(s, s + down) for s in range(rows) if 0 <= s + down < rows]
        return lax.ppermute(piece, "row", pairs)
    if down == 0:
        pairs = [(s, s + right) for s in range(cols) if 0 <= s + right < cols]
        return lax.ppermute(piece, "col", pairs)
    pairs = []
    for sr in range(rows):
        for sc in range(cols):
            tr, tc = sr + down, sc + right
            if 0 <= tr < rows and 0 <= tc < cols:
                pairs.append((sr * cols + sc, tr * cols + tc))
    return lax.ppermute(piece, ("row", "col"), pairs)


def dense_shifted(piece, down, right):
    rows, cols = piece.shape[-2], piece.shape[-1]
    lanes = 128 if (rows * cols) % 128 == 0 and cols < 128 else cols
    packed = piece.reshape(piece.shape[:-2] + (rows * cols // lanes, lanes))
    return shifted(packed, down, right).reshape(piece.shape)


def halo_sides(x):
    top = dense_shifted(x[-1], 1, 0)
    bottom = dense_shifted(x[0], -1, 0)
    left = dense_shifted(jnp.concatenate([top[-1:], x[:, -1], bottom[-1:]], axis=0), 0, 1)
    right = dense_shifted(jnp.concatenate([top[:1], x[:, 0], bottom[:1]], axis=0), 0, -1)
    return top, bottom, left, right


def with_halo(x):
    top, bottom, left, right = halo_sides(x)
    middle = jnp.concatenate([top[None], x, bottom[None]], axis=0)
    return jnp.concatenate([left[:, None], middle, right[:, None]], axis=1)


def halo_ring(x):
    top, bottom, left, right = halo_sides(x)
    return jnp.concatenate(
        [left[:1], top, right[:1], left[-1:], bottom, right[-1:], left[1:-1], right[1:-1]], axis=0
    )


def ap_kernel(near_ref, slot_ref, a_ref, p_ref, out_ref, dense_ref, acc_ref, *, n_r, n_c):
    tiles, terms = a_ref.shape[0], a_ref.shape[1]

    def one_tile(t, carry):
        acc_ref[...] = jnp.zeros(acc_ref.shape, jnp.float32)
        for k in range(terms):
            j = near_ref[t * terms + k]
            a = a_ref[t, k]
            for q in range(4):
                e = slot_ref[(t * terms + k) * 4 + q]
                keep = jnp.where(e >= 0, 1.0, 0.0).astype(jnp.float32)
                prod = jnp.dot(a, p_ref[j, q], preferred_element_type=jnp.float32)
                acc_ref[jnp.clip(e, 0, 8)] += prod * keep

        ap = acc_ref[...].astype(out_ref.dtype)
        out_ref[t] = ap
        row, col = t // n_c, t % n_c

        @pl.when((row == 0) | (row == n_r - 1) | (col == 0) | (col == n_c - 1))
        def _():
            dense_ref[t] = ap.reshape(dense_ref.shape[1:])

        return carry

    lax.fori_loop(0, tiles, one_tile, 0)


def add_terms(where_ref, target_ref, ap_ref, pt_ref, acc_ref):
    def one_tile(t, carry):
        w = where_ref[t]
        blocks = [ap_ref[t, e].reshape(pt_ref.shape[1:]) for e in range(9)]
        for q in range(4):
            g = target_ref[t * 4 + q]

            @pl.when(g >= 0)
            def _():
                p = pt_ref[w * 4 + q]
                for e in range(9):
                    acc_ref[g + (e // 3) * 5 + e % 3] += lax.dot_general(
                        p, blocks[e], (((0,), (0,)), ((), ())), preferred_element_type=jnp.float32
                    )

        return carry

    lax.fori_loop(0, ap_ref.shape[0], one_tile, 0)


def own_kernel(where_ref, target_ref, ap_ref, pt_ref, acc_ref):
    acc_ref[...] = jnp.zeros(acc_ref.shape, jnp.float32)
    add_terms(where_ref, target_ref, ap_ref, pt_ref, acc_ref)


def coarse_kernel(*refs):
    groups = (len(refs) - 5) // 3
    tables, pick_ref = refs[: 2 * groups], refs[2 * groups]
    blocks = refs[2 * groups + 1 : 3 * groups + 1]
    pt_ref, part_ref, out_ref, acc_ref = refs[-4], refs[-3], refs[-2], refs[-1]
    acc_ref[...] = part_ref[...]
    for i in range(groups):
        add_terms(tables[2 * i], tables[2 * i + 1], blocks[i], pt_ref, acc_ref)
    owned, stencil = out_ref.shape[0], out_ref.shape[1]

    def one_pick(i, carry):
        a = i // stencil
        out_ref[a, i % stencil] = acc_ref[a * stencil + pick_ref[i]].astype(out_ref.dtype)
        return carry

    lax.fori_loop(0, owned * stencil, one_pick, 0)


def ring_of(x):
    return jnp.concatenate([x[0], x[-1], x[1:-1, 0], x[1:-1, -1]], axis=0)


def body(a_blocks, a_cols, p_blocks, p_cols, c_cols):
    n_r, n_c = a_blocks.shape[0], a_blocks.shape[1]
    bs = a_blocks.shape[-1]
    terms = a_blocks.shape[2]
    grid_rows = n_r * lax.axis_size("row")
    grid_cols = n_c * lax.axis_size("col")
    coarse_rows, coarse_cols = grid_rows // 2, grid_cols // 2
    y0 = lax.axis_index("row") * n_r
    x0 = lax.axis_index("col") * n_c
    ys = y0 + jnp.arange(n_r, dtype=jnp.int32)
    xs = x0 + jnp.arange(n_c, dtype=jnp.int32)
    two = jnp.arange(2, dtype=jnp.int32)

    agg_y = mirror((ys - 1)[:, None] // 2 + two, coarse_rows)
    agg_x = mirror((xs - 1)[:, None] // 2 + two, coarse_cols)
    wanted = (agg_y[:, None, :, None] * coarse_cols + agg_x[None, :, None, :]).reshape(n_r, n_c, 4)
    match = p_cols[:, :, None, :] == wanted[:, :, :, None]
    canon = jnp.sum(
        jnp.where(match[..., None, None], p_blocks[:, :, None], jnp.zeros((), p_blocks.dtype)),
        axis=3,
        dtype=p_blocks.dtype,
    )
    p_ext = with_halo(canon)
    ext_r, ext_c = n_r + 2, n_c + 2

    near_y = a_cols // grid_cols
    near_x = a_cols % grid_cols
    near = jnp.clip(near_y - (y0 - 1), 0, ext_r - 1) * ext_c + jnp.clip(near_x - (x0 - 1), 0, ext_c - 1)
    near_agg_y = mirror((near_y - 1)[..., None] // 2 + two, coarse_rows)
    near_agg_x = mirror((near_x - 1)[..., None] // 2 + two, coarse_cols)
    slot_y = near_agg_y - (ys // 2 - 1)[:, None, None, None]
    slot_x = near_agg_x - (xs // 2 - 1)[None, :, None, None]
    slot = (slot_y[..., :, None] * 3 + slot_x[..., None, :]).reshape(n_r, n_c, terms, 4)
    slot = jnp.where((slot >= 0) & (slot < 9), slot, -1)

    ap, ap_dense = pl.pallas_call(
        functools.partial(ap_kernel, n_r=n_r, n_c=n_c),
        out_shape=(
            jax.ShapeDtypeStruct((n_r * n_c, 9, bs, bs), jnp.bfloat16),
            jax.ShapeDtypeStruct((n_r * n_c, 9, bs * bs // 128, 128), jnp.bfloat16),
        ),
        in_specs=[
            pl.BlockSpec(memory_space=pltpu.SMEM),
            pl.BlockSpec(memory_space=pltpu.SMEM),
            pl.BlockSpec(memory_space=pltpu.VMEM),
            pl.BlockSpec(memory_space=pltpu.VMEM),
        ],
        out_specs=(pl.BlockSpec(memory_space=pltpu.VMEM), pl.BlockSpec(memory_space=pltpu.VMEM)),
        scratch_shapes=[pltpu.VMEM((9, bs, bs), jnp.float32)],
    )(
        near.reshape(-1),
        slot.reshape(-1),
        a_blocks.reshape(n_r * n_c, terms, bs, bs),
        p_ext.reshape(ext_r * ext_c, 4, bs, bs),
    )
    ap = ap.reshape(n_r, n_c, 9, bs, bs)
    ap_dense = ap_dense.reshape((n_r, n_c) + ap_dense.shape[1:])

    o_r, o_c = n_r // 2, n_c // 2
    ey = y0 - 1 + jnp.arange(ext_r, dtype=jnp.int32)
    ex = x0 - 1 + jnp.arange(ext_c, dtype=jnp.int32)
    e_agg_y = mirror((ey - 1)[:, None] // 2 + two, coarse_rows)
    e_agg_x = mirror((ex - 1)[:, None] // 2 + two, coarse_cols)
    own_y = e_agg_y - y0 // 2
    own_x = e_agg_x - x0 // 2
    off_y = (ey // 2 - 1)[:, None] - e_agg_y + 2
    off_x = (ex // 2 - 1)[:, None] - e_agg_x + 2
    ok_y = (ey >= 0)[:, None] & (ey < grid_rows)[:, None] & (own_y >= 0) & (own_y < o_r) & (off_y >= 0) & (off_y <= 2)
    ok_x = (ex >= 0)[:, None] & (ex < grid_cols)[:, None] & (own_x >= 0) & (own_x < o_c) & (off_x >= 0) & (off_x <= 2)
    target = (own_y[:, None, :, None] * o_c + own_x[None, :, None, :]) * 25 + (
        off_y[:, None, :, None] * 5 + off_x[None, :, None, :]
    )
    target = jnp.where(ok_y[:, None, :, None] & ok_x[None, :, None, :], target, -1).reshape(ext_r, ext_c, 4)
    place = jnp.arange(ext_r * ext_c, dtype=jnp.int32).reshape(ext_r, ext_c)

    cy = ys[0] // 2 + jnp.arange(o_r, dtype=jnp.int32)
    cx = xs[0] // 2 + jnp.arange(o_c, dtype=jnp.int32)
    pick = (c_cols // coarse_cols - cy[:, None, None] + 2) * 5 + (c_cols % coarse_cols - cx[None, :, None] + 2)
    pick = jnp.clip(pick, 0, 24).reshape(-1)

    p_t = p_ext.reshape(ext_r * ext_c * 4, bs, bs)
    stencil = c_cols.shape[-1]
    smem = pl.BlockSpec(memory_space=pltpu.SMEM)
    vmem = pl.BlockSpec(memory_space=pltpu.VMEM)
    acc_shape = (o_r * o_c * 25, bs, bs)
    part = pl.pallas_call(
        own_kernel,
        out_shape=jax.ShapeDtypeStruct(acc_shape, jnp.float32),
        in_specs=[smem, smem, vmem, vmem],
        out_specs=vmem,
        cost_estimate=pl.CostEstimate(
            flops=2 * bs * bs * bs * 9 * n_r * n_c * 4, bytes_accessed=6 * 1024 * 1024, transcendentals=0
        ),
    )(place[1:-1, 1:-1].reshape(-1), target[1:-1, 1:-1].reshape(-1), ap.reshape(n_r * n_c, 9, bs, bs), p_t)
    top, bottom, left, right = halo_sides(ap_dense)
    parts = [
        (place[0, 1:-1], target[0, 1:-1], top),
        (place[-1, 1:-1], target[-1, 1:-1], bottom),
        (place[:, 0], target[:, 0], left),
        (place[:, -1], target[:, -1], right),
    ]
    out = pl.pallas_call(
        coarse_kernel,
        out_shape=jax.ShapeDtypeStruct((o_r * o_c, stencil, bs, bs), jnp.bfloat16),
        in_specs=[smem] * (2 * len(parts) + 1) + [vmem] * (len(parts) + 2),
        out_specs=vmem,
        scratch_shapes=[pltpu.VMEM(acc_shape, jnp.float32)],
    )(
        *[t for w, g, _ in parts for t in (w.reshape(-1), g.reshape(-1))],
        pick,
        *[b for _, _, b in parts],
        p_t,
        part,
    )
    return out.reshape(o_r, o_c, stencil, bs, bs)


def solution(mesh):
    return jax.shard_map(
        body,
        mesh=mesh,
        in_specs=(
            P("row", "col", None, None, None),
            P("row", "col", None),
            P("row", "col", None, None, None),
            P("row", "col", None),
            P("row", "col", None),
        ),
        out_specs=P("row", "col", None, None, None),
        check_vma=False,
    )
```

```python
import functools

import jax
import jax.numpy as jnp
from jax import lax
from jax.experimental import pallas as pl
from jax.experimental.pallas import tpu as pltpu
from jax.sharding import PartitionSpec as P


def mirror(values, limit):
    values = jnp.where(values < 0, -values, values)
    return jnp.where(values >= limit, 2 * (limit - 1) - values, values)


def shifted(piece, down, right):
    rows, cols = lax.axis_size("row"), lax.axis_size("col")
    if right == 0:
        pairs = [(s, s + down) for s in range(rows) if 0 <= s + down < rows]
        return lax.ppermute(piece, "row", pairs)
    if down == 0:
        pairs = [(s, s + right) for s in range(cols) if 0 <= s + right < cols]
        return lax.ppermute(piece, "col", pairs)
    pairs = []
    for sr in range(rows):
        for sc in range(cols):
            tr, tc = sr + down, sc + right
            if 0 <= tr < rows and 0 <= tc < cols:
                pairs.append((sr * cols + sc, tr * cols + tc))
    return lax.ppermute(piece, ("row", "col"), pairs)


def dense_shifted(piece, down, right):
    rows, cols = piece.shape[-2], piece.shape[-1]
    lanes = 128 if (rows * cols) % 128 == 0 and cols < 128 else cols
    packed = piece.reshape(piece.shape[:-2] + (rows * cols // lanes, lanes))
    return shifted(packed, down, right).reshape(piece.shape)


def halo_sides(x):
    top = dense_shifted(x[-1], 1, 0)
    bottom = dense_shifted(x[0], -1, 0)
    left = dense_shifted(jnp.concatenate([top[-1:], x[:, -1], bottom[-1:]], axis=0), 0, 1)
    right = dense_shifted(jnp.concatenate([top[:1], x[:, 0], bottom[:1]], axis=0), 0, -1)
    return top, bottom, left, right


def with_halo(x):
    top, bottom, left, right = halo_sides(x)
    middle = jnp.concatenate([top[None], x, bottom[None]], axis=0)
    return jnp.concatenate([left[:, None], middle, right[:, None]], axis=1)


def halo_ring(x):
    top, bottom, left, right = halo_sides(x)
    return jnp.concatenate(
        [left[:1], top, right[:1], left[-1:], bottom, right[-1:], left[1:-1], right[1:-1]], axis=0
    )


def ap_kernel(near_ref, slot_ref, a_ref, p_ref, out_ref, dense_ref, acc_ref, *, n_r, n_c):
    tiles, terms = a_ref.shape[0], a_ref.shape[1]

    def one_tile(t, carry):
        acc_ref[...] = jnp.zeros(acc_ref.shape, jnp.float32)
        for k in range(terms):
            j = near_ref[t * terms + k]
            a = a_ref[t, k]
            for q in range(4):
                e = slot_ref[(t * terms + k) * 4 + q]
                keep = jnp.where(e >= 0, 1.0, 0.0).astype(jnp.float32)
                prod = jnp.dot(a, p_ref[j, q], preferred_element_type=jnp.float32)
                acc_ref[jnp.clip(e, 0, 8)] += prod * keep

        ap = acc_ref[...].astype(out_ref.dtype)
        out_ref[t] = ap
        row, col = t // n_c, t % n_c

        @pl.when((row == 0) | (row == n_r - 1) | (col == 0) | (col == n_c - 1))
        def _():
            dense_ref[t] = ap.reshape(dense_ref.shape[1:])

        return carry

    lax.fori_loop(0, tiles, one_tile, 0, unroll=2)


def add_terms(where_ref, target_ref, ap_ref, pt_ref, acc_ref):
    def one_tile(t, carry):
        w = where_ref[t]
        blocks = [ap_ref[t, e].reshape(pt_ref.shape[1:]) for e in range(9)]
        for q in range(4):
            g = target_ref[t * 4 + q]

            @pl.when(g >= 0)
            def _():
                p = pt_ref[w * 4 + q]
                for e in range(9):
                    acc_ref[g + (e // 3) * 5 + e % 3] += lax.dot_general(
                        p, blocks[e], (((0,), (0,)), ((), ())), preferred_element_type=jnp.float32
                    )

        return carry

    lax.fori_loop(0, ap_ref.shape[0], one_tile, 0, unroll=2)


def own_kernel(where_ref, target_ref, ap_ref, pt_ref, acc_ref):
    acc_ref[...] = jnp.zeros(acc_ref.shape, jnp.float32)
    add_terms(where_ref, target_ref, ap_ref, pt_ref, acc_ref)


def coarse_kernel(*refs):
    groups = (len(refs) - 5) // 3
    tables, pick_ref = refs[: 2 * groups], refs[2 * groups]
    blocks = refs[2 * groups + 1 : 3 * groups + 1]
    pt_ref, part_ref, out_ref, acc_ref = refs[-4], refs[-3], refs[-2], refs[-1]
    acc_ref[...] = part_ref[...]
    for i in range(groups):
        add_terms(tables[2 * i], tables[2 * i + 1], blocks[i], pt_ref, acc_ref)
    owned, stencil = out_ref.shape[0], out_ref.shape[1]

    def one_pick(i, carry):
        a = i // stencil
        out_ref[a, i % stencil] = acc_ref[a * stencil + pick_ref[i]].astype(out_ref.dtype)
        return carry

    lax.fori_loop(0, owned * stencil, one_pick, 0)


def ring_of(x):
    return jnp.concatenate([x[0], x[-1], x[1:-1, 0], x[1:-1, -1]], axis=0)


def body(a_blocks, a_cols, p_blocks, p_cols, c_cols):
    n_r, n_c = a_blocks.shape[0], a_blocks.shape[1]
    bs = a_blocks.shape[-1]
    terms = a_blocks.shape[2]
    grid_rows = n_r * lax.axis_size("row")
    grid_cols = n_c * lax.axis_size("col")
    coarse_rows, coarse_cols = grid_rows // 2, grid_cols // 2
    y0 = lax.axis_index("row") * n_r
    x0 = lax.axis_index("col") * n_c
    ys = y0 + jnp.arange(n_r, dtype=jnp.int32)
    xs = x0 + jnp.arange(n_c, dtype=jnp.int32)
    two = jnp.arange(2, dtype=jnp.int32)

    agg_y = mirror((ys - 1)[:, None] // 2 + two, coarse_rows)
    agg_x = mirror((xs - 1)[:, None] // 2 + two, coarse_cols)
    wanted = (agg_y[:, None, :, None] * coarse_cols + agg_x[None, :, None, :]).reshape(n_r, n_c, 4)
    match = p_cols[:, :, None, :] == wanted[:, :, :, None]
    canon = jnp.sum(
        jnp.where(match[..., None, None], p_blocks[:, :, None], jnp.zeros((), p_blocks.dtype)),
        axis=3,
        dtype=p_blocks.dtype,
    )
    p_ext = with_halo(canon)
    ext_r, ext_c = n_r + 2, n_c + 2

    near_y = a_cols // grid_cols
    near_x = a_cols % grid_cols
    near = jnp.clip(near_y - (y0 - 1), 0, ext_r - 1) * ext_c + jnp.clip(near_x - (x0 - 1), 0, ext_c - 1)
    near_agg_y = mirror((near_y - 1)[..., None] // 2 + two, coarse_rows)
    near_agg_x = mirror((near_x - 1)[..., None] // 2 + two, coarse_cols)
    slot_y = near_agg_y - (ys // 2 - 1)[:, None, None, None]
    slot_x = near_agg_x - (xs // 2 - 1)[None, :, None, None]
    slot = (slot_y[..., :, None] * 3 + slot_x[..., None, :]).reshape(n_r, n_c, terms, 4)
    slot = jnp.where((slot >= 0) & (slot < 9), slot, -1)

    ap, ap_dense = pl.pallas_call(
        functools.partial(ap_kernel, n_r=n_r, n_c=n_c),
        out_shape=(
            jax.ShapeDtypeStruct((n_r * n_c, 9, bs, bs), jnp.bfloat16),
            jax.ShapeDtypeStruct((n_r * n_c, 9, bs * bs // 128, 128), jnp.bfloat16),
        ),
        in_specs=[
            pl.BlockSpec(memory_space=pltpu.SMEM),
            pl.BlockSpec(memory_space=pltpu.SMEM),
            pl.BlockSpec(memory_space=pltpu.VMEM),
            pl.BlockSpec(memory_space=pltpu.VMEM),
        ],
        out_specs=(pl.BlockSpec(memory_space=pltpu.VMEM), pl.BlockSpec(memory_space=pltpu.VMEM)),
        scratch_shapes=[pltpu.VMEM((9, bs, bs), jnp.float32)],
    )(
        near.reshape(-1),
        slot.reshape(-1),
        a_blocks.reshape(n_r * n_c, terms, bs, bs),
        p_ext.reshape(ext_r * ext_c, 4, bs, bs),
    )
    ap = ap.reshape(n_r, n_c, 9, bs, bs)
    ap_dense = ap_dense.reshape((n_r, n_c) + ap_dense.shape[1:])

    o_r, o_c = n_r // 2, n_c // 2
    ey = y0 - 1 + jnp.arange(ext_r, dtype=jnp.int32)
    ex = x0 - 1 + jnp.arange(ext_c, dtype=jnp.int32)
    e_agg_y = mirror((ey - 1)[:, None] // 2 + two, coarse_rows)
    e_agg_x = mirror((ex - 1)[:, None] // 2 + two, coarse_cols)
    own_y = e_agg_y - y0 // 2
    own_x = e_agg_x - x0 // 2
    off_y = (ey // 2 - 1)[:, None] - e_agg_y + 2
    off_x = (ex // 2 - 1)[:, None] - e_agg_x + 2
    ok_y = (ey >= 0)[:, None] & (ey < grid_rows)[:, None] & (own_y >= 0) & (own_y < o_r) & (off_y >= 0) & (off_y <= 2)
    ok_x = (ex >= 0)[:, None] & (ex < grid_cols)[:, None] & (own_x >= 0) & (own_x < o_c) & (off_x >= 0) & (off_x <= 2)
    target = (own_y[:, None, :, None] * o_c + own_x[None, :, None, :]) * 25 + (
        off_y[:, None, :, None] * 5 + off_x[None, :, None, :]
    )
    target = jnp.where(ok_y[:, None, :, None] & ok_x[None, :, None, :], target, -1).reshape(ext_r, ext_c, 4)
    place = jnp.arange(ext_r * ext_c, dtype=jnp.int32).reshape(ext_r, ext_c)

    cy = ys[0] // 2 + jnp.arange(o_r, dtype=jnp.int32)
    cx = xs[0] // 2 + jnp.arange(o_c, dtype=jnp.int32)
    pick = (c_cols // coarse_cols - cy[:, None, None] + 2) * 5 + (c_cols % coarse_cols - cx[None, :, None] + 2)
    pick = jnp.clip(pick, 0, 24).reshape(-1)

    p_t = p_ext.reshape(ext_r * ext_c * 4, bs, bs)
    stencil = c_cols.shape[-1]
    smem = pl.BlockSpec(memory_space=pltpu.SMEM)
    vmem = pl.BlockSpec(memory_space=pltpu.VMEM)
    acc_shape = (o_r * o_c * 25, bs, bs)
    part = pl.pallas_call(
        own_kernel,
        out_shape=jax.ShapeDtypeStruct(acc_shape, jnp.float32),
        in_specs=[smem, smem, vmem, vmem],
        out_specs=vmem,
        cost_estimate=pl.CostEstimate(
            flops=2 * bs * bs * bs * 9 * n_r * n_c * 4, bytes_accessed=6 * 1024 * 1024, transcendentals=0
        ),
    )(place[1:-1, 1:-1].reshape(-1), target[1:-1, 1:-1].reshape(-1), ap.reshape(n_r * n_c, 9, bs, bs), p_t)
    top, bottom, left, right = halo_sides(ap_dense)
    parts = [
        (place[0, 1:-1], target[0, 1:-1], top),
        (place[-1, 1:-1], target[-1, 1:-1], bottom),
        (place[:, 0], target[:, 0], left),
        (place[:, -1], target[:, -1], right),
    ]
    out = pl.pallas_call(
        coarse_kernel,
        out_shape=jax.ShapeDtypeStruct((o_r * o_c, stencil, bs, bs), jnp.bfloat16),
        in_specs=[smem] * (2 * len(parts) + 1) + [vmem] * (len(parts) + 2),
        out_specs=vmem,
        scratch_shapes=[pltpu.VMEM(acc_shape, jnp.float32)],
    )(
        *[t for w, g, _ in parts for t in (w.reshape(-1), g.reshape(-1))],
        pick,
        *[b for _, _, b in parts],
        p_t,
        part,
    )
    return out.reshape(o_r, o_c, stencil, bs, bs)


def solution(mesh):
    return jax.shard_map(
        body,
        mesh=mesh,
        in_specs=(
            P("row", "col", None, None, None),
            P("row", "col", None),
            P("row", "col", None, None, None),
            P("row", "col", None),
            P("row", "col", None),
        ),
        out_specs=P("row", "col", None, None, None),
        check_vma=False,
    )
```

```python
import functools

import jax
import jax.numpy as jnp
from jax import lax
from jax.experimental import pallas as pl
from jax.experimental.pallas import tpu as pltpu
from jax.sharding import PartitionSpec as P


def mirror(values, limit):
    values = jnp.where(values < 0, -values, values)
    return jnp.where(values >= limit, 2 * (limit - 1) - values, values)


def shifted(piece, down, right):
    rows, cols = lax.axis_size("row"), lax.axis_size("col")
    if right == 0:
        pairs = [(s, s + down) for s in range(rows) if 0 <= s + down < rows]
        return lax.ppermute(piece, "row", pairs)
    if down == 0:
        pairs = [(s, s + right) for s in range(cols) if 0 <= s + right < cols]
        return lax.ppermute(piece, "col", pairs)
    pairs = []
    for sr in range(rows):
        for sc in range(cols):
            tr, tc = sr + down, sc + right
            if 0 <= tr < rows and 0 <= tc < cols:
                pairs.append((sr * cols + sc, tr * cols + tc))
    return lax.ppermute(piece, ("row", "col"), pairs)


def dense_shifted(piece, down, right):
    rows, cols = piece.shape[-2], piece.shape[-1]
    lanes = 128 if (rows * cols) % 128 == 0 and cols < 128 else cols
    packed = piece.reshape(piece.shape[:-2] + (rows * cols // lanes, lanes))
    return shifted(packed, down, right).reshape(piece.shape)


def halo_sides(x):
    top = dense_shifted(x[-1], 1, 0)
    bottom = dense_shifted(x[0], -1, 0)
    left = dense_shifted(jnp.concatenate([top[-1:], x[:, -1], bottom[-1:]], axis=0), 0, 1)
    right = dense_shifted(jnp.concatenate([top[:1], x[:, 0], bottom[:1]], axis=0), 0, -1)
    return top, bottom, left, right


def with_halo(x):
    top, bottom, left, right = halo_sides(x)
    middle = jnp.concatenate([top[None], x, bottom[None]], axis=0)
    return jnp.concatenate([left[:, None], middle, right[:, None]], axis=1)


def halo_ring(x):
    top, bottom, left, right = halo_sides(x)
    return jnp.concatenate(
        [left[:1], top, right[:1], left[-1:], bottom, right[-1:], left[1:-1], right[1:-1]], axis=0
    )


def ap_kernel(near_ref, slot_ref, a_ref, p_ref, out_ref, dense_ref, acc_ref, *, n_r, n_c):
    tiles, terms = a_ref.shape[0], a_ref.shape[1]

    def one_tile(t, carry):
        acc_ref[...] = jnp.zeros(acc_ref.shape, jnp.float32)
        for k in range(terms):
            j = near_ref[t * terms + k]
            a = a_ref[t, k]
            for q in range(4):
                e = slot_ref[(t * terms + k) * 4 + q]
                keep = jnp.where(e >= 0, 1.0, 0.0).astype(jnp.float32)
                prod = jnp.dot(a, p_ref[j, q], preferred_element_type=jnp.float32)
                acc_ref[jnp.clip(e, 0, 8)] += prod * keep

        ap = acc_ref[...].astype(out_ref.dtype)
        out_ref[t] = ap
        row, col = t // n_c, t % n_c

        @pl.when((row == 0) | (row == n_r - 1) | (col == 0) | (col == n_c - 1))
        def _():
            dense_ref[t] = ap.reshape(dense_ref.shape[1:])

        return carry

    lax.fori_loop(0, tiles, one_tile, 0)


def add_terms(where_ref, target_ref, ap_ref, pt_ref, acc_ref, transposed=True):
    def one_tile(t, carry):
        w = where_ref[t]
        blocks = [ap_ref[t, e].reshape(pt_ref.shape[1:]) for e in range(9)]
        for q in range(4):
            g = target_ref[t * 4 + q]

            @pl.when(g >= 0)
            def _():
                p = pt_ref[w * 4 + q]
                pair = (((0 if transposed else 1,), (0,)), ((), ()))
                for e in range(9):
                    acc_ref[g + (e // 3) * 5 + e % 3] += lax.dot_general(
                        p, blocks[e], pair, preferred_element_type=jnp.float32
                    )

        return carry

    lax.fori_loop(0, ap_ref.shape[0], one_tile, 0)


def own_kernel(where_ref, target_ref, ap_ref, pt_ref, acc_ref):
    acc_ref[...] = jnp.zeros(acc_ref.shape, jnp.float32)
    add_terms(where_ref, target_ref, ap_ref, pt_ref, acc_ref, transposed=False)


def coarse_kernel(*refs):
    groups = (len(refs) - 5) // 3
    tables, pick_ref = refs[: 2 * groups], refs[2 * groups]
    blocks = refs[2 * groups + 1 : 3 * groups + 1]
    pt_ref, part_ref, out_ref, acc_ref = refs[-4], refs[-3], refs[-2], refs[-1]
    acc_ref[...] = part_ref[...]
    for i in range(groups):
        add_terms(tables[2 * i], tables[2 * i + 1], blocks[i], pt_ref, acc_ref)
    owned, stencil = out_ref.shape[0], out_ref.shape[1]

    def one_pick(i, carry):
        a = i // stencil
        out_ref[a, i % stencil] = acc_ref[a * stencil + pick_ref[i]].astype(out_ref.dtype)
        return carry

    lax.fori_loop(0, owned * stencil, one_pick, 0)


def ring_of(x):
    return jnp.concatenate([x[0], x[-1], x[1:-1, 0], x[1:-1, -1]], axis=0)


def body(a_blocks, a_cols, p_blocks, p_cols, c_cols):
    n_r, n_c = a_blocks.shape[0], a_blocks.shape[1]
    bs = a_blocks.shape[-1]
    terms = a_blocks.shape[2]
    grid_rows = n_r * lax.axis_size("row")
    grid_cols = n_c * lax.axis_size("col")
    coarse_rows, coarse_cols = grid_rows // 2, grid_cols // 2
    y0 = lax.axis_index("row") * n_r
    x0 = lax.axis_index("col") * n_c
    ys = y0 + jnp.arange(n_r, dtype=jnp.int32)
    xs = x0 + jnp.arange(n_c, dtype=jnp.int32)
    two = jnp.arange(2, dtype=jnp.int32)

    agg_y = mirror((ys - 1)[:, None] // 2 + two, coarse_rows)
    agg_x = mirror((xs - 1)[:, None] // 2 + two, coarse_cols)
    wanted = (agg_y[:, None, :, None] * coarse_cols + agg_x[None, :, None, :]).reshape(n_r, n_c, 4)
    match = p_cols[:, :, None, :] == wanted[:, :, :, None]
    canon = jnp.sum(
        jnp.where(match[..., None, None], p_blocks[:, :, None], jnp.zeros((), p_blocks.dtype)),
        axis=3,
        dtype=p_blocks.dtype,
    )
    p_ext = with_halo(canon)
    ext_r, ext_c = n_r + 2, n_c + 2

    near_y = a_cols // grid_cols
    near_x = a_cols % grid_cols
    near = jnp.clip(near_y - (y0 - 1), 0, ext_r - 1) * ext_c + jnp.clip(near_x - (x0 - 1), 0, ext_c - 1)
    near_agg_y = mirror((near_y - 1)[..., None] // 2 + two, coarse_rows)
    near_agg_x = mirror((near_x - 1)[..., None] // 2 + two, coarse_cols)
    slot_y = near_agg_y - (ys // 2 - 1)[:, None, None, None]
    slot_x = near_agg_x - (xs // 2 - 1)[None, :, None, None]
    slot = (slot_y[..., :, None] * 3 + slot_x[..., None, :]).reshape(n_r, n_c, terms, 4)
    slot = jnp.where((slot >= 0) & (slot < 9), slot, -1)

    ap, ap_dense = pl.pallas_call(
        functools.partial(ap_kernel, n_r=n_r, n_c=n_c),
        out_shape=(
            jax.ShapeDtypeStruct((n_r * n_c, 9, bs, bs), jnp.bfloat16),
            jax.ShapeDtypeStruct((n_r * n_c, 9, bs * bs // 128, 128), jnp.bfloat16),
        ),
        in_specs=[
            pl.BlockSpec(memory_space=pltpu.SMEM),
            pl.BlockSpec(memory_space=pltpu.SMEM),
            pl.BlockSpec(memory_space=pltpu.VMEM),
            pl.BlockSpec(memory_space=pltpu.VMEM),
        ],
        out_specs=(pl.BlockSpec(memory_space=pltpu.VMEM), pl.BlockSpec(memory_space=pltpu.VMEM)),
        scratch_shapes=[pltpu.VMEM((9, bs, bs), jnp.float32)],
    )(
        near.reshape(-1),
        slot.reshape(-1),
        a_blocks.reshape(n_r * n_c, terms, bs, bs),
        p_ext.reshape(ext_r * ext_c, 4, bs, bs),
    )
    ap = ap.reshape(n_r, n_c, 9, bs, bs)
    ap_dense = ap_dense.reshape((n_r, n_c) + ap_dense.shape[1:])

    o_r, o_c = n_r // 2, n_c // 2
    ey = y0 - 1 + jnp.arange(ext_r, dtype=jnp.int32)
    ex = x0 - 1 + jnp.arange(ext_c, dtype=jnp.int32)
    e_agg_y = mirror((ey - 1)[:, None] // 2 + two, coarse_rows)
    e_agg_x = mirror((ex - 1)[:, None] // 2 + two, coarse_cols)
    own_y = e_agg_y - y0 // 2
    own_x = e_agg_x - x0 // 2
    off_y = (ey // 2 - 1)[:, None] - e_agg_y + 2
    off_x = (ex // 2 - 1)[:, None] - e_agg_x + 2
    ok_y = (ey >= 0)[:, None] & (ey < grid_rows)[:, None] & (own_y >= 0) & (own_y < o_r) & (off_y >= 0) & (off_y <= 2)
    ok_x = (ex >= 0)[:, None] & (ex < grid_cols)[:, None] & (own_x >= 0) & (own_x < o_c) & (off_x >= 0) & (off_x <= 2)
    target = (own_y[:, None, :, None] * o_c + own_x[None, :, None, :]) * 25 + (
        off_y[:, None, :, None] * 5 + off_x[None, :, None, :]
    )
    target = jnp.where(ok_y[:, None, :, None] & ok_x[None, :, None, :], target, -1).reshape(ext_r, ext_c, 4)
    place = jnp.arange(ext_r * ext_c, dtype=jnp.int32).reshape(ext_r, ext_c)

    cy = ys[0] // 2 + jnp.arange(o_r, dtype=jnp.int32)
    cx = xs[0] // 2 + jnp.arange(o_c, dtype=jnp.int32)
    pick = (c_cols // coarse_cols - cy[:, None, None] + 2) * 5 + (c_cols % coarse_cols - cx[None, :, None] + 2)
    pick = jnp.clip(pick, 0, 24).reshape(-1)

    p_t = p_ext.reshape(ext_r * ext_c * 4, bs, bs)
    stencil = c_cols.shape[-1]
    smem = pl.BlockSpec(memory_space=pltpu.SMEM)
    vmem = pl.BlockSpec(memory_space=pltpu.VMEM)
    acc_shape = (o_r * o_c * 25, bs, bs)
    part = pl.pallas_call(
        own_kernel,
        out_shape=jax.ShapeDtypeStruct(acc_shape, jnp.float32),
        in_specs=[smem, smem, vmem, vmem],
        out_specs=vmem,
        cost_estimate=pl.CostEstimate(
            flops=2 * bs * bs * bs * 9 * n_r * n_c * 4, bytes_accessed=6 * 1024 * 1024, transcendentals=0
        ),
    )(
        jnp.arange(n_r * n_c, dtype=jnp.int32),
        target[1:-1, 1:-1].reshape(-1),
        ap.reshape(n_r * n_c, 9, bs, bs),
        jnp.swapaxes(canon, -1, -2).reshape(n_r * n_c * 4, bs, bs),
    )
    top, bottom, left, right = halo_sides(ap_dense)
    parts = [
        (place[0, 1:-1], target[0, 1:-1], top),
        (place[-1, 1:-1], target[-1, 1:-1], bottom),
        (place[:, 0], target[:, 0], left),
        (place[:, -1], target[:, -1], right),
    ]
    out = pl.pallas_call(
        coarse_kernel,
        out_shape=jax.ShapeDtypeStruct((o_r * o_c, stencil, bs, bs), jnp.bfloat16),
        in_specs=[smem] * (2 * len(parts) + 1) + [vmem] * (len(parts) + 2),
        out_specs=vmem,
        scratch_shapes=[pltpu.VMEM(acc_shape, jnp.float32)],
    )(
        *[t for w, g, _ in parts for t in (w.reshape(-1), g.reshape(-1))],
        pick,
        *[b for _, _, b in parts],
        p_t,
        part,
    )
    return out.reshape(o_r, o_c, stencil, bs, bs)


def solution(mesh):
    return jax.shard_map(
        body,
        mesh=mesh,
        in_specs=(
            P("row", "col", None, None, None),
            P("row", "col", None),
            P("row", "col", None, None, None),
            P("row", "col", None),
            P("row", "col", None),
        ),
        out_specs=P("row", "col", None, None, None),
        check_vma=False,
    )
```

```python
import functools

import jax
import jax.numpy as jnp
from jax import lax
from jax.experimental import pallas as pl
from jax.experimental.pallas import tpu as pltpu
from jax.sharding import PartitionSpec as P


def mirror(values, limit):
    values = jnp.where(values < 0, -values, values)
    return jnp.where(values >= limit, 2 * (limit - 1) - values, values)


def shifted(piece, down, right):
    rows, cols = lax.axis_size("row"), lax.axis_size("col")
    if right == 0:
        pairs = [(s, s + down) for s in range(rows) if 0 <= s + down < rows]
        return lax.ppermute(piece, "row", pairs)
    if down == 0:
        pairs = [(s, s + right) for s in range(cols) if 0 <= s + right < cols]
        return lax.ppermute(piece, "col", pairs)
    pairs = []
    for sr in range(rows):
        for sc in range(cols):
            tr, tc = sr + down, sc + right
            if 0 <= tr < rows and 0 <= tc < cols:
                pairs.append((sr * cols + sc, tr * cols + tc))
    return lax.ppermute(piece, ("row", "col"), pairs)


def dense_shifted(piece, down, right):
    rows, cols = piece.shape[-2], piece.shape[-1]
    lanes = 128 if (rows * cols) % 128 == 0 and cols < 128 else cols
    packed = piece.reshape(piece.shape[:-2] + (rows * cols // lanes, lanes))
    return shifted(packed, down, right).reshape(piece.shape)


def halo_sides(x):
    top = dense_shifted(x[-1], 1, 0)
    bottom = dense_shifted(x[0], -1, 0)
    left = dense_shifted(jnp.concatenate([top[-1:], x[:, -1], bottom[-1:]], axis=0), 0, 1)
    right = dense_shifted(jnp.concatenate([top[:1], x[:, 0], bottom[:1]], axis=0), 0, -1)
    return top, bottom, left, right


def with_halo(x):
    top, bottom, left, right = halo_sides(x)
    middle = jnp.concatenate([top[None], x, bottom[None]], axis=0)
    return jnp.concatenate([left[:, None], middle, right[:, None]], axis=1)


def halo_ring(x):
    top, bottom, left, right = halo_sides(x)
    return jnp.concatenate(
        [left[:1], top, right[:1], left[-1:], bottom, right[-1:], left[1:-1], right[1:-1]], axis=0
    )


def ap_kernel(near_ref, slot_ref, a_ref, p_ref, out_ref, dense_ref, acc_ref, *, n_r, n_c):
    tiles, terms = a_ref.shape[0], a_ref.shape[1]

    def one_tile(t, carry):
        acc_ref[...] = jnp.zeros(acc_ref.shape, jnp.float32)
        for k in range(terms):
            j = near_ref[t * terms + k]
            a = a_ref[t, k]
            for q in range(4):
                e = slot_ref[(t * terms + k) * 4 + q]
                keep = jnp.where(e >= 0, 1.0, 0.0).astype(jnp.float32)
                prod = jnp.dot(a, p_ref[j, q], preferred_element_type=jnp.float32)
                acc_ref[jnp.clip(e, 0, 8)] += prod * keep

        ap = acc_ref[...].astype(out_ref.dtype)
        out_ref[t] = ap
        row, col = t // n_c, t % n_c

        @pl.when((row == 0) | (row == n_r - 1) | (col == 0) | (col == n_c - 1))
        def _():
            dense_ref[t] = ap.reshape(dense_ref.shape[1:])

        return carry

    lax.fori_loop(0, tiles, one_tile, 0)


def add_terms(where_ref, target_ref, ap_ref, pt_ref, acc_ref):
    def one_tile(t, carry):
        w = where_ref[t]
        dense = ap_ref.shape[-2:] != pt_ref.shape[1:]
        blocks = [ap_ref[t, e].reshape(pt_ref.shape[1:]) for e in range(9)] if dense else None
        for q in range(4):
            g = target_ref[t * 4 + q]

            @pl.when(g >= 0)
            def _():
                p = pt_ref[w * 4 + q]
                for e in range(9):
                    block = blocks[e] if dense else ap_ref[t, e]
                    acc_ref[g + (e // 3) * 5 + e % 3] += lax.dot_general(
                        p, block, (((0,), (0,)), ((), ())), preferred_element_type=jnp.float32
                    )

        return carry

    lax.fori_loop(0, ap_ref.shape[0], one_tile, 0)


def own_kernel(where_ref, target_ref, ap_ref, pt_ref, acc_ref):
    acc_ref[...] = jnp.zeros(acc_ref.shape, jnp.float32)
    add_terms(where_ref, target_ref, ap_ref, pt_ref, acc_ref)


def coarse_kernel(*refs):
    groups = (len(refs) - 5) // 3
    tables, pick_ref = refs[: 2 * groups], refs[2 * groups]
    blocks = refs[2 * groups + 1 : 3 * groups + 1]
    pt_ref, part_ref, out_ref, acc_ref = refs[-4], refs[-3], refs[-2], refs[-1]
    acc_ref[...] = part_ref[...]
    for i in range(groups):
        add_terms(tables[2 * i], tables[2 * i + 1], blocks[i], pt_ref, acc_ref)
    owned, stencil = out_ref.shape[0], out_ref.shape[1]

    def one_pick(i, carry):
        a = i // stencil
        out_ref[a, i % stencil] = acc_ref[a * stencil + pick_ref[i]].astype(out_ref.dtype)
        return carry

    lax.fori_loop(0, owned * stencil, one_pick, 0)


def ring_of(x):
    return jnp.concatenate([x[0], x[-1], x[1:-1, 0], x[1:-1, -1]], axis=0)


def body(a_blocks, a_cols, p_blocks, p_cols, c_cols):
    n_r, n_c = a_blocks.shape[0], a_blocks.shape[1]
    bs = a_blocks.shape[-1]
    terms = a_blocks.shape[2]
    grid_rows = n_r * lax.axis_size("row")
    grid_cols = n_c * lax.axis_size("col")
    coarse_rows, coarse_cols = grid_rows // 2, grid_cols // 2
    y0 = lax.axis_index("row") * n_r
    x0 = lax.axis_index("col") * n_c
    ys = y0 + jnp.arange(n_r, dtype=jnp.int32)
    xs = x0 + jnp.arange(n_c, dtype=jnp.int32)
    two = jnp.arange(2, dtype=jnp.int32)

    agg_y = mirror((ys - 1)[:, None] // 2 + two, coarse_rows)
    agg_x = mirror((xs - 1)[:, None] // 2 + two, coarse_cols)
    wanted = (agg_y[:, None, :, None] * coarse_cols + agg_x[None, :, None, :]).reshape(n_r, n_c, 4)
    match = p_cols[:, :, None, :] == wanted[:, :, :, None]
    canon = jnp.sum(
        jnp.where(match[..., None, None], p_blocks[:, :, None], jnp.zeros((), p_blocks.dtype)),
        axis=3,
        dtype=p_blocks.dtype,
    )
    p_ext = with_halo(canon)
    ext_r, ext_c = n_r + 2, n_c + 2

    near_y = a_cols // grid_cols
    near_x = a_cols % grid_cols
    near = jnp.clip(near_y - (y0 - 1), 0, ext_r - 1) * ext_c + jnp.clip(near_x - (x0 - 1), 0, ext_c - 1)
    near_agg_y = mirror((near_y - 1)[..., None] // 2 + two, coarse_rows)
    near_agg_x = mirror((near_x - 1)[..., None] // 2 + two, coarse_cols)
    slot_y = near_agg_y - (ys // 2 - 1)[:, None, None, None]
    slot_x = near_agg_x - (xs // 2 - 1)[None, :, None, None]
    slot = (slot_y[..., :, None] * 3 + slot_x[..., None, :]).reshape(n_r, n_c, terms, 4)
    slot = jnp.where((slot >= 0) & (slot < 9), slot, -1)

    ap, ap_dense = pl.pallas_call(
        functools.partial(ap_kernel, n_r=n_r, n_c=n_c),
        out_shape=(
            jax.ShapeDtypeStruct((n_r * n_c, 9, bs, bs), jnp.bfloat16),
            jax.ShapeDtypeStruct((n_r * n_c, 9, bs * bs // 128, 128), jnp.bfloat16),
        ),
        in_specs=[
            pl.BlockSpec(memory_space=pltpu.SMEM),
            pl.BlockSpec(memory_space=pltpu.SMEM),
            pl.BlockSpec(memory_space=pltpu.VMEM),
            pl.BlockSpec(memory_space=pltpu.VMEM),
        ],
        out_specs=(pl.BlockSpec(memory_space=pltpu.VMEM), pl.BlockSpec(memory_space=pltpu.VMEM)),
        scratch_shapes=[pltpu.VMEM((9, bs, bs), jnp.float32)],
    )(
        near.reshape(-1),
        slot.reshape(-1),
        a_blocks.reshape(n_r * n_c, terms, bs, bs),
        p_ext.reshape(ext_r * ext_c, 4, bs, bs),
    )
    ap = ap.reshape(n_r, n_c, 9, bs, bs)
    ap_dense = ap_dense.reshape((n_r, n_c) + ap_dense.shape[1:])

    o_r, o_c = n_r // 2, n_c // 2
    ey = y0 - 1 + jnp.arange(ext_r, dtype=jnp.int32)
    ex = x0 - 1 + jnp.arange(ext_c, dtype=jnp.int32)
    e_agg_y = mirror((ey - 1)[:, None] // 2 + two, coarse_rows)
    e_agg_x = mirror((ex - 1)[:, None] // 2 + two, coarse_cols)
    own_y = e_agg_y - y0 // 2
    own_x = e_agg_x - x0 // 2
    off_y = (ey // 2 - 1)[:, None] - e_agg_y + 2
    off_x = (ex // 2 - 1)[:, None] - e_agg_x + 2
    ok_y = (ey >= 0)[:, None] & (ey < grid_rows)[:, None] & (own_y >= 0) & (own_y < o_r) & (off_y >= 0) & (off_y <= 2)
    ok_x = (ex >= 0)[:, None] & (ex < grid_cols)[:, None] & (own_x >= 0) & (own_x < o_c) & (off_x >= 0) & (off_x <= 2)
    target = (own_y[:, None, :, None] * o_c + own_x[None, :, None, :]) * 25 + (
        off_y[:, None, :, None] * 5 + off_x[None, :, None, :]
    )
    target = jnp.where(ok_y[:, None, :, None] & ok_x[None, :, None, :], target, -1).reshape(ext_r, ext_c, 4)
    place = jnp.arange(ext_r * ext_c, dtype=jnp.int32).reshape(ext_r, ext_c)

    cy = ys[0] // 2 + jnp.arange(o_r, dtype=jnp.int32)
    cx = xs[0] // 2 + jnp.arange(o_c, dtype=jnp.int32)
    pick = (c_cols // coarse_cols - cy[:, None, None] + 2) * 5 + (c_cols % coarse_cols - cx[None, :, None] + 2)
    pick = jnp.clip(pick, 0, 24).reshape(-1)

    p_t = p_ext.reshape(ext_r * ext_c * 4, bs, bs)
    stencil = c_cols.shape[-1]
    smem = pl.BlockSpec(memory_space=pltpu.SMEM)
    vmem = pl.BlockSpec(memory_space=pltpu.VMEM)
    acc_shape = (o_r * o_c * 25, bs, bs)
    part = pl.pallas_call(
        own_kernel,
        out_shape=jax.ShapeDtypeStruct(acc_shape, jnp.float32),
        in_specs=[smem, smem, vmem, vmem],
        out_specs=vmem,
        cost_estimate=pl.CostEstimate(
            flops=2 * bs * bs * bs * 9 * n_r * n_c * 4, bytes_accessed=6 * 1024 * 1024, transcendentals=0
        ),
    )(place[1:-1, 1:-1].reshape(-1), target[1:-1, 1:-1].reshape(-1), ap.reshape(n_r * n_c, 9, bs, bs), p_t)
    top, bottom, left, right = halo_sides(ap_dense)
    parts = [
        (place[0, 1:-1], target[0, 1:-1], top),
        (place[-1, 1:-1], target[-1, 1:-1], bottom),
        (place[:, 0], target[:, 0], left),
        (place[:, -1], target[:, -1], right),
    ]
    out = pl.pallas_call(
        coarse_kernel,
        out_shape=jax.ShapeDtypeStruct((o_r * o_c, stencil, bs, bs), jnp.bfloat16),
        in_specs=[smem] * (2 * len(parts) + 1) + [vmem] * (len(parts) + 2),
        out_specs=vmem,
        scratch_shapes=[pltpu.VMEM(acc_shape, jnp.float32)],
    )(
        *[t for w, g, _ in parts for t in (w.reshape(-1), g.reshape(-1))],
        pick,
        *[b for _, _, b in parts],
        p_t,
        part,
    )
    return out.reshape(o_r, o_c, stencil, bs, bs)


def solution(mesh):
    return jax.shard_map(
        body,
        mesh=mesh,
        in_specs=(
            P("row", "col", None, None, None),
            P("row", "col", None),
            P("row", "col", None, None, None),
            P("row", "col", None),
            P("row", "col", None),
        ),
        out_specs=P("row", "col", None, None, None),
        check_vma=False,
    )
```

```python
import functools

import jax
import jax.numpy as jnp
from jax import lax
from jax.experimental import pallas as pl
from jax.experimental.pallas import tpu as pltpu
from jax.sharding import PartitionSpec as P


def mirror(values, limit):
    values = jnp.where(values < 0, -values, values)
    return jnp.where(values >= limit, 2 * (limit - 1) - values, values)


def shifted(piece, down, right):
    rows, cols = lax.axis_size("row"), lax.axis_size("col")
    if right == 0:
        pairs = [(s, s + down) for s in range(rows) if 0 <= s + down < rows]
        return lax.ppermute(piece, "row", pairs)
    if down == 0:
        pairs = [(s, s + right) for s in range(cols) if 0 <= s + right < cols]
        return lax.ppermute(piece, "col", pairs)
    pairs = []
    for sr in range(rows):
        for sc in range(cols):
            tr, tc = sr + down, sc + right
            if 0 <= tr < rows and 0 <= tc < cols:
                pairs.append((sr * cols + sc, tr * cols + tc))
    return lax.ppermute(piece, ("row", "col"), pairs)


def dense_shifted(piece, down, right):
    rows, cols = piece.shape[-2], piece.shape[-1]
    lanes = 128 if (rows * cols) % 128 == 0 and cols < 128 else cols
    packed = piece.reshape(piece.shape[:-2] + (rows * cols // lanes, lanes))
    return shifted(packed, down, right).reshape(piece.shape)


def halo_sides(x):
    top = dense_shifted(x[-1], 1, 0)
    bottom = dense_shifted(x[0], -1, 0)
    left = dense_shifted(jnp.concatenate([top[-1:], x[:, -1], bottom[-1:]], axis=0), 0, 1)
    right = dense_shifted(jnp.concatenate([top[:1], x[:, 0], bottom[:1]], axis=0), 0, -1)
    return top, bottom, left, right


def with_halo(x):
    top, bottom, left, right = halo_sides(x)
    middle = jnp.concatenate([top[None], x, bottom[None]], axis=0)
    return jnp.concatenate([left[:, None], middle, right[:, None]], axis=1)


def halo_ring(x):
    top, bottom, left, right = halo_sides(x)
    return jnp.concatenate(
        [left[:1], top, right[:1], left[-1:], bottom, right[-1:], left[1:-1], right[1:-1]], axis=0
    )


def ap_kernel(near_ref, slot_ref, a_ref, p_ref, out_ref, dense_ref, acc_ref, *, n_r, n_c):
    tiles, terms = a_ref.shape[0], a_ref.shape[1]

    def one_tile(t, carry):
        acc_ref[...] = jnp.zeros(acc_ref.shape, jnp.float32)
        for k in range(terms):
            j = near_ref[t * terms + k]
            a = a_ref[t, k]
            for q in range(4):
                e = slot_ref[(t * terms + k) * 4 + q]
                keep = jnp.where(e >= 0, 1.0, 0.0).astype(jnp.float32)
                prod = jnp.dot(a, p_ref[j, q], preferred_element_type=jnp.float32)
                acc_ref[jnp.clip(e, 0, 8)] += prod * keep

        ap = acc_ref[...].astype(out_ref.dtype)
        out_ref[t] = ap
        row, col = t // n_c, t % n_c

        @pl.when((row == 0) | (row == n_r - 1) | (col == 0) | (col == n_c - 1))
        def _():
            dense_ref[t] = ap.reshape(dense_ref.shape[1:])

        return carry

    lax.fori_loop(0, tiles, one_tile, 0)


def add_terms(where_ref, target_ref, ap_ref, pt_ref, acc_ref):
    def one_tile(t, carry):
        w = where_ref[t]
        for q in range(4):
            g = target_ref[t * 4 + q]

            @pl.when(g >= 0)
            def _():
                p = pt_ref[w * 4 + q]
                for e in range(9):
                    block = ap_ref[t, e].reshape(p.shape)
                    acc_ref[g + (e // 3) * 5 + e % 3] += lax.dot_general(
                        p, block, (((0,), (0,)), ((), ())), preferred_element_type=jnp.float32
                    )

        return carry

    lax.fori_loop(0, ap_ref.shape[0], one_tile, 0)


def own_kernel(where_ref, target_ref, ap_ref, pt_ref, acc_ref):
    acc_ref[...] = jnp.zeros(acc_ref.shape, jnp.float32)
    add_terms(where_ref, target_ref, ap_ref, pt_ref, acc_ref)


def coarse_kernel(*refs):
    groups = (len(refs) - 5) // 3
    tables, pick_ref = refs[: 2 * groups], refs[2 * groups]
    blocks = refs[2 * groups + 1 : 3 * groups + 1]
    pt_ref, part_ref, out_ref, acc_ref = refs[-4], refs[-3], refs[-2], refs[-1]
    acc_ref[...] = part_ref[...]
    for i in range(groups):
        add_terms(tables[2 * i], tables[2 * i + 1], blocks[i], pt_ref, acc_ref)
    owned, stencil = out_ref.shape[0], out_ref.shape[1]

    def one_pick(i, carry):
        a = i // stencil
        out_ref[a, i % stencil] = acc_ref[a * stencil + pick_ref[i]].astype(out_ref.dtype)
        return carry

    lax.fori_loop(0, owned * stencil, one_pick, 0)


def ring_of(x):
    return jnp.concatenate([x[0], x[-1], x[1:-1, 0], x[1:-1, -1]], axis=0)


def body(a_blocks, a_cols, p_blocks, p_cols, c_cols):
    n_r, n_c = a_blocks.shape[0], a_blocks.shape[1]
    bs = a_blocks.shape[-1]
    terms = a_blocks.shape[2]
    grid_rows = n_r * lax.axis_size("row")
    grid_cols = n_c * lax.axis_size("col")
    coarse_rows, coarse_cols = grid_rows // 2, grid_cols // 2
    y0 = lax.axis_index("row") * n_r
    x0 = lax.axis_index("col") * n_c
    ys = y0 + jnp.arange(n_r, dtype=jnp.int32)
    xs = x0 + jnp.arange(n_c, dtype=jnp.int32)
    two = jnp.arange(2, dtype=jnp.int32)

    agg_y = mirror((ys - 1)[:, None] // 2 + two, coarse_rows)
    agg_x = mirror((xs - 1)[:, None] // 2 + two, coarse_cols)
    wanted = (agg_y[:, None, :, None] * coarse_cols + agg_x[None, :, None, :]).reshape(n_r, n_c, 4)
    match = p_cols[:, :, None, :] == wanted[:, :, :, None]
    canon = jnp.sum(
        jnp.where(match[..., None, None], p_blocks[:, :, None], jnp.zeros((), p_blocks.dtype)),
        axis=3,
        dtype=p_blocks.dtype,
    )
    p_ext = with_halo(canon)
    ext_r, ext_c = n_r + 2, n_c + 2

    near_y = a_cols // grid_cols
    near_x = a_cols % grid_cols
    near = jnp.clip(near_y - (y0 - 1), 0, ext_r - 1) * ext_c + jnp.clip(near_x - (x0 - 1), 0, ext_c - 1)
    near_agg_y = mirror((near_y - 1)[..., None] // 2 + two, coarse_rows)
    near_agg_x = mirror((near_x - 1)[..., None] // 2 + two, coarse_cols)
    slot_y = near_agg_y - (ys // 2 - 1)[:, None, None, None]
    slot_x = near_agg_x - (xs // 2 - 1)[None, :, None, None]
    slot = (slot_y[..., :, None] * 3 + slot_x[..., None, :]).reshape(n_r, n_c, terms, 4)
    slot = jnp.where((slot >= 0) & (slot < 9), slot, -1)

    ap, ap_dense = pl.pallas_call(
        functools.partial(ap_kernel, n_r=n_r, n_c=n_c),
        out_shape=(
            jax.ShapeDtypeStruct((n_r * n_c, 9, bs, bs), jnp.bfloat16),
            jax.ShapeDtypeStruct((n_r * n_c, 9, bs * bs // 128, 128), jnp.bfloat16),
        ),
        in_specs=[
            pl.BlockSpec(memory_space=pltpu.SMEM),
            pl.BlockSpec(memory_space=pltpu.SMEM),
            pl.BlockSpec(memory_space=pltpu.VMEM),
            pl.BlockSpec(memory_space=pltpu.VMEM),
        ],
        out_specs=(pl.BlockSpec(memory_space=pltpu.VMEM), pl.BlockSpec(memory_space=pltpu.VMEM)),
        scratch_shapes=[pltpu.VMEM((9, bs, bs), jnp.float32)],
    )(
        near.reshape(-1),
        slot.reshape(-1),
        a_blocks.reshape(n_r * n_c, terms, bs, bs),
        p_ext.reshape(ext_r * ext_c, 4, bs, bs),
    )
    ap = ap.reshape(n_r, n_c, 9, bs, bs)
    ap_dense = ap_dense.reshape((n_r, n_c) + ap_dense.shape[1:])

    o_r, o_c = n_r // 2, n_c // 2
    ey = y0 - 1 + jnp.arange(ext_r, dtype=jnp.int32)
    ex = x0 - 1 + jnp.arange(ext_c, dtype=jnp.int32)
    e_agg_y = mirror((ey - 1)[:, None] // 2 + two, coarse_rows)
    e_agg_x = mirror((ex - 1)[:, None] // 2 + two, coarse_cols)
    own_y = e_agg_y - y0 // 2
    own_x = e_agg_x - x0 // 2
    off_y = (ey // 2 - 1)[:, None] - e_agg_y + 2
    off_x = (ex // 2 - 1)[:, None] - e_agg_x + 2
    ok_y = (ey >= 0)[:, None] & (ey < grid_rows)[:, None] & (own_y >= 0) & (own_y < o_r) & (off_y >= 0) & (off_y <= 2)
    ok_x = (ex >= 0)[:, None] & (ex < grid_cols)[:, None] & (own_x >= 0) & (own_x < o_c) & (off_x >= 0) & (off_x <= 2)
    target = (own_y[:, None, :, None] * o_c + own_x[None, :, None, :]) * 25 + (
        off_y[:, None, :, None] * 5 + off_x[None, :, None, :]
    )
    target = jnp.where(ok_y[:, None, :, None] & ok_x[None, :, None, :], target, -1).reshape(ext_r, ext_c, 4)
    place = jnp.arange(ext_r * ext_c, dtype=jnp.int32).reshape(ext_r, ext_c)

    cy = ys[0] // 2 + jnp.arange(o_r, dtype=jnp.int32)
    cx = xs[0] // 2 + jnp.arange(o_c, dtype=jnp.int32)
    pick = (c_cols // coarse_cols - cy[:, None, None] + 2) * 5 + (c_cols % coarse_cols - cx[None, :, None] + 2)
    pick = jnp.clip(pick, 0, 24).reshape(-1)

    p_t = p_ext.reshape(ext_r * ext_c * 4, bs, bs)
    stencil = c_cols.shape[-1]
    smem = pl.BlockSpec(memory_space=pltpu.SMEM)
    vmem = pl.BlockSpec(memory_space=pltpu.VMEM)
    acc_shape = (o_r * o_c * 25, bs, bs)
    part = pl.pallas_call(
        own_kernel,
        out_shape=jax.ShapeDtypeStruct(acc_shape, jnp.float32),
        in_specs=[smem, smem, vmem, vmem],
        out_specs=vmem,
        cost_estimate=pl.CostEstimate(
            flops=2 * bs * bs * bs * 9 * n_r * n_c * 4, bytes_accessed=6 * 1024 * 1024, transcendentals=0
        ),
    )(place[1:-1, 1:-1].reshape(-1), target[1:-1, 1:-1].reshape(-1), ap.reshape(n_r * n_c, 9, bs, bs), p_t)
    top, bottom, left, right = halo_sides(ap_dense)
    parts = [
        (place[0, 1:-1], target[0, 1:-1], top),
        (place[-1, 1:-1], target[-1, 1:-1], bottom),
        (place[:, 0], target[:, 0], left),
        (place[:, -1], target[:, -1], right),
    ]
    out = pl.pallas_call(
        coarse_kernel,
        out_shape=jax.ShapeDtypeStruct((o_r * o_c, stencil, bs, bs), jnp.bfloat16),
        in_specs=[smem] * (2 * len(parts) + 1) + [vmem] * (len(parts) + 2),
        out_specs=vmem,
        scratch_shapes=[pltpu.VMEM(acc_shape, jnp.float32)],
    )(
        *[t for w, g, _ in parts for t in (w.reshape(-1), g.reshape(-1))],
        pick,
        *[b for _, _, b in parts],
        p_t,
        part,
    )
    return out.reshape(o_r, o_c, stencil, bs, bs)


def solution(mesh):
    return jax.shard_map(
        body,
        mesh=mesh,
        in_specs=(
            P("row", "col", None, None, None),
            P("row", "col", None),
            P("row", "col", None, None, None),
            P("row", "col", None),
            P("row", "col", None),
        ),
        out_specs=P("row", "col", None, None, None),
        check_vma=False,
    )
```

```python
import functools

import jax
import jax.numpy as jnp
from jax import lax
from jax.experimental import pallas as pl
from jax.experimental.pallas import tpu as pltpu
from jax.sharding import PartitionSpec as P


def mirror(values, limit):
    values = jnp.where(values < 0, -values, values)
    return jnp.where(values >= limit, 2 * (limit - 1) - values, values)


def shifted(piece, down, right):
    rows, cols = lax.axis_size("row"), lax.axis_size("col")
    if right == 0:
        pairs = [(s, s + down) for s in range(rows) if 0 <= s + down < rows]
        return lax.ppermute(piece, "row", pairs)
    if down == 0:
        pairs = [(s, s + right) for s in range(cols) if 0 <= s + right < cols]
        return lax.ppermute(piece, "col", pairs)
    pairs = []
    for sr in range(rows):
        for sc in range(cols):
            tr, tc = sr + down, sc + right
            if 0 <= tr < rows and 0 <= tc < cols:
                pairs.append((sr * cols + sc, tr * cols + tc))
    return lax.ppermute(piece, ("row", "col"), pairs)


def dense_shifted(piece, down, right):
    rows, cols = piece.shape[-2], piece.shape[-1]
    lanes = 128 if (rows * cols) % 128 == 0 and cols < 128 else cols
    packed = piece.reshape(piece.shape[:-2] + (rows * cols // lanes, lanes))
    return shifted(packed, down, right).reshape(piece.shape)


def halo_sides(x):
    top = dense_shifted(x[-1], 1, 0)
    bottom = dense_shifted(x[0], -1, 0)
    left = dense_shifted(jnp.concatenate([top[-1:], x[:, -1], bottom[-1:]], axis=0), 0, 1)
    right = dense_shifted(jnp.concatenate([top[:1], x[:, 0], bottom[:1]], axis=0), 0, -1)
    return top, bottom, left, right


def with_halo(x):
    top, bottom, left, right = halo_sides(x)
    middle = jnp.concatenate([top[None], x, bottom[None]], axis=0)
    return jnp.concatenate([left[:, None], middle, right[:, None]], axis=1)


def halo_ring(x):
    top, bottom, left, right = halo_sides(x)
    return jnp.concatenate(
        [left[:1], top, right[:1], left[-1:], bottom, right[-1:], left[1:-1], right[1:-1]], axis=0
    )


def ap_kernel(near_ref, slot_ref, a_ref, p_ref, out_ref, dense_ref, acc_ref, *, n_r, n_c):
    tiles, terms = a_ref.shape[0], a_ref.shape[1]

    def one_tile(t, carry):
        acc_ref[...] = jnp.zeros(acc_ref.shape, jnp.float32)
        for k in range(terms):
            j = near_ref[t * terms + k]
            a = a_ref[t, k]
            for q in range(4):
                e = slot_ref[(t * terms + k) * 4 + q]
                keep = jnp.where(e >= 0, 1.0, 0.0).astype(jnp.float32)
                prod = jnp.dot(a, p_ref[j, q], preferred_element_type=jnp.float32)
                acc_ref[jnp.clip(e, 0, 8)] += prod * keep

        ap = acc_ref[...].astype(out_ref.dtype)
        out_ref[t] = ap
        row, col = t // n_c, t % n_c

        @pl.when((row == 0) | (row == n_r - 1) | (col == 0) | (col == n_c - 1))
        def _():
            dense_ref[t] = ap.reshape(dense_ref.shape[1:])

        return carry

    lax.fori_loop(0, tiles, one_tile, 0)


def add_terms(where_ref, target_ref, ap_ref, pt_ref, acc_ref):
    def one_tile(t, carry):
        w = where_ref[t]
        dense = ap_ref.shape[-2:] != pt_ref.shape[1:]
        blocks = [ap_ref[t, e].reshape(pt_ref.shape[1:]) for e in range(9)] if dense else None
        for q in range(4):
            g = target_ref[t * 4 + q]

            @pl.when(g >= 0)
            def _():
                p = pt_ref[w * 4 + q]
                for e in range(9):
                    block = blocks[e] if dense else ap_ref[t, e]
                    acc_ref[g + (e // 3) * 5 + e % 3] += lax.dot_general(
                        p, block, (((0,), (0,)), ((), ())), preferred_element_type=jnp.float32
                    )

        return carry

    lax.fori_loop(0, ap_ref.shape[0], one_tile, 0)


def own_kernel(where_ref, target_ref, ap_ref, pt_ref, acc_ref):
    acc_ref[...] = jnp.zeros(acc_ref.shape, jnp.float32)
    add_terms(where_ref, target_ref, ap_ref, pt_ref, acc_ref)


def coarse_kernel(*refs):
    groups = (len(refs) - 5) // 3
    tables, pick_ref = refs[: 2 * groups], refs[2 * groups]
    blocks = refs[2 * groups + 1 : 3 * groups + 1]
    pt_ref, part_ref, out_ref, acc_ref = refs[-4], refs[-3], refs[-2], refs[-1]
    acc_ref[...] = part_ref[...]
    for i in range(groups):
        add_terms(tables[2 * i], tables[2 * i + 1], blocks[i], pt_ref, acc_ref)
    owned, stencil = out_ref.shape[0], out_ref.shape[1]

    def one_pick(i, carry):
        a = i // stencil
        out_ref[a, i % stencil] = acc_ref[a * stencil + pick_ref[i]].astype(out_ref.dtype)
        return carry

    lax.fori_loop(0, owned * stencil, one_pick, 0)


def ring_of(x):
    return jnp.concatenate([x[0], x[-1], x[1:-1, 0], x[1:-1, -1]], axis=0)


def body(a_blocks, a_cols, p_blocks, p_cols, c_cols):
    n_r, n_c = a_blocks.shape[0], a_blocks.shape[1]
    bs = a_blocks.shape[-1]
    terms = a_blocks.shape[2]
    grid_rows = n_r * lax.axis_size("row")
    grid_cols = n_c * lax.axis_size("col")
    coarse_rows, coarse_cols = grid_rows // 2, grid_cols // 2
    y0 = lax.axis_index("row") * n_r
    x0 = lax.axis_index("col") * n_c
    ys = y0 + jnp.arange(n_r, dtype=jnp.int32)
    xs = x0 + jnp.arange(n_c, dtype=jnp.int32)
    two = jnp.arange(2, dtype=jnp.int32)

    agg_y = mirror((ys - 1)[:, None] // 2 + two, coarse_rows)
    agg_x = mirror((xs - 1)[:, None] // 2 + two, coarse_cols)
    wanted = (agg_y[:, None, :, None] * coarse_cols + agg_x[None, :, None, :]).reshape(n_r, n_c, 4)
    match = p_cols[:, :, None, :] == wanted[:, :, :, None]
    which = jnp.argmax(match, axis=-1).astype(jnp.int32)
    canon = jnp.take_along_axis(p_blocks, which[..., None, None], axis=2)
    p_ext = with_halo(canon)
    ext_r, ext_c = n_r + 2, n_c + 2

    near_y = a_cols // grid_cols
    near_x = a_cols % grid_cols
    near = jnp.clip(near_y - (y0 - 1), 0, ext_r - 1) * ext_c + jnp.clip(near_x - (x0 - 1), 0, ext_c - 1)
    near_agg_y = mirror((near_y - 1)[..., None] // 2 + two, coarse_rows)
    near_agg_x = mirror((near_x - 1)[..., None] // 2 + two, coarse_cols)
    slot_y = near_agg_y - (ys // 2 - 1)[:, None, None, None]
    slot_x = near_agg_x - (xs // 2 - 1)[None, :, None, None]
    slot = (slot_y[..., :, None] * 3 + slot_x[..., None, :]).reshape(n_r, n_c, terms, 4)
    slot = jnp.where((slot >= 0) & (slot < 9), slot, -1)

    ap, ap_dense = pl.pallas_call(
        functools.partial(ap_kernel, n_r=n_r, n_c=n_c),
        out_shape=(
            jax.ShapeDtypeStruct((n_r * n_c, 9, bs, bs), jnp.bfloat16),
            jax.ShapeDtypeStruct((n_r * n_c, 9, bs * bs // 128, 128), jnp.bfloat16),
        ),
        in_specs=[
            pl.BlockSpec(memory_space=pltpu.SMEM),
            pl.BlockSpec(memory_space=pltpu.SMEM),
            pl.BlockSpec(memory_space=pltpu.VMEM),
            pl.BlockSpec(memory_space=pltpu.VMEM),
        ],
        out_specs=(pl.BlockSpec(memory_space=pltpu.VMEM), pl.BlockSpec(memory_space=pltpu.VMEM)),
        scratch_shapes=[pltpu.VMEM((9, bs, bs), jnp.float32)],
    )(
        near.reshape(-1),
        slot.reshape(-1),
        a_blocks.reshape(n_r * n_c, terms, bs, bs),
        p_ext.reshape(ext_r * ext_c, 4, bs, bs),
    )
    ap = ap.reshape(n_r, n_c, 9, bs, bs)
    ap_dense = ap_dense.reshape((n_r, n_c) + ap_dense.shape[1:])

    o_r, o_c = n_r // 2, n_c // 2
    ey = y0 - 1 + jnp.arange(ext_r, dtype=jnp.int32)
    ex = x0 - 1 + jnp.arange(ext_c, dtype=jnp.int32)
    e_agg_y = mirror((ey - 1)[:, None] // 2 + two, coarse_rows)
    e_agg_x = mirror((ex - 1)[:, None] // 2 + two, coarse_cols)
    own_y = e_agg_y - y0 // 2
    own_x = e_agg_x - x0 // 2
    off_y = (ey // 2 - 1)[:, None] - e_agg_y + 2
    off_x = (ex // 2 - 1)[:, None] - e_agg_x + 2
    ok_y = (ey >= 0)[:, None] & (ey < grid_rows)[:, None] & (own_y >= 0) & (own_y < o_r) & (off_y >= 0) & (off_y <= 2)
    ok_x = (ex >= 0)[:, None] & (ex < grid_cols)[:, None] & (own_x >= 0) & (own_x < o_c) & (off_x >= 0) & (off_x <= 2)
    target = (own_y[:, None, :, None] * o_c + own_x[None, :, None, :]) * 25 + (
        off_y[:, None, :, None] * 5 + off_x[None, :, None, :]
    )
    target = jnp.where(ok_y[:, None, :, None] & ok_x[None, :, None, :], target, -1).reshape(ext_r, ext_c, 4)
    place = jnp.arange(ext_r * ext_c, dtype=jnp.int32).reshape(ext_r, ext_c)

    cy = ys[0] // 2 + jnp.arange(o_r, dtype=jnp.int32)
    cx = xs[0] // 2 + jnp.arange(o_c, dtype=jnp.int32)
    pick = (c_cols // coarse_cols - cy[:, None, None] + 2) * 5 + (c_cols % coarse_cols - cx[None, :, None] + 2)
    pick = jnp.clip(pick, 0, 24).reshape(-1)

    p_t = p_ext.reshape(ext_r * ext_c * 4, bs, bs)
    stencil = c_cols.shape[-1]
    smem = pl.BlockSpec(memory_space=pltpu.SMEM)
    vmem = pl.BlockSpec(memory_space=pltpu.VMEM)
    acc_shape = (o_r * o_c * 25, bs, bs)
    part = pl.pallas_call(
        own_kernel,
        out_shape=jax.ShapeDtypeStruct(acc_shape, jnp.float32),
        in_specs=[smem, smem, vmem, vmem],
        out_specs=vmem,
        cost_estimate=pl.CostEstimate(
            flops=2 * bs * bs * bs * 9 * n_r * n_c * 4, bytes_accessed=6 * 1024 * 1024, transcendentals=0
        ),
    )(place[1:-1, 1:-1].reshape(-1), target[1:-1, 1:-1].reshape(-1), ap.reshape(n_r * n_c, 9, bs, bs), p_t)
    top, bottom, left, right = halo_sides(ap_dense)
    parts = [
        (place[0, 1:-1], target[0, 1:-1], top),
        (place[-1, 1:-1], target[-1, 1:-1], bottom),
        (place[:, 0], target[:, 0], left),
        (place[:, -1], target[:, -1], right),
    ]
    out = pl.pallas_call(
        coarse_kernel,
        out_shape=jax.ShapeDtypeStruct((o_r * o_c, stencil, bs, bs), jnp.bfloat16),
        in_specs=[smem] * (2 * len(parts) + 1) + [vmem] * (len(parts) + 2),
        out_specs=vmem,
        scratch_shapes=[pltpu.VMEM(acc_shape, jnp.float32)],
    )(
        *[t for w, g, _ in parts for t in (w.reshape(-1), g.reshape(-1))],
        pick,
        *[b for _, _, b in parts],
        p_t,
        part,
    )
    return out.reshape(o_r, o_c, stencil, bs, bs)


def solution(mesh):
    return jax.shard_map(
        body,
        mesh=mesh,
        in_specs=(
            P("row", "col", None, None, None),
            P("row", "col", None),
            P("row", "col", None, None, None),
            P("row", "col", None),
            P("row", "col", None),
        ),
        out_specs=P("row", "col", None, None, None),
        check_vma=False,
    )
```

```python
import functools

import jax
import jax.numpy as jnp
from jax import lax
from jax.experimental import pallas as pl
from jax.experimental.pallas import tpu as pltpu
from jax.sharding import PartitionSpec as P


def mirror(values, limit):
    values = jnp.where(values < 0, -values, values)
    return jnp.where(values >= limit, 2 * (limit - 1) - values, values)


def shifted(piece, down, right):
    rows, cols = lax.axis_size("row"), lax.axis_size("col")
    if right == 0:
        pairs = [(s, s + down) for s in range(rows) if 0 <= s + down < rows]
        return lax.ppermute(piece, "row", pairs)
    if down == 0:
        pairs = [(s, s + right) for s in range(cols) if 0 <= s + right < cols]
        return lax.ppermute(piece, "col", pairs)
    pairs = []
    for sr in range(rows):
        for sc in range(cols):
            tr, tc = sr + down, sc + right
            if 0 <= tr < rows and 0 <= tc < cols:
                pairs.append((sr * cols + sc, tr * cols + tc))
    return lax.ppermute(piece, ("row", "col"), pairs)


def dense_shifted(piece, down, right):
    rows, cols = piece.shape[-2], piece.shape[-1]
    lanes = 128 if (rows * cols) % 128 == 0 and cols < 128 else cols
    packed = piece.reshape(piece.shape[:-2] + (rows * cols // lanes, lanes))
    return shifted(packed, down, right).reshape(piece.shape)


def halo_sides(x):
    top = dense_shifted(x[-1], 1, 0)
    bottom = dense_shifted(x[0], -1, 0)
    left = dense_shifted(jnp.concatenate([top[-1:], x[:, -1], bottom[-1:]], axis=0), 0, 1)
    right = dense_shifted(jnp.concatenate([top[:1], x[:, 0], bottom[:1]], axis=0), 0, -1)
    return top, bottom, left, right


def with_halo(x):
    top, bottom, left, right = halo_sides(x)
    middle = jnp.concatenate([top[None], x, bottom[None]], axis=0)
    return jnp.concatenate([left[:, None], middle, right[:, None]], axis=1)


def halo_ring(x):
    top, bottom, left, right = halo_sides(x)
    return jnp.concatenate(
        [left[:1], top, right[:1], left[-1:], bottom, right[-1:], left[1:-1], right[1:-1]], axis=0
    )


def ap_kernel(near_ref, slot_ref, a_ref, p_ref, out_ref, dense_ref, acc_ref, *, n_r, n_c):
    tiles, terms = a_ref.shape[0], a_ref.shape[1]

    def one_tile(t, carry):
        acc_ref[...] = jnp.zeros(acc_ref.shape, jnp.float32)
        for k in range(terms):
            j = near_ref[t * terms + k]
            a = a_ref[t, k]
            for q in range(4):
                e = slot_ref[(t * terms + k) * 4 + q]
                keep = jnp.where(e >= 0, 1.0, 0.0).astype(jnp.float32)
                prod = jnp.dot(a, p_ref[j, q], preferred_element_type=jnp.float32)
                acc_ref[jnp.clip(e, 0, 8)] += prod * keep

        ap = acc_ref[...].astype(out_ref.dtype)
        out_ref[t] = ap
        row, col = t // n_c, t % n_c

        @pl.when((row == 0) | (row == n_r - 1) | (col == 0) | (col == n_c - 1))
        def _():
            dense_ref[t] = ap.reshape(dense_ref.shape[1:])

        return carry

    lax.fori_loop(0, tiles, one_tile, 0)


def add_terms(where_ref, target_ref, ap_ref, pt_ref, acc_ref):
    def one_tile(t, carry):
        w = where_ref[t]
        dense = ap_ref.shape[-2:] != pt_ref.shape[1:]
        blocks = [ap_ref[t, e].reshape(pt_ref.shape[1:]) for e in range(9)] if dense else None
        for q in range(4):
            g = target_ref[t * 4 + q]

            @pl.when(g >= 0)
            def _():
                p = pt_ref[w * 4 + q]
                for e in range(9):
                    block = blocks[e] if dense else ap_ref[t, e]
                    acc_ref[g + (e // 3) * 5 + e % 3] += lax.dot_general(
                        p, block, (((0,), (0,)), ((), ())), preferred_element_type=jnp.float32
                    )

        return carry

    lax.fori_loop(0, ap_ref.shape[0], one_tile, 0)


def own_kernel(where_ref, target_ref, ap_ref, pt_ref, acc_ref):
    acc_ref[...] = jnp.zeros(acc_ref.shape, jnp.float32)
    add_terms(where_ref, target_ref, ap_ref, pt_ref, acc_ref)


def coarse_kernel(*refs):
    groups = (len(refs) - 5) // 3
    tables, pick_ref = refs[: 2 * groups], refs[2 * groups]
    blocks = refs[2 * groups + 1 : 3 * groups + 1]
    pt_ref, part_ref, out_ref, acc_ref = refs[-4], refs[-3], refs[-2], refs[-1]
    acc_ref[...] = jnp.zeros(acc_ref.shape, jnp.float32)
    for i in range(groups):
        add_terms(tables[2 * i], tables[2 * i + 1], blocks[i], pt_ref, acc_ref)
    owned, stencil = out_ref.shape[0], out_ref.shape[1]

    def one_pick(i, carry):
        a = i // stencil
        at = a * stencil + pick_ref[i]
        out_ref[a, i % stencil] = (part_ref[at] + acc_ref[at]).astype(out_ref.dtype)
        return carry

    lax.fori_loop(0, owned * stencil, one_pick, 0)


def ring_of(x):
    return jnp.concatenate([x[0], x[-1], x[1:-1, 0], x[1:-1, -1]], axis=0)


def body(a_blocks, a_cols, p_blocks, p_cols, c_cols):
    n_r, n_c = a_blocks.shape[0], a_blocks.shape[1]
    bs = a_blocks.shape[-1]
    terms = a_blocks.shape[2]
    grid_rows = n_r * lax.axis_size("row")
    grid_cols = n_c * lax.axis_size("col")
    coarse_rows, coarse_cols = grid_rows // 2, grid_cols // 2
    y0 = lax.axis_index("row") * n_r
    x0 = lax.axis_index("col") * n_c
    ys = y0 + jnp.arange(n_r, dtype=jnp.int32)
    xs = x0 + jnp.arange(n_c, dtype=jnp.int32)
    two = jnp.arange(2, dtype=jnp.int32)

    agg_y = mirror((ys - 1)[:, None] // 2 + two, coarse_rows)
    agg_x = mirror((xs - 1)[:, None] // 2 + two, coarse_cols)
    wanted = (agg_y[:, None, :, None] * coarse_cols + agg_x[None, :, None, :]).reshape(n_r, n_c, 4)
    match = p_cols[:, :, None, :] == wanted[:, :, :, None]
    canon = jnp.sum(
        jnp.where(match[..., None, None], p_blocks[:, :, None], jnp.zeros((), p_blocks.dtype)),
        axis=3,
        dtype=p_blocks.dtype,
    )
    p_ext = with_halo(canon)
    ext_r, ext_c = n_r + 2, n_c + 2

    near_y = a_cols // grid_cols
    near_x = a_cols % grid_cols
    near = jnp.clip(near_y - (y0 - 1), 0, ext_r - 1) * ext_c + jnp.clip(near_x - (x0 - 1), 0, ext_c - 1)
    near_agg_y = mirror((near_y - 1)[..., None] // 2 + two, coarse_rows)
    near_agg_x = mirror((near_x - 1)[..., None] // 2 + two, coarse_cols)
    slot_y = near_agg_y - (ys // 2 - 1)[:, None, None, None]
    slot_x = near_agg_x - (xs // 2 - 1)[None, :, None, None]
    slot = (slot_y[..., :, None] * 3 + slot_x[..., None, :]).reshape(n_r, n_c, terms, 4)
    slot = jnp.where((slot >= 0) & (slot < 9), slot, -1)

    ap, ap_dense = pl.pallas_call(
        functools.partial(ap_kernel, n_r=n_r, n_c=n_c),
        out_shape=(
            jax.ShapeDtypeStruct((n_r * n_c, 9, bs, bs), jnp.bfloat16),
            jax.ShapeDtypeStruct((n_r * n_c, 9, bs * bs // 128, 128), jnp.bfloat16),
        ),
        in_specs=[
            pl.BlockSpec(memory_space=pltpu.SMEM),
            pl.BlockSpec(memory_space=pltpu.SMEM),
            pl.BlockSpec(memory_space=pltpu.VMEM),
            pl.BlockSpec(memory_space=pltpu.VMEM),
        ],
        out_specs=(pl.BlockSpec(memory_space=pltpu.VMEM), pl.BlockSpec(memory_space=pltpu.VMEM)),
        scratch_shapes=[pltpu.VMEM((9, bs, bs), jnp.float32)],
    )(
        near.reshape(-1),
        slot.reshape(-1),
        a_blocks.reshape(n_r * n_c, terms, bs, bs),
        p_ext.reshape(ext_r * ext_c, 4, bs, bs),
    )
    ap = ap.reshape(n_r, n_c, 9, bs, bs)
    ap_dense = ap_dense.reshape((n_r, n_c) + ap_dense.shape[1:])

    o_r, o_c = n_r // 2, n_c // 2
    ey = y0 - 1 + jnp.arange(ext_r, dtype=jnp.int32)
    ex = x0 - 1 + jnp.arange(ext_c, dtype=jnp.int32)
    e_agg_y = mirror((ey - 1)[:, None] // 2 + two, coarse_rows)
    e_agg_x = mirror((ex - 1)[:, None] // 2 + two, coarse_cols)
    own_y = e_agg_y - y0 // 2
    own_x = e_agg_x - x0 // 2
    off_y = (ey // 2 - 1)[:, None] - e_agg_y + 2
    off_x = (ex // 2 - 1)[:, None] - e_agg_x + 2
    ok_y = (ey >= 0)[:, None] & (ey < grid_rows)[:, None] & (own_y >= 0) & (own_y < o_r) & (off_y >= 0) & (off_y <= 2)
    ok_x = (ex >= 0)[:, None] & (ex < grid_cols)[:, None] & (own_x >= 0) & (own_x < o_c) & (off_x >= 0) & (off_x <= 2)
    target = (own_y[:, None, :, None] * o_c + own_x[None, :, None, :]) * 25 + (
        off_y[:, None, :, None] * 5 + off_x[None, :, None, :]
    )
    target = jnp.where(ok_y[:, None, :, None] & ok_x[None, :, None, :], target, -1).reshape(ext_r, ext_c, 4)
    place = jnp.arange(ext_r * ext_c, dtype=jnp.int32).reshape(ext_r, ext_c)

    cy = ys[0] // 2 + jnp.arange(o_r, dtype=jnp.int32)
    cx = xs[0] // 2 + jnp.arange(o_c, dtype=jnp.int32)
    pick = (c_cols // coarse_cols - cy[:, None, None] + 2) * 5 + (c_cols % coarse_cols - cx[None, :, None] + 2)
    pick = jnp.clip(pick, 0, 24).reshape(-1)

    p_t = p_ext.reshape(ext_r * ext_c * 4, bs, bs)
    stencil = c_cols.shape[-1]
    smem = pl.BlockSpec(memory_space=pltpu.SMEM)
    vmem = pl.BlockSpec(memory_space=pltpu.VMEM)
    acc_shape = (o_r * o_c * 25, bs, bs)
    part = pl.pallas_call(
        own_kernel,
        out_shape=jax.ShapeDtypeStruct(acc_shape, jnp.float32),
        in_specs=[smem, smem, vmem, vmem],
        out_specs=vmem,
        cost_estimate=pl.CostEstimate(
            flops=2 * bs * bs * bs * 9 * n_r * n_c * 4, bytes_accessed=6 * 1024 * 1024, transcendentals=0
        ),
    )(place[1:-1, 1:-1].reshape(-1), target[1:-1, 1:-1].reshape(-1), ap.reshape(n_r * n_c, 9, bs, bs), p_t)
    top, bottom, left, right = halo_sides(ap_dense)
    parts = [
        (place[0, 1:-1], target[0, 1:-1], top),
        (place[-1, 1:-1], target[-1, 1:-1], bottom),
        (place[:, 0], target[:, 0], left),
        (place[:, -1], target[:, -1], right),
    ]
    out = pl.pallas_call(
        coarse_kernel,
        out_shape=jax.ShapeDtypeStruct((o_r * o_c, stencil, bs, bs), jnp.bfloat16),
        in_specs=[smem] * (2 * len(parts) + 1) + [vmem] * (len(parts) + 2),
        out_specs=vmem,
        scratch_shapes=[pltpu.VMEM(acc_shape, jnp.float32)],
    )(
        *[t for w, g, _ in parts for t in (w.reshape(-1), g.reshape(-1))],
        pick,
        *[b for _, _, b in parts],
        p_t,
        part,
    )
    return out.reshape(o_r, o_c, stencil, bs, bs)


def solution(mesh):
    return jax.shard_map(
        body,
        mesh=mesh,
        in_specs=(
            P("row", "col", None, None, None),
            P("row", "col", None),
            P("row", "col", None, None, None),
            P("row", "col", None),
            P("row", "col", None),
        ),
        out_specs=P("row", "col", None, None, None),
        check_vma=False,
    )
```
